512 devices in a mesh: space: 256 (over z, y, x), vec: 2 (over core).
Axes of the slice: x: 4, y: 4, z: 16, core: 2. Of those that a mesh axis runs over, the one named last changes fastest.
Arguments:
- vectors: bfloat16 [262144, 256], P('space', 'vec'), may hold values from -6 to 6
- points: float32 [3, 262144], P(None, 'space'), may hold values from 0 to 1024, as said below
- near_index: int32 [4096, 3], P('space'), may hold values from -1 to 4095, as said below
- leaf_basis: bfloat16 [32, 262144], P(None, 'space'), may hold values from -0.75 to 0.75
- transfer: bfloat16 [256, 15, 32, 64], P('space'), may hold values from -0.875 to 0.875
- coupling: bfloat16 [256, 31, 32, 96], P('space'), may hold values from -0.1875 to 0.1875
- upper_transfer: bfloat16 [256, 32, 64], P('space'), may hold values from -0.875 to 0.875
- upper_coupling: bfloat16 [256, 32, 96], P('space'), may hold values from -0.1875 to 0.1875
Outputs:
- covariance_product: bfloat16 [262144, 256], P('space', 'vec')
The draws below stay inside these ranges and needn't reach their ends.
Inputs may be any that keep to these rules, and one draw needn't show every extreme that they name: `near_index`: entry 0 of row t is t; entry 1 is t - 1 or -1, entry 2 is t + 1 or -1; -1 marks an absent block, and it stands in entry 1 of row 0 and entry 2 of row 4095; entry 1 of a row t > 0 that is a multiple of 16 is t - 1, and entry 2 of a row t < 4095 with t + 1 a multiple of 16 is t + 1. `points`: the first coordinate of a point of leaf t lies in [t / 4, (t + 1) / 4], the other two in [0, 1/4].
All inputs are finite; a program needn't handle non-finite values.
Results may differ from the reference program's by a relative error of at most 0.005.
Values may be sent and summed in bfloat16 or wider, within the bound.
No kernel may reach another device: no remote copies, remote signals or barrier semaphores. Data moves between devices by JAX's collectives and lax.ppermute only.
A program may use at most 64 MiB of HBM per device.

```python
import jax
import jax.numpy as jnp
import numpy as np
from jax import lax

LEAF = 64
RANK = 32
VECS = 256
LEVELS = 4
LEAF_DEV = 16
LEAVES = 4096
POINTS = 262144
SPACE_BITS = 8
TOP = 10
N_SPACE = 256


def draw_points(key, part):
    first_key, second_key = jax.random.split(jax.random.fold_in(key, 11))
    leaf_number = (jnp.arange(POINTS, dtype=jnp.int32) // LEAF).astype(jnp.float32)
    along = jax.random.uniform(first_key, (POINTS,), jnp.float32)
    across = jax.random.uniform(second_key, (2, POINTS), jnp.float32)
    head_row = (leaf_number + along) * 0.25
    return jnp.concatenate([head_row[None], 0.25 * across], 0)


def draw_near_index(key, part):
    leaf_number = jnp.arange(LEAVES, dtype=jnp.int32)
    present = jax.random.randint(jax.random.fold_in(key, 23), (2, LEAVES), 0, 4, dtype=jnp.int32) > 0
    left_edge = leaf_number % LEAF_DEV == 0
    right_edge = leaf_number % LEAF_DEV == LEAF_DEV - 1
    left_leaf = jnp.where((present[0] | left_edge) & (leaf_number > 0), leaf_number - 1, -1)
    right_leaf = jnp.where((present[1] | right_edge) & (leaf_number < LEAVES - 1), leaf_number + 1, -1)
    return jnp.stack([leaf_number, left_leaf, right_leaf], 1).astype(jnp.int32)


def block_levels(key, extent, cuts, low, top_value):
    def one(position, parts):
        heights = jax.random.uniform(jax.random.fold_in(jax.random.fold_in(key, 6), position), (parts,), jnp.float32, low / len(cuts), top_value / len(cuts))
        return jnp.repeat(jnp.exp(heights), extent[position] // parts).reshape((-1,) + (1,) * (len(extent) - position - 1))

    gain = one(*cuts[0])
    for cut in cuts[1:]:
        gain = gain * one(*cut)
    return gain


def centred(stream_key, dims, width, most, pieces=(), held_as=jnp.bfloat16):
    loudness = block_levels(stream_key, dims, pieces, -0.22, 0.18) if pieces else 1.0
    entries = jax.random.normal(stream_key, dims, jnp.float32) * width * loudness
    return jnp.minimum(jnp.maximum(entries, -most), most).astype(held_as)


def setup_inputs(seed: int = 0) -> dict:
    keys = jax.random.split(jax.random.key(seed), 9)
    return {
        "vectors": centred(keys[0], (POINTS, VECS), 1.0, 6.0, ((0, 256), (1, 2))),
        "points": draw_points(jax.random.fold_in(keys[8], 71), 0),
        "near_index": draw_near_index(jax.random.fold_in(keys[8], 71), 0),
        "leaf_basis": centred(keys[3], (RANK, POINTS), LEAF ** -0.5, 0.75, ((1, 256),)),
        "transfer": centred(keys[4], (N_SPACE, LEAF_DEV - 1, RANK, 2 * RANK), (RANK * 1414 // 1000) ** -0.5, 0.875, ((0, 256),)),
        "coupling": centred(keys[5], (N_SPACE, 2 * LEAF_DEV - 1, RANK, 3 * RANK), (3 * RANK * (LEVELS + SPACE_BITS)) ** -0.5, 0.1875, ((0, 256),)),
        "upper_transfer": centred(keys[6], (N_SPACE, RANK, 2 * RANK), (RANK * 1414 // 1000) ** -0.5, 0.875, ((0, 256),)),
        "upper_coupling": centred(keys[7], (N_SPACE, RANK, 3 * RANK), (3 * RANK * (LEVELS + SPACE_BITS)) ** -0.5, 0.1875, ((0, 256),)),
    }


SCALE_A = 2.0 * 3.0 ** 0.5
VARIANCE = 0.0625
NUGGET = 0.5
HIGHEST = lax.Precision.HIGHEST

def matern(own_points, other_points):
    difference = own_points[:, :, None, :, None] - other_points[:, :, :, None, :]
    distance = jnp.sqrt(lax.optimization_barrier(jnp.sum(difference * difference, axis=0)))
    return (VARIANCE * (1.0 + SCALE_A * distance) * jnp.exp(-SCALE_A * distance)).astype(jnp.bfloat16)

def near_field(vectors, points, near_index):
    group_size = min(32, LEAVES)
    leaf_vectors = vectors.reshape(LEAVES, LEAF, VECS)
    leaf_points = points.reshape(3, LEAVES, LEAF)

    def one_group(first_leaf):
        listed = lax.dynamic_slice_in_dim(near_index, first_leaf, group_size, 0)
        present = (listed >= 0).astype(jnp.float32)
        partner_rows = jnp.maximum(listed, 0).astype(jnp.int32)
        own_points = lax.dynamic_slice_in_dim(leaf_points, first_leaf, group_size, 1)
        blocks = matern(own_points, leaf_points[:, partner_rows]).astype(jnp.float32) * present[:, :, None, None]
        sources = leaf_vectors[partner_rows].astype(jnp.float32)
        return jnp.einsum('gkij,gkjv->giv', blocks, sources, precision=HIGHEST)
    starts = jnp.arange(LEAVES // group_size, dtype=jnp.int32) * group_size
    return lax.map(one_group, starts).reshape(POINTS, VECS)

def partner_table(cluster_count):
    base = np.arange(cluster_count)
    odd_mask = base % 2 == 1
    return np.stack([np.where(odd_mask, -3, -2), np.where(odd_mask, -2, 2), np.where(odd_mask, 2, 3)], 1) + base[:, None]

def partners(coefs):
    cluster_count = coefs.shape[0]
    padded = jnp.pad(coefs, ((3, 3), (0, 0), (0, 0)))
    return padded[partner_table(cluster_count) + 3].reshape(cluster_count, 3 * RANK, coefs.shape[2])

def local_slice(stack, height, first_slot):
    cluster_count = LEAF_DEV >> height
    return stack[:, first_slot:first_slot + cluster_count].reshape((N_SPACE * cluster_count,) + stack.shape[2:])

def upper_slice(upper, height):
    middles = np.arange(N_SPACE >> height) * 2 ** height + 2 ** (height - 1)
    return upper[middles]

def transfer_at(transfer, upper_transfer, height):
    if height <= LEVELS:
        return local_slice(transfer, height, LEAF_DEV - (2 * LEAF_DEV >> height))
    return upper_slice(upper_transfer, height - LEVELS)

def coupling_at(coupling, upper_coupling, height):
    if height <= LEVELS:
        return local_slice(coupling, height, 2 * LEAF_DEV - (2 * LEAF_DEV >> height))
    return upper_slice(upper_coupling, height - LEVELS)

def reference(vectors, points, near_index, leaf_basis, transfer, coupling, upper_transfer, upper_coupling):
    nearby = near_field(vectors, points, near_index)
    basis_leaves = leaf_basis.astype(jnp.float32).reshape(RANK, LEAVES, LEAF)
    leaf_vectors = vectors.astype(jnp.float32).reshape(LEAVES, LEAF, VECS)
    coefficients = [jnp.einsum('rlp,lpv->lrv', basis_leaves, leaf_vectors, precision=HIGHEST)]
    for height in range(1, TOP + 1):
        lift_mats = transfer_at(transfer, upper_transfer, height).astype(jnp.float32)
        children = coefficients[-1].reshape(lift_mats.shape[0], 2 * RANK, VECS)
        coefficients.append(jnp.einsum('cra,cav->crv', lift_mats, children, precision=HIGHEST))
    fields = []
    for height in range(TOP + 1):
        mixers = coupling_at(coupling, upper_coupling, height).astype(jnp.float32)
        fields.append(jnp.einsum('cra,cav->crv', mixers, partners(coefficients[height]), precision=HIGHEST))
    downward = fields[TOP]
    for height in range(TOP - 1, -1, -1):
        lift_mats = transfer_at(transfer, upper_transfer, height + 1).astype(jnp.float32)
        spread = jnp.einsum('cra,crv->cav', lift_mats, downward, precision=HIGHEST)
        downward = fields[height] + spread.reshape(fields[height].shape)
    far_field = jnp.einsum('rlp,lrv->lpv', basis_leaves, downward, precision=HIGHEST).reshape(POINTS, VECS)
    return (nearby + NUGGET * vectors.astype(jnp.float32) + far_field).astype(jnp.bfloat16)
```

```python
import jax
import jax.numpy as jnp
import numpy as np
from jax import lax
from jax.sharding import PartitionSpec as P

LEAF = 64
RANK = 32


SCALE_A = 2.0 * 3.0**0.5
VARIANCE = 0.0625
NUGGET = 0.5
HIGHEST = lax.Precision.HIGHEST


def extended_2(cells, sides, width):
    for axis, dim in sides:
        count = lax.axis_size(axis)
        ends = count - 1
        head = lax.slice_in_dim(cells, 0, width, axis=dim)
        tail = lax.slice_in_dim(cells, cells.shape[dim] - width, cells.shape[dim], axis=dim)
        cells = jnp.concatenate(
            [
                lax.ppermute(tail, axis, [(i, (i + 1) % count) for i in range(ends)]),
                cells,
                lax.ppermute(head, axis, [((i + 1) % count, i) for i in range(ends)]),
            ],
            axis=dim,
        )
    return cells


def matern(own_points, other_points):
    difference = own_points[:, :, None, :, None] - other_points[:, :, :, None, :]
    distance = jnp.sqrt(jnp.sum(difference * difference, axis=0))
    return (VARIANCE * (1.0 + SCALE_A * distance) * jnp.exp(-SCALE_A * distance)).astype(
        jnp.bfloat16
    )


def near_field(source, extended_points, index_rows, first_leaf, leaf_zero, leaf_count):
    block_count = index_rows.shape[0]
    col_width = source.shape[1]
    group_size = min(8, block_count)
    source_leaves = source.reshape(leaf_count + 2, LEAF, col_width)
    point_leaves = extended_points.reshape(3, leaf_count + 2, LEAF)
    present = (index_rows >= 0).astype(jnp.bfloat16)
    located = jnp.where(index_rows >= 0, index_rows - leaf_zero + 1, 0)

    def one_group(first_row):
        own_points = lax.dynamic_slice_in_dim(
            point_leaves, first_row + first_leaf + 1, group_size, 1
        )
        blocks = matern(own_points, point_leaves[:, located]) * present[:, :, None, None]
        return jnp.einsum(
            "gkij,gkjv->giv", blocks, source_leaves[located], preferred_element_type=jnp.float32
        )

    starts = jnp.arange(block_count // group_size, dtype=jnp.int32) * group_size
    return lax.map(one_group, starts).reshape(block_count * LEAF, col_width)


def partner_table(cluster_count):
    base = np.arange(cluster_count)
    odd_mask = base % 2 == 1
    return (
        np.stack(
            [np.where(odd_mask, -3, -2), np.where(odd_mask, -2, 2), np.where(odd_mask, 2, 3)], 1
        )
        + base[:, None]
    )


def as_float(matrix):
    return matrix.astype(jnp.float32)


def product(matrix, operand):
    return jnp.dot(matrix, operand, precision=HIGHEST)


def neighbours(coefs, cluster):
    padded = jnp.pad(coefs, ((3, 3), (0, 0), (0, 0)))
    odd_mask = cluster % 2 == 1
    offsets = (
        jnp.where(odd_mask, -3, -2),
        jnp.where(odd_mask, -2, 2),
        jnp.where(odd_mask, 2, 3),
    )
    picked = [lax.dynamic_index_in_dim(padded, cluster + 3 + step, 0, False) for step in offsets]
    return jnp.concatenate(picked, 0)


def upper_tree(device_coef, device_coupling, upper_transfer, upper_coupling, position, space_bits):
    count = 2**space_bits
    summit = space_bits - 2
    level_coefs = [lax.all_gather(device_coef, "space")]
    lift_all = as_float(lax.all_gather(upper_transfer[0], "space"))
    mix_all = as_float(lax.all_gather(upper_coupling[0], "space"))
    for height in range(1, summit + 1):
        cluster_count = count >> height
        lift_mats = lift_all[2 ** (height - 1) :: 2**height]
        children = level_coefs[-1].reshape(cluster_count, 2 * RANK, -1)
        level_coefs.append(jnp.einsum("cra,cav->crv", lift_mats, children, precision=HIGHEST))

    def field(height, cluster):
        if height == 0:
            mixer = device_coupling
        else:
            mixer = lax.dynamic_index_in_dim(
                mix_all, cluster * 2**height + 2 ** (height - 1), 0, False
            )
        return product(mixer, neighbours(level_coefs[height], cluster))

    downward = field(summit, position >> summit)
    for height in range(summit - 1, -1, -1):
        cluster = position >> height
        parent = cluster >> 1
        lift = lax.dynamic_index_in_dim(lift_all, parent * 2 ** (height + 1) + 2**height, 0, False)
        half = jnp.where(cluster % 2 == 1, lift[:, RANK:], lift[:, :RANK])
        downward = field(height, cluster) + product(half.T, downward)
    return downward


def local(
    vectors, points, near_index, leaf_basis, transfer, coupling, upper_transfer, upper_coupling
):
    row_count, columns = vectors.shape
    leaf_count = row_count // LEAF
    depth_local = leaf_count.bit_length() - 1
    space_bits = lax.axis_size("space").bit_length() - 1
    position = lax.axis_index("space")
    leaf_zero = position * leaf_count
    vector_rims = extended_2(vectors, (("space", 0),), LEAF)
    point_rims = extended_2(points, (("space", 1),), LEAF)
    lane_count = lax.axis_size("vec")
    lane_leaves = leaf_count // lane_count
    first_leaf = lax.axis_index("vec") * lane_leaves
    all_columns = lax.all_gather(vector_rims, "vec", axis=1, tiled=True)
    own_rows = lax.dynamic_slice_in_dim(near_index, first_leaf, lane_leaves, 0)
    half_near = near_field(all_columns, point_rims, own_rows, first_leaf, leaf_zero, leaf_count)
    nearby = lax.all_to_all(half_near, "vec", split_axis=1, concat_axis=0, tiled=True)
    basis_leaves = leaf_basis.reshape(RANK, leaf_count, LEAF)
    leaf_vectors = vectors.reshape(leaf_count, LEAF, columns)
    coefficients = [
        jnp.einsum("rlp,lpv->lrv", basis_leaves, leaf_vectors, preferred_element_type=jnp.float32)
    ]
    for height in range(1, depth_local + 1):
        cluster_count = leaf_count >> height
        first_slot = leaf_count - (2 * leaf_count >> height)
        lift_mats = as_float(transfer[0, first_slot : first_slot + cluster_count])
        children = coefficients[-1].reshape(cluster_count, 2 * RANK, columns)
        coefficients.append(jnp.einsum("cra,cav->crv", lift_mats, children, precision=HIGHEST))
    edge_coefs = jnp.stack(
        [
            jnp.concatenate([coefficients[height][:2], coefficients[height][-2:]], 0)
            for height in range(depth_local)
        ],
        0,
    )
    wide_edges = extended_2(edge_coefs.astype(jnp.bfloat16), (("space", 1),), 2).astype(
        edge_coefs.dtype
    )
    fields = []
    for height in range(depth_local):
        cluster_count = leaf_count >> height
        first_slot = 2 * leaf_count - (2 * leaf_count >> height)
        extended = jnp.concatenate(
            [wide_edges[height, :2], coefficients[height], wide_edges[height, 6:]], 0
        )
        stacked = extended[partner_table(cluster_count) + 2].reshape(
            cluster_count, 3 * RANK, columns
        )
        mixers = as_float(coupling[0, first_slot : first_slot + cluster_count])
        fields.append(jnp.einsum("cra,cav->crv", mixers, stacked, precision=HIGHEST))
    device_coupling = as_float(coupling[0, 2 * leaf_count - 2])
    device_coef = coefficients[depth_local][0]
    downward = upper_tree(
        device_coef, device_coupling, upper_transfer, upper_coupling, position, space_bits
    )
    downward = downward[None]
    for height in range(depth_local - 1, -1, -1):
        cluster_count = leaf_count >> height + 1
        first_slot = leaf_count - (2 * leaf_count >> height + 1)
        lift_mats = as_float(transfer[0, first_slot : first_slot + cluster_count])
        spread = jnp.einsum("cra,crv->cav", lift_mats, downward, precision=HIGHEST)
        downward = fields[height] + spread.reshape(2 * cluster_count, RANK, columns)
    far_field = jnp.einsum(
        "rlp,lrv->lpv", as_float(basis_leaves), downward, precision=HIGHEST
    ).reshape(row_count, columns)
    return (nearby + NUGGET * vectors.astype(jnp.float32) + far_field).astype(jnp.bfloat16)


def solution(mesh):
    return jax.shard_map(
        local,
        mesh=mesh,
        in_specs=(
            P("space", "vec"),
            P(None, "space"),
            P("space", None),
            P(None, "space"),
            P("space", None, None, None),
            P("space", None, None, None),
            P("space", None, None),
            P("space", None, None),
        ),
        out_specs=P("space", "vec"),
        check_vma=False,
    )
```

```python
import jax
import jax.numpy as jnp
import numpy as np
from jax import lax
from jax.sharding import PartitionSpec as P

LEAF = 64
RANK = 32


SCALE_A = 2.0 * 3.0**0.5
VARIANCE = 0.0625
NUGGET = 0.5
HIGHEST = lax.Precision.HIGHEST


def extended_2(cells, sides, width):
    for axis, dim in sides:
        count = lax.axis_size(axis)
        ends = count - 1
        head = lax.slice_in_dim(cells, 0, width, axis=dim)
        tail = lax.slice_in_dim(cells, cells.shape[dim] - width, cells.shape[dim], axis=dim)
        cells = jnp.concatenate(
            [
                lax.ppermute(tail, axis, [(i, (i + 1) % count) for i in range(ends)]),
                cells,
                lax.ppermute(head, axis, [((i + 1) % count, i) for i in range(ends)]),
            ],
            axis=dim,
        )
    return cells


def matern(own_points, other_points):
    difference = own_points[:, :, None, :, None] - other_points[:, :, :, None, :]
    distance = jnp.sqrt(jnp.sum(difference * difference, axis=0))
    return (VARIANCE * (1.0 + SCALE_A * distance) * jnp.exp(-SCALE_A * distance)).astype(
        jnp.bfloat16
    )


def near_field(source, extended_points, index_rows, first_leaf, leaf_zero, leaf_count):
    block_count = index_rows.shape[0]
    col_width = source.shape[1]
    group_size = min(8, block_count)
    source_leaves = source.reshape(leaf_count + 2, LEAF, col_width)
    point_leaves = extended_points.reshape(3, leaf_count + 2, LEAF)
    present = (index_rows >= 0).astype(jnp.bfloat16)
    located = jnp.where(index_rows >= 0, index_rows - leaf_zero + 1, 0)

    def one_group(first_row):
        own_points = lax.dynamic_slice_in_dim(
            point_leaves, first_row + first_leaf + 1, group_size, 1
        )
        blocks = matern(own_points, point_leaves[:, located]) * present[:, :, None, None]
        return jnp.einsum(
            "gkij,gkjv->giv", blocks, source_leaves[located], preferred_element_type=jnp.float32
        )

    starts = jnp.arange(block_count // group_size, dtype=jnp.int32) * group_size
    return lax.map(one_group, starts).reshape(block_count * LEAF, col_width)


def partner_table(cluster_count):
    base = np.arange(cluster_count)
    odd_mask = base % 2 == 1
    return (
        np.stack(
            [np.where(odd_mask, -3, -2), np.where(odd_mask, -2, 2), np.where(odd_mask, 2, 3)], 1
        )
        + base[:, None]
    )


def as_float(matrix):
    return matrix.astype(jnp.float32)


def product(matrix, operand):
    return jnp.dot(matrix, operand, precision=HIGHEST)


SPACE = ("z", "y", "x")
PLANE = ("y", "x")
CUTS = (16, 4, 4)


def neighbours(padded, cluster):
    odd_mask = cluster % 2 == 1
    offsets = (
        jnp.where(odd_mask, -3, -2),
        jnp.where(odd_mask, -2, 2),
        jnp.where(odd_mask, 2, 3),
    )
    picked = [lax.dynamic_index_in_dim(padded, cluster + 3 + step, 0, False) for step in offsets]
    return jnp.concatenate(picked, 0)


def pick(stack, index):
    return lax.dynamic_index_in_dim(stack, index, 0, False)


def lift_up(lift_mats, coefs):
    children = coefs.reshape(lift_mats.shape[0], 2 * RANK, coefs.shape[-1])
    return jnp.einsum("cra,cav->crv", lift_mats, children, precision=HIGHEST)


def rims(own, left_tail, right_head):
    zeros = jnp.zeros((3 - left_tail.shape[0],) + own.shape[1:], own.dtype)
    return jnp.concatenate([zeros, left_tail, own, right_head, zeros], 0)


def upper_tree(device_coef, device_coupling, upper_transfer, upper_coupling):
    planes = lax.axis_size("z")
    plane_bits = lax.axis_size(PLANE).bit_length() - 1
    plane = lax.axis_index("z")
    seat = lax.axis_index(PLANE)
    plane_lift_held = lax.all_gather(upper_transfer[0], PLANE)
    plane_mix_held = lax.all_gather(upper_coupling[0], PLANE)
    plane_lift = as_float(plane_lift_held)
    plane_mix = as_float(plane_mix_held)
    inner = [lax.all_gather(device_coef, PLANE)]
    for height in range(1, plane_bits + 1):
        inner.append(lift_up(plane_lift[2 ** (height - 1) :: 2**height], inner[-1]))
    tails = jnp.concatenate([level[-3:] for level in inner[:plane_bits]], 0)
    heads = jnp.concatenate([level[:3] for level in inner[:plane_bits]], 0)
    from_left = lax.ppermute(tails, "z", [(i, i + 1) for i in range(planes - 1)])
    from_right = lax.ppermute(heads, "z", [(i + 1, i) for i in range(planes - 1)])
    summary = lax.all_gather(inner[plane_bits][0], "z")
    outer_lift = as_float(lax.all_gather(plane_lift_held[0], "z"))
    outer_mix = as_float(lax.all_gather(plane_mix_held[0], "z"))
    outer = [summary]
    for height in range(1, (planes.bit_length() - 1) - 1):
        outer.append(lift_up(outer_lift[2 ** (height - 1) :: 2**height], outer[-1]))
    summit = plane_bits + len(outer) - 1
    fields = []
    lifts = []
    done = 0
    for height in range(plane_bits):
        width = min(3, inner[height].shape[0])
        extended = rims(
            inner[height], from_left[done : done + width], from_right[done : done + width]
        )
        done += width
        cluster = seat >> height
        if height == 0:
            mixer = device_coupling
        else:
            mixer = pick(plane_mix, cluster * 2**height + 2 ** (height - 1))
        fields.append(product(mixer, neighbours(extended, cluster)))
        parent = cluster >> 1
        lifts.append((cluster, pick(plane_lift, parent * 2 ** (height + 1) + 2**height)))
    for level, coefs in enumerate(outer):
        height = plane_bits + level
        cluster = plane >> level
        if level == 0:
            mixer = pick(plane_mix, 2 ** (height - 1))
        else:
            mixer = pick(outer_mix, cluster * 2**level + 2 ** (level - 1))
        padded = jnp.pad(coefs, ((3, 3), (0, 0), (0, 0)))
        fields.append(product(mixer, neighbours(padded, cluster)))
        if height < summit:
            parent = cluster >> 1
            lifts.append((cluster, pick(outer_lift, parent * 2 ** (level + 1) + 2**level)))
    downward = fields[summit]
    for height in range(summit - 1, -1, -1):
        cluster, lift = lifts[height]
        half = jnp.where(cluster % 2 == 1, lift[:, RANK:], lift[:, :RANK])
        downward = fields[height] + product(half.T, downward)
    return downward


def local(
    vectors, points, near_index, leaf_basis, transfer, coupling, upper_transfer, upper_coupling
):
    row_count, columns = vectors.shape
    leaf_count = row_count // LEAF
    depth_local = leaf_count.bit_length() - 1
    position = lax.axis_index(SPACE)
    leaf_zero = position * leaf_count
    vector_rims = extended_2(vectors, ((SPACE, 0),), LEAF)
    point_rims = extended_2(points, ((SPACE, 1),), LEAF)
    lane_count = lax.axis_size("vec")
    lane_leaves = leaf_count // lane_count
    first_leaf = lax.axis_index("vec") * lane_leaves
    all_columns = lax.all_gather(vector_rims, "vec", axis=1, tiled=True)
    own_rows = lax.dynamic_slice_in_dim(near_index, first_leaf, lane_leaves, 0)
    half_near = near_field(all_columns, point_rims, own_rows, first_leaf, leaf_zero, leaf_count)
    nearby = lax.all_to_all(half_near, "vec", split_axis=1, concat_axis=0, tiled=True)
    basis_leaves = leaf_basis.reshape(RANK, leaf_count, LEAF)
    leaf_vectors = vectors.reshape(leaf_count, LEAF, columns)
    coefficients = [
        jnp.einsum("rlp,lpv->lrv", basis_leaves, leaf_vectors, preferred_element_type=jnp.float32)
    ]
    for height in range(1, depth_local + 1):
        cluster_count = leaf_count >> height
        first_slot = leaf_count - (2 * leaf_count >> height)
        lift_mats = as_float(transfer[0, first_slot : first_slot + cluster_count])
        children = coefficients[-1].reshape(cluster_count, 2 * RANK, columns)
        coefficients.append(jnp.einsum("cra,cav->crv", lift_mats, children, precision=HIGHEST))
    edge_coefs = jnp.stack(
        [
            jnp.concatenate([coefficients[height][:2], coefficients[height][-2:]], 0)
            for height in range(depth_local)
        ],
        0,
    )
    wide_edges = extended_2(edge_coefs.astype(jnp.bfloat16), ((SPACE, 1),), 2).astype(
        edge_coefs.dtype
    )
    fields = []
    for height in range(depth_local):
        cluster_count = leaf_count >> height
        first_slot = 2 * leaf_count - (2 * leaf_count >> height)
        extended = jnp.concatenate(
            [wide_edges[height, :2], coefficients[height], wide_edges[height, 6:]], 0
        )
        stacked = extended[partner_table(cluster_count) + 2].reshape(
            cluster_count, 3 * RANK, columns
        )
        mixers = as_float(coupling[0, first_slot : first_slot + cluster_count])
        fields.append(jnp.einsum("cra,cav->crv", mixers, stacked, precision=HIGHEST))
    device_coupling = as_float(coupling[0, 2 * leaf_count - 2])
    device_coef = coefficients[depth_local][0]
    downward = upper_tree(device_coef, device_coupling, upper_transfer, upper_coupling)
    downward = downward[None]
    for height in range(depth_local - 1, -1, -1):
        cluster_count = leaf_count >> height + 1
        first_slot = leaf_count - (2 * leaf_count >> height + 1)
        lift_mats = as_float(transfer[0, first_slot : first_slot + cluster_count])
        spread = jnp.einsum("cra,crv->cav", lift_mats, downward, precision=HIGHEST)
        downward = fields[height] + spread.reshape(2 * cluster_count, RANK, columns)
    far_field = jnp.einsum(
        "rlp,lrv->lpv", as_float(basis_leaves), downward, precision=HIGHEST
    ).reshape(row_count, columns)
    return (nearby + NUGGET * vectors.astype(jnp.float32) + far_field).astype(jnp.bfloat16)


def solution(mesh):
    devices = mesh.devices.reshape(CUTS + (mesh.shape["vec"],))
    split_mesh = jax.sharding.Mesh(devices, SPACE + ("vec",))
    return jax.shard_map(
        local,
        mesh=split_mesh,
        in_specs=(
            P(SPACE, "vec"),
            P(None, SPACE),
            P(SPACE, None),
            P(None, SPACE),
            P(SPACE, None, None, None),
            P(SPACE, None, None, None),
            P(SPACE, None, None),
            P(SPACE, None, None),
        ),
        out_specs=P(SPACE, "vec"),
        check_vma=False,
    )
```

```python
import jax
import jax.numpy as jnp
import numpy as np
from jax import lax
from jax.sharding import PartitionSpec as P

LEAF = 64
RANK = 32


SCALE_A = 2.0 * 3.0**0.5
VARIANCE = 0.0625
NUGGET = 0.5
HIGHEST = lax.Precision.HIGHEST


def extended_2(cells, sides, width):
    for axis, dim in sides:
        count = lax.axis_size(axis)
        ends = count - 1
        head = lax.slice_in_dim(cells, 0, width, axis=dim)
        tail = lax.slice_in_dim(cells, cells.shape[dim] - width, cells.shape[dim], axis=dim)
        cells = jnp.concatenate(
            [
                lax.ppermute(tail, axis, [(i, (i + 1) % count) for i in range(ends)]),
                cells,
                lax.ppermute(head, axis, [((i + 1) % count, i) for i in range(ends)]),
            ],
            axis=dim,
        )
    return cells


def matern(own_points, other_points):
    difference = own_points[:, :, None, :, None] - other_points[:, :, :, None, :]
    distance = jnp.sqrt(jnp.sum(difference * difference, axis=0))
    return (VARIANCE * (1.0 + SCALE_A * distance) * jnp.exp(-SCALE_A * distance)).astype(
        jnp.bfloat16
    )


def near_field(source, extended_points, index_rows, first_leaf, leaf_zero, leaf_count):
    block_count = index_rows.shape[0]
    col_width = source.shape[1]
    group_size = min(8, block_count)
    source_leaves = source.reshape(leaf_count + 2, LEAF, col_width)
    point_leaves = extended_points.reshape(3, leaf_count + 2, LEAF)
    present = (index_rows >= 0).astype(jnp.bfloat16)
    located = jnp.where(index_rows >= 0, index_rows - leaf_zero + 1, 0)

    def one_group(first_row):
        own_points = lax.dynamic_slice_in_dim(
            point_leaves, first_row + first_leaf + 1, group_size, 1
        )
        blocks = matern(own_points, point_leaves[:, located]) * present[:, :, None, None]
        return jnp.einsum(
            "gkij,gkjv->giv", blocks, source_leaves[located], preferred_element_type=jnp.float32
        )

    starts = jnp.arange(block_count // group_size, dtype=jnp.int32) * group_size
    return lax.map(one_group, starts).reshape(block_count * LEAF, col_width)


def partner_table(cluster_count):
    base = np.arange(cluster_count)
    odd_mask = base % 2 == 1
    return (
        np.stack(
            [np.where(odd_mask, -3, -2), np.where(odd_mask, -2, 2), np.where(odd_mask, 2, 3)], 1
        )
        + base[:, None]
    )


def as_float(matrix):
    return matrix.astype(jnp.float32)


def product(matrix, operand):
    return jnp.dot(matrix, operand, precision=HIGHEST)


SPACE = ("z", "y", "x")
PLANE = ("y", "x")
CUTS = (16, 4, 4)


def neighbours(padded, cluster):
    odd_mask = cluster % 2 == 1
    offsets = (
        jnp.where(odd_mask, -3, -2),
        jnp.where(odd_mask, -2, 2),
        jnp.where(odd_mask, 2, 3),
    )
    picked = [lax.dynamic_index_in_dim(padded, cluster + 3 + step, 0, False) for step in offsets]
    return jnp.concatenate(picked, 0)


def pick(stack, index):
    return lax.dynamic_index_in_dim(stack, index, 0, False)


def lift_up(lift_mats, coefs):
    children = coefs.reshape(lift_mats.shape[0], 2 * RANK, coefs.shape[-1])
    return jnp.einsum("cra,cav->crv", lift_mats, children, precision=HIGHEST)


def rims(own, left_tail, right_head):
    zeros = jnp.zeros((3 - left_tail.shape[0],) + own.shape[1:], own.dtype)
    return jnp.concatenate([zeros, left_tail, own, right_head, zeros], 0)


def doubling_gather(block, axis):
    count = lax.axis_size(axis)
    index = lax.axis_index(axis)
    gathered = block[None]
    step = 1
    while step < count:
        received = lax.ppermute(gathered, axis, [(i, i ^ step) for i in range(count)])
        upper = (index & step) != 0
        gathered = jnp.where(
            upper,
            jnp.concatenate([received, gathered], 0),
            jnp.concatenate([gathered, received], 0),
        )
        step *= 2
    return gathered


def upper_tree(device_coef, device_coupling, upper_transfer, upper_coupling):
    planes = lax.axis_size("z")
    plane_bits = lax.axis_size(PLANE).bit_length() - 1
    plane = lax.axis_index("z")
    seat = lax.axis_index(PLANE)
    matrices = doubling_gather(jnp.concatenate([upper_transfer[0], upper_coupling[0]], 1), PLANE)
    plane_lift_held = matrices[:, :, : 2 * RANK]
    plane_mix_held = matrices[:, :, 2 * RANK :]
    plane_lift = as_float(plane_lift_held)
    plane_mix = as_float(plane_mix_held)
    inner = [doubling_gather(device_coef, PLANE)]
    for height in range(1, plane_bits + 1):
        inner.append(lift_up(plane_lift[2 ** (height - 1) :: 2**height], inner[-1]))
    tails = jnp.concatenate([level[-3:] for level in inner[:plane_bits]], 0)
    heads = jnp.concatenate([level[:3] for level in inner[:plane_bits]], 0)
    from_left = lax.ppermute(tails, "z", [(i, i + 1) for i in range(planes - 1)])
    from_right = lax.ppermute(heads, "z", [(i + 1, i) for i in range(planes - 1)])
    summary = doubling_gather(inner[plane_bits][0], "z")
    outer_matrices = as_float(doubling_gather(matrices[0], "z"))
    outer_lift = outer_matrices[:, :, : 2 * RANK]
    outer_mix = outer_matrices[:, :, 2 * RANK :]
    outer = [summary]
    for height in range(1, (planes.bit_length() - 1) - 1):
        outer.append(lift_up(outer_lift[2 ** (height - 1) :: 2**height], outer[-1]))
    summit = plane_bits + len(outer) - 1
    fields = []
    lifts = []
    done = 0
    for height in range(plane_bits):
        width = min(3, inner[height].shape[0])
        extended = rims(
            inner[height], from_left[done : done + width], from_right[done : done + width]
        )
        done += width
        cluster = seat >> height
        if height == 0:
            mixer = device_coupling
        else:
            mixer = pick(plane_mix, cluster * 2**height + 2 ** (height - 1))
        fields.append(product(mixer, neighbours(extended, cluster)))
        parent = cluster >> 1
        lifts.append((cluster, pick(plane_lift, parent * 2 ** (height + 1) + 2**height)))
    for level, coefs in enumerate(outer):
        height = plane_bits + level
        cluster = plane >> level
        if level == 0:
            mixer = pick(plane_mix, 2 ** (height - 1))
        else:
            mixer = pick(outer_mix, cluster * 2**level + 2 ** (level - 1))
        padded = jnp.pad(coefs, ((3, 3), (0, 0), (0, 0)))
        fields.append(product(mixer, neighbours(padded, cluster)))
        if height < summit:
            parent = cluster >> 1
            lifts.append((cluster, pick(outer_lift, parent * 2 ** (level + 1) + 2**level)))
    downward = fields[summit]
    for height in range(summit - 1, -1, -1):
        cluster, lift = lifts[height]
        half = jnp.where(cluster % 2 == 1, lift[:, RANK:], lift[:, :RANK])
        downward = fields[height] + product(half.T, downward)
    return downward


def local(
    vectors, points, near_index, leaf_basis, transfer, coupling, upper_transfer, upper_coupling
):
    row_count, columns = vectors.shape
    leaf_count = row_count // LEAF
    depth_local = leaf_count.bit_length() - 1
    position = lax.axis_index(SPACE)
    leaf_zero = position * leaf_count
    vector_rims = extended_2(vectors, ((SPACE, 0),), LEAF)
    point_rims = extended_2(points, ((SPACE, 1),), LEAF)
    lane_count = lax.axis_size("vec")
    lane_leaves = leaf_count // lane_count
    first_leaf = lax.axis_index("vec") * lane_leaves
    all_columns = lax.all_gather(vector_rims, "vec", axis=1, tiled=True)
    own_rows = lax.dynamic_slice_in_dim(near_index, first_leaf, lane_leaves, 0)
    half_near = near_field(all_columns, point_rims, own_rows, first_leaf, leaf_zero, leaf_count)
    nearby = lax.all_to_all(half_near, "vec", split_axis=1, concat_axis=0, tiled=True)
    basis_leaves = leaf_basis.reshape(RANK, leaf_count, LEAF)
    leaf_vectors = vectors.reshape(leaf_count, LEAF, columns)
    coefficients = [
        jnp.einsum("rlp,lpv->lrv", basis_leaves, leaf_vectors, preferred_element_type=jnp.float32)
    ]
    for height in range(1, depth_local + 1):
        cluster_count = leaf_count >> height
        first_slot = leaf_count - (2 * leaf_count >> height)
        lift_mats = as_float(transfer[0, first_slot : first_slot + cluster_count])
        children = coefficients[-1].reshape(cluster_count, 2 * RANK, columns)
        coefficients.append(jnp.einsum("cra,cav->crv", lift_mats, children, precision=HIGHEST))
    edge_coefs = jnp.stack(
        [
            jnp.concatenate([coefficients[height][:2], coefficients[height][-2:]], 0)
            for height in range(depth_local)
        ],
        0,
    )
    wide_edges = extended_2(edge_coefs.astype(jnp.bfloat16), ((SPACE, 1),), 2).astype(
        edge_coefs.dtype
    )
    fields = []
    for height in range(depth_local):
        cluster_count = leaf_count >> height
        first_slot = 2 * leaf_count - (2 * leaf_count >> height)
        extended = jnp.concatenate(
            [wide_edges[height, :2], coefficients[height], wide_edges[height, 6:]], 0
        )
        stacked = extended[partner_table(cluster_count) + 2].reshape(
            cluster_count, 3 * RANK, columns
        )
        mixers = as_float(coupling[0, first_slot : first_slot + cluster_count])
        fields.append(jnp.einsum("cra,cav->crv", mixers, stacked, precision=HIGHEST))
    device_coupling = as_float(coupling[0, 2 * leaf_count - 2])
    device_coef = coefficients[depth_local][0]
    downward = upper_tree(device_coef, device_coupling, upper_transfer, upper_coupling)
    downward = downward[None]
    for height in range(depth_local - 1, -1, -1):
        cluster_count = leaf_count >> height + 1
        first_slot = leaf_count - (2 * leaf_count >> height + 1)
        lift_mats = as_float(transfer[0, first_slot : first_slot + cluster_count])
        spread = jnp.einsum("cra,crv->cav", lift_mats, downward, precision=HIGHEST)
        downward = fields[height] + spread.reshape(2 * cluster_count, RANK, columns)
    far_field = jnp.einsum(
        "rlp,lrv->lpv", as_float(basis_leaves), downward, precision=HIGHEST
    ).reshape(row_count, columns)
    return (nearby + NUGGET * vectors.astype(jnp.float32) + far_field).astype(jnp.bfloat16)


def solution(mesh):
    devices = mesh.devices.reshape(CUTS + (mesh.shape["vec"],))
    split_mesh = jax.sharding.Mesh(devices, SPACE + ("vec",))
    return jax.shard_map(
        local,
        mesh=split_mesh,
        in_specs=(
            P(SPACE, "vec"),
            P(None, SPACE),
            P(SPACE, None),
            P(None, SPACE),
            P(SPACE, None, None, None),
            P(SPACE, None, None, None),
            P(SPACE, None, None),
            P(SPACE, None, None),
        ),
        out_specs=P(SPACE, "vec"),
        check_vma=False,
    )
```

```python
import jax
import jax.numpy as jnp
import numpy as np
from jax import lax
from jax.sharding import PartitionSpec as P

LEAF = 64
RANK = 32


SCALE_A = 2.0 * 3.0**0.5
VARIANCE = 0.0625
NUGGET = 0.5
HIGHEST = lax.Precision.HIGHEST


def extended_2(cells, sides, width):
    for axis, dim in sides:
        count = lax.axis_size(axis)
        ends = count - 1
        head = lax.slice_in_dim(cells, 0, width, axis=dim)
        tail = lax.slice_in_dim(cells, cells.shape[dim] - width, cells.shape[dim], axis=dim)
        cells = jnp.concatenate(
            [
                lax.ppermute(tail, axis, [(i, (i + 1) % count) for i in range(ends)]),
                cells,
                lax.ppermute(head, axis, [((i + 1) % count, i) for i in range(ends)]),
            ],
            axis=dim,
        )
    return cells


def matern(own_points, other_points):
    difference = own_points[:, :, None, :, None] - other_points[:, :, :, None, :]
    distance = jnp.sqrt(jnp.sum(difference * difference, axis=0))
    return (VARIANCE * (1.0 + SCALE_A * distance) * jnp.exp(-SCALE_A * distance)).astype(
        jnp.bfloat16
    )


def near_field(source, extended_points, index_rows, first_leaf, leaf_zero, leaf_count):
    block_count = index_rows.shape[0]
    col_width = source.shape[1]
    group_size = block_count
    source_leaves = source.reshape(leaf_count + 2, LEAF, col_width)
    point_leaves = extended_points.reshape(3, leaf_count + 2, LEAF)
    present = (index_rows >= 0).astype(jnp.bfloat16)
    located = jnp.where(index_rows >= 0, index_rows - leaf_zero + 1, 0)

    def one_group(first_row):
        own_points = lax.dynamic_slice_in_dim(
            point_leaves, first_row + first_leaf + 1, group_size, 1
        )
        blocks = matern(own_points, point_leaves[:, located]) * present[:, :, None, None]
        return jnp.einsum(
            "gkij,gkjv->giv", blocks, source_leaves[located], preferred_element_type=jnp.float32
        )

    starts = jnp.arange(block_count // group_size, dtype=jnp.int32) * group_size
    return lax.map(one_group, starts).reshape(block_count * LEAF, col_width)


def partner_table(cluster_count):
    base = np.arange(cluster_count)
    odd_mask = base % 2 == 1
    return (
        np.stack(
            [np.where(odd_mask, -3, -2), np.where(odd_mask, -2, 2), np.where(odd_mask, 2, 3)], 1
        )
        + base[:, None]
    )


def as_float(matrix):
    return matrix.astype(jnp.float32)


def product(matrix, operand):
    return jnp.dot(matrix, operand, precision=HIGHEST)


SPACE = ("z", "y", "x")
PLANE = ("y", "x")
CUTS = (16, 4, 4)


def neighbours(padded, cluster):
    odd_mask = cluster % 2 == 1
    offsets = (
        jnp.where(odd_mask, -3, -2),
        jnp.where(odd_mask, -2, 2),
        jnp.where(odd_mask, 2, 3),
    )
    picked = [lax.dynamic_index_in_dim(padded, cluster + 3 + step, 0, False) for step in offsets]
    return jnp.concatenate(picked, 0)


def pick(stack, index):
    return lax.dynamic_index_in_dim(stack, index, 0, False)


def lift_up(lift_mats, coefs):
    children = coefs.reshape(lift_mats.shape[0], 2 * RANK, coefs.shape[-1])
    return jnp.einsum("cra,cav->crv", lift_mats, children, precision=HIGHEST)


def rims(own, left_tail, right_head):
    zeros = jnp.zeros((3 - left_tail.shape[0],) + own.shape[1:], own.dtype)
    return jnp.concatenate([zeros, left_tail, own, right_head, zeros], 0)


def doubling_gather(block, axis):
    count = lax.axis_size(axis)
    index = lax.axis_index(axis)
    gathered = block[None]
    step = 1
    while step < count:
        received = lax.ppermute(gathered, axis, [(i, i ^ step) for i in range(count)])
        upper = (index & step) != 0
        gathered = jnp.where(
            upper,
            jnp.concatenate([received, gathered], 0),
            jnp.concatenate([gathered, received], 0),
        )
        step *= 2
    return gathered


def upper_tree(device_coef, device_coupling, upper_transfer, upper_coupling):
    planes = lax.axis_size("z")
    plane_bits = lax.axis_size(PLANE).bit_length() - 1
    plane = lax.axis_index("z")
    seat = lax.axis_index(PLANE)
    matrices = as_float(jnp.concatenate([upper_transfer[0], upper_coupling[0]], 1))
    columns = device_coef.shape[1]
    plane_held = doubling_gather(jnp.concatenate([device_coef, matrices], 1), PLANE)
    plane_lift = plane_held[:, :, columns : columns + 2 * RANK]
    plane_mix = plane_held[:, :, columns + 2 * RANK :]
    inner = [plane_held[:, :, :columns]]
    for height in range(1, plane_bits + 1):
        inner.append(lift_up(plane_lift[2 ** (height - 1) :: 2**height], inner[-1]))
    tails = jnp.concatenate([level[-3:] for level in inner[:plane_bits]], 0)
    heads = jnp.concatenate([level[:3] for level in inner[:plane_bits]], 0)
    from_left = lax.ppermute(tails, "z", [(i, i + 1) for i in range(planes - 1)])
    from_right = lax.ppermute(heads, "z", [(i + 1, i) for i in range(planes - 1)])
    outer_held = doubling_gather(
        jnp.concatenate([inner[plane_bits][0], plane_held[0, :, columns:]], 1), "z"
    )
    summary = outer_held[:, :, :columns]
    outer_lift = outer_held[:, :, columns : columns + 2 * RANK]
    outer_mix = outer_held[:, :, columns + 2 * RANK :]
    outer = [summary]
    for height in range(1, (planes.bit_length() - 1) - 1):
        outer.append(lift_up(outer_lift[2 ** (height - 1) :: 2**height], outer[-1]))
    summit = plane_bits + len(outer) - 1
    fields = []
    lifts = []
    done = 0
    for height in range(plane_bits):
        width = min(3, inner[height].shape[0])
        extended = rims(
            inner[height], from_left[done : done + width], from_right[done : done + width]
        )
        done += width
        cluster = seat >> height
        if height == 0:
            mixer = device_coupling
        else:
            mixer = pick(plane_mix, cluster * 2**height + 2 ** (height - 1))
        fields.append(product(mixer, neighbours(extended, cluster)))
        parent = cluster >> 1
        lifts.append((cluster, pick(plane_lift, parent * 2 ** (height + 1) + 2**height)))
    for level, coefs in enumerate(outer):
        height = plane_bits + level
        cluster = plane >> level
        if level == 0:
            mixer = pick(plane_mix, 2 ** (height - 1))
        else:
            mixer = pick(outer_mix, cluster * 2**level + 2 ** (level - 1))
        padded = jnp.pad(coefs, ((3, 3), (0, 0), (0, 0)))
        fields.append(product(mixer, neighbours(padded, cluster)))
        if height < summit:
            parent = cluster >> 1
            lifts.append((cluster, pick(outer_lift, parent * 2 ** (level + 1) + 2**level)))
    downward = fields[summit]
    for height in range(summit - 1, -1, -1):
        cluster, lift = lifts[height]
        half = jnp.where(cluster % 2 == 1, lift[:, RANK:], lift[:, :RANK])
        downward = fields[height] + product(half.T, downward)
    return downward


def local(
    vectors, points, near_index, leaf_basis, transfer, coupling, upper_transfer, upper_coupling
):
    row_count, columns = vectors.shape
    leaf_count = row_count // LEAF
    depth_local = leaf_count.bit_length() - 1
    position = lax.axis_index(SPACE)
    leaf_zero = position * leaf_count
    vector_rims = extended_2(vectors, ((SPACE, 0),), LEAF)
    point_rims = extended_2(points, ((SPACE, 1),), LEAF)
    nearby = near_field(vector_rims, point_rims, near_index, 0, leaf_zero, leaf_count)
    basis_leaves = leaf_basis.reshape(RANK, leaf_count, LEAF)
    leaf_vectors = vectors.reshape(leaf_count, LEAF, columns)
    coefficients = [
        jnp.einsum("rlp,lpv->lrv", basis_leaves, leaf_vectors, preferred_element_type=jnp.float32)
    ]
    for height in range(1, depth_local + 1):
        cluster_count = leaf_count >> height
        first_slot = leaf_count - (2 * leaf_count >> height)
        lift_mats = as_float(transfer[0, first_slot : first_slot + cluster_count])
        children = coefficients[-1].reshape(cluster_count, 2 * RANK, columns)
        coefficients.append(jnp.einsum("cra,cav->crv", lift_mats, children, precision=HIGHEST))
    edge_coefs = jnp.stack(
        [
            jnp.concatenate([coefficients[height][:2], coefficients[height][-2:]], 0)
            for height in range(depth_local)
        ],
        0,
    )
    wide_edges = extended_2(edge_coefs.astype(jnp.bfloat16), ((SPACE, 1),), 2).astype(
        edge_coefs.dtype
    )
    fields = []
    for height in range(depth_local):
        cluster_count = leaf_count >> height
        first_slot = 2 * leaf_count - (2 * leaf_count >> height)
        extended = jnp.concatenate(
            [wide_edges[height, :2], coefficients[height], wide_edges[height, 6:]], 0
        )
        stacked = extended[partner_table(cluster_count) + 2].reshape(
            cluster_count, 3 * RANK, columns
        )
        mixers = as_float(coupling[0, first_slot : first_slot + cluster_count])
        fields.append(jnp.einsum("cra,cav->crv", mixers, stacked, precision=HIGHEST))
    device_coupling = as_float(coupling[0, 2 * leaf_count - 2])
    device_coef = coefficients[depth_local][0]
    downward = upper_tree(device_coef, device_coupling, upper_transfer, upper_coupling)
    downward = downward[None]
    for height in range(depth_local - 1, -1, -1):
        cluster_count = leaf_count >> height + 1
        first_slot = leaf_count - (2 * leaf_count >> height + 1)
        lift_mats = as_float(transfer[0, first_slot : first_slot + cluster_count])
        spread = jnp.einsum("cra,crv->cav", lift_mats, downward, precision=HIGHEST)
        downward = fields[height] + spread.reshape(2 * cluster_count, RANK, columns)
    far_field = jnp.einsum(
        "rlp,lrv->lpv", as_float(basis_leaves), downward, precision=HIGHEST
    ).reshape(row_count, columns)
    return (nearby + NUGGET * vectors.astype(jnp.float32) + far_field).astype(jnp.bfloat16)


def solution(mesh):
    devices = mesh.devices.reshape(CUTS + (mesh.shape["vec"],))
    split_mesh = jax.sharding.Mesh(devices, SPACE + ("vec",))
    return jax.shard_map(
        local,
        mesh=split_mesh,
        in_specs=(
            P(SPACE, "vec"),
            P(None, SPACE),
            P(SPACE, None),
            P(None, SPACE),
            P(SPACE, None, None, None),
            P(SPACE, None, None, None),
            P(SPACE, None, None),
            P(SPACE, None, None),
        ),
        out_specs=P(SPACE, "vec"),
        check_vma=False,
    )
```

```python
import jax
import jax.numpy as jnp
import numpy as np
from jax import lax
from jax.sharding import PartitionSpec as P

LEAF = 64
RANK = 32


SCALE_A = 2.0 * 3.0**0.5
VARIANCE = 0.0625
NUGGET = 0.5
HIGHEST = lax.Precision.HIGHEST


def extended_2(cells, sides, width):
    for axis, dim in sides:
        count = lax.axis_size(axis)
        ends = count - 1
        head = lax.slice_in_dim(cells, 0, width, axis=dim)
        tail = lax.slice_in_dim(cells, cells.shape[dim] - width, cells.shape[dim], axis=dim)
        cells = jnp.concatenate(
            [
                lax.ppermute(tail, axis, [(i, (i + 1) % count) for i in range(ends)]),
                cells,
                lax.ppermute(head, axis, [((i + 1) % count, i) for i in range(ends)]),
            ],
            axis=dim,
        )
    return cells


def matern(own_points, other_points):
    difference = own_points[:, :, None, :, None] - other_points[:, :, :, None, :]
    distance = jnp.sqrt(jnp.sum(difference * difference, axis=0))
    return (VARIANCE * (1.0 + SCALE_A * distance) * jnp.exp(-SCALE_A * distance)).astype(
        jnp.bfloat16
    )


def near_field(source, extended_points, index_rows, first_leaf, leaf_zero, leaf_count):
    block_count = index_rows.shape[0]
    col_width = source.shape[1]
    group_size = block_count
    source_leaves = source.reshape(leaf_count + 2, LEAF, col_width)
    point_leaves = extended_points.reshape(3, leaf_count + 2, LEAF)
    present = (index_rows >= 0).astype(jnp.bfloat16)
    located = jnp.where(index_rows >= 0, index_rows - leaf_zero + 1, 0)

    def one_group(first_row):
        own_points = lax.dynamic_slice_in_dim(
            point_leaves, first_row + first_leaf + 1, group_size, 1
        )
        blocks = matern(own_points, point_leaves[:, located]) * present[:, :, None, None]
        return jnp.einsum(
            "gkij,gkjv->giv", blocks, source_leaves[located], preferred_element_type=jnp.float32
        )

    starts = jnp.arange(block_count // group_size, dtype=jnp.int32) * group_size
    return lax.map(one_group, starts).reshape(block_count * LEAF, col_width)


def partner_table(cluster_count):
    base = np.arange(cluster_count)
    odd_mask = base % 2 == 1
    return (
        np.stack(
            [np.where(odd_mask, -3, -2), np.where(odd_mask, -2, 2), np.where(odd_mask, 2, 3)], 1
        )
        + base[:, None]
    )


def as_float(matrix):
    return matrix.astype(jnp.float32)


def product(matrix, operand):
    return jnp.dot(matrix, operand, precision=HIGHEST)


SPACE = ("z", "y", "x")
PLANE = ("y", "x")
CUTS = (16, 4, 4)


def neighbours(padded, cluster):
    odd_mask = cluster % 2 == 1
    offsets = (
        jnp.where(odd_mask, -3, -2),
        jnp.where(odd_mask, -2, 2),
        jnp.where(odd_mask, 2, 3),
    )
    picked = [lax.dynamic_index_in_dim(padded, cluster + 3 + step, 0, False) for step in offsets]
    return jnp.concatenate(picked, 0)


def pick(stack, index):
    return lax.dynamic_index_in_dim(stack, index, 0, False)


def lift_up(lift_mats, coefs):
    children = coefs.reshape(lift_mats.shape[0], 2 * RANK, coefs.shape[-1])
    return jnp.einsum("cra,cav->crv", lift_mats, children, precision=HIGHEST)


def rims(own, left_tail, right_head):
    zeros = jnp.zeros((3 - left_tail.shape[0],) + own.shape[1:], own.dtype)
    return jnp.concatenate([zeros, left_tail, own, right_head, zeros], 0)


def doubling_gather(block, axis):
    count = lax.axis_size(axis)
    index = lax.axis_index(axis)
    gathered = block[None]
    step = count // 2
    while step >= 1:
        received = lax.ppermute(gathered, axis, [(i, i ^ step) for i in range(count)])
        upper = (index & step) != 0
        gathered = jnp.where(
            upper,
            jnp.concatenate([received, gathered], 0),
            jnp.concatenate([gathered, received], 0),
        )
        step //= 2
    bits = count.bit_length() - 1
    order = [int(format(i, f"0{bits}b")[::-1], 2) for i in range(count)]
    return jnp.take(gathered, np.array(order), axis=0)


def upper_tree(device_coef, device_coupling, upper_transfer, upper_coupling):
    planes = lax.axis_size("z")
    plane_bits = lax.axis_size(PLANE).bit_length() - 1
    plane = lax.axis_index("z")
    seat = lax.axis_index(PLANE)
    matrices = as_float(jnp.concatenate([upper_transfer[0], upper_coupling[0]], 1))
    columns = device_coef.shape[1]
    plane_held = doubling_gather(jnp.concatenate([device_coef, matrices], 1), PLANE)
    plane_lift = plane_held[:, :, columns : columns + 2 * RANK]
    plane_mix = plane_held[:, :, columns + 2 * RANK :]
    inner = [plane_held[:, :, :columns]]
    for height in range(1, plane_bits + 1):
        inner.append(lift_up(plane_lift[2 ** (height - 1) :: 2**height], inner[-1]))
    tails = jnp.concatenate([level[-3:] for level in inner[:plane_bits]], 0)
    heads = jnp.concatenate([level[:3] for level in inner[:plane_bits]], 0)
    from_left = lax.ppermute(tails, "z", [(i, i + 1) for i in range(planes - 1)])
    from_right = lax.ppermute(heads, "z", [(i + 1, i) for i in range(planes - 1)])
    outer_held = doubling_gather(
        jnp.concatenate([inner[plane_bits][0], plane_held[0, :, columns:]], 1), "z"
    )
    summary = outer_held[:, :, :columns]
    outer_lift = outer_held[:, :, columns : columns + 2 * RANK]
    outer_mix = outer_held[:, :, columns + 2 * RANK :]
    outer = [summary]
    for height in range(1, (planes.bit_length() - 1) - 1):
        outer.append(lift_up(outer_lift[2 ** (height - 1) :: 2**height], outer[-1]))
    summit = plane_bits + len(outer) - 1
    fields = []
    lifts = []
    done = 0
    for height in range(plane_bits):
        width = min(3, inner[height].shape[0])
        extended = rims(
            inner[height], from_left[done : done + width], from_right[done : done + width]
        )
        done += width
        cluster = seat >> height
        if height == 0:
            mixer = device_coupling
        else:
            mixer = pick(plane_mix, cluster * 2**height + 2 ** (height - 1))
        fields.append(product(mixer, neighbours(extended, cluster)))
        parent = cluster >> 1
        lifts.append((cluster, pick(plane_lift, parent * 2 ** (height + 1) + 2**height)))
    for level, coefs in enumerate(outer):
        height = plane_bits + level
        cluster = plane >> level
        if level == 0:
            mixer = pick(plane_mix, 2 ** (height - 1))
        else:
            mixer = pick(outer_mix, cluster * 2**level + 2 ** (level - 1))
        padded = jnp.pad(coefs, ((3, 3), (0, 0), (0, 0)))
        fields.append(product(mixer, neighbours(padded, cluster)))
        if height < summit:
            parent = cluster >> 1
            lifts.append((cluster, pick(outer_lift, parent * 2 ** (level + 1) + 2**level)))
    downward = fields[summit]
    for height in range(summit - 1, -1, -1):
        cluster, lift = lifts[height]
        half = jnp.where(cluster % 2 == 1, lift[:, RANK:], lift[:, :RANK])
        downward = fields[height] + product(half.T, downward)
    return downward


def local(
    vectors, points, near_index, leaf_basis, transfer, coupling, upper_transfer, upper_coupling
):
    row_count, columns = vectors.shape
    leaf_count = row_count // LEAF
    depth_local = leaf_count.bit_length() - 1
    position = lax.axis_index(SPACE)
    leaf_zero = position * leaf_count
    vector_rims = extended_2(vectors, ((SPACE, 0),), LEAF)
    point_rims = extended_2(points, ((SPACE, 1),), LEAF)
    nearby = near_field(vector_rims, point_rims, near_index, 0, leaf_zero, leaf_count)
    basis_leaves = leaf_basis.reshape(RANK, leaf_count, LEAF)
    leaf_vectors = vectors.reshape(leaf_count, LEAF, columns)
    coefficients = [
        jnp.einsum("rlp,lpv->lrv", basis_leaves, leaf_vectors, preferred_element_type=jnp.float32)
    ]
    for height in range(1, depth_local + 1):
        cluster_count = leaf_count >> height
        first_slot = leaf_count - (2 * leaf_count >> height)
        lift_mats = as_float(transfer[0, first_slot : first_slot + cluster_count])
        children = coefficients[-1].reshape(cluster_count, 2 * RANK, columns)
        coefficients.append(jnp.einsum("cra,cav->crv", lift_mats, children, precision=HIGHEST))
    edge_coefs = jnp.stack(
        [
            jnp.concatenate([coefficients[height][:2], coefficients[height][-2:]], 0)
            for height in range(depth_local)
        ],
        0,
    )
    wide_edges = extended_2(edge_coefs.astype(jnp.bfloat16), ((SPACE, 1),), 2).astype(
        edge_coefs.dtype
    )
    fields = []
    for height in range(depth_local):
        cluster_count = leaf_count >> height
        first_slot = 2 * leaf_count - (2 * leaf_count >> height)
        extended = jnp.concatenate(
            [wide_edges[height, :2], coefficients[height], wide_edges[height, 6:]], 0
        )
        stacked = extended[partner_table(cluster_count) + 2].reshape(
            cluster_count, 3 * RANK, columns
        )
        mixers = as_float(coupling[0, first_slot : first_slot + cluster_count])
        fields.append(jnp.einsum("cra,cav->crv", mixers, stacked, precision=HIGHEST))
    device_coupling = as_float(coupling[0, 2 * leaf_count - 2])
    device_coef = coefficients[depth_local][0]
    downward = upper_tree(device_coef, device_coupling, upper_transfer, upper_coupling)
    downward = downward[None]
    for height in range(depth_local - 1, -1, -1):
        cluster_count = leaf_count >> height + 1
        first_slot = leaf_count - (2 * leaf_count >> height + 1)
        lift_mats = as_float(transfer[0, first_slot : first_slot + cluster_count])
        spread = jnp.einsum("cra,crv->cav", lift_mats, downward, precision=HIGHEST)
        downward = fields[height] + spread.reshape(2 * cluster_count, RANK, columns)
    far_field = jnp.einsum(
        "rlp,lrv->lpv", as_float(basis_leaves), downward, precision=HIGHEST
    ).reshape(row_count, columns)
    return (nearby + NUGGET * vectors.astype(jnp.float32) + far_field).astype(jnp.bfloat16)


def solution(mesh):
    devices = mesh.devices.reshape(CUTS + (mesh.shape["vec"],))
    split_mesh = jax.sharding.Mesh(devices, SPACE + ("vec",))
    return jax.shard_map(
        local,
        mesh=split_mesh,
        in_specs=(
            P(SPACE, "vec"),
            P(None, SPACE),
            P(SPACE, None),
            P(None, SPACE),
            P(SPACE, None, None, None),
            P(SPACE, None, None, None),
            P(SPACE, None, None),
            P(SPACE, None, None),
        ),
        out_specs=P(SPACE, "vec"),
        check_vma=False,
    )
```

```python
import jax
import jax.numpy as jnp
import numpy as np
from jax import lax
from jax.sharding import PartitionSpec as P

LEAF = 64
RANK = 32


SCALE_A = 2.0 * 3.0**0.5
VARIANCE = 0.0625
NUGGET = 0.5
HIGHEST = lax.Precision.HIGHEST


def matern(own_points, other_points):
    difference = own_points[:, :, None, :, None] - other_points[:, :, :, None, :]
    distance = jnp.sqrt(jnp.sum(difference * difference, axis=0))
    return (VARIANCE * (1.0 + SCALE_A * distance) * jnp.exp(-SCALE_A * distance)).astype(
        jnp.bfloat16
    )


def near_field(source, extended_points, index_rows, first_leaf, leaf_zero, leaf_count):
    block_count = index_rows.shape[0]
    col_width = source.shape[1]
    group_size = block_count
    source_leaves = source.reshape(leaf_count + 2, LEAF, col_width)
    point_leaves = extended_points.reshape(3, leaf_count + 2, LEAF)
    present = (index_rows >= 0).astype(jnp.bfloat16)
    located = jnp.where(index_rows >= 0, index_rows - leaf_zero + 1, 0)

    def one_group(first_row):
        own_points = lax.dynamic_slice_in_dim(
            point_leaves, first_row + first_leaf + 1, group_size, 1
        )
        blocks = matern(own_points, point_leaves[:, located]) * present[:, :, None, None]
        return jnp.einsum(
            "gkij,gkjv->giv", blocks, source_leaves[located], preferred_element_type=jnp.float32
        )

    starts = jnp.arange(block_count // group_size, dtype=jnp.int32) * group_size
    return lax.map(one_group, starts).reshape(block_count * LEAF, col_width)


def partner_table(cluster_count):
    base = np.arange(cluster_count)
    odd_mask = base % 2 == 1
    return (
        np.stack(
            [np.where(odd_mask, -3, -2), np.where(odd_mask, -2, 2), np.where(odd_mask, 2, 3)], 1
        )
        + base[:, None]
    )


def as_float(matrix):
    return matrix.astype(jnp.float32)


def product(matrix, operand):
    return jnp.dot(matrix, operand, precision=HIGHEST)


SPACE = ("z", "y", "x")
PLANE = ("y", "x")
CUTS = (16, 4, 4)


def neighbours(padded, cluster):
    odd_mask = cluster % 2 == 1
    offsets = (
        jnp.where(odd_mask, -3, -2),
        jnp.where(odd_mask, -2, 2),
        jnp.where(odd_mask, 2, 3),
    )
    picked = [lax.dynamic_index_in_dim(padded, cluster + 3 + step, 0, False) for step in offsets]
    return jnp.concatenate(picked, 0)


def pick(stack, index):
    return lax.dynamic_index_in_dim(stack, index, 0, False)


def lift_up(lift_mats, coefs):
    children = coefs.reshape(lift_mats.shape[0], 2 * RANK, coefs.shape[-1])
    return jnp.einsum("cra,cav->crv", lift_mats, children, precision=HIGHEST)


def rims(own, left_tail, right_head):
    zeros = jnp.zeros((3 - left_tail.shape[0],) + own.shape[1:], own.dtype)
    return jnp.concatenate([zeros, left_tail, own, right_head, zeros], 0)


def doubling_gather(block, axis):
    count = lax.axis_size(axis)
    index = lax.axis_index(axis)
    gathered = block[None]
    step = count // 2
    while step >= 1:
        received = lax.ppermute(gathered, axis, [(i, i ^ step) for i in range(count)])
        upper = (index & step) != 0
        gathered = jnp.where(
            upper,
            jnp.concatenate([received, gathered], 0),
            jnp.concatenate([gathered, received], 0),
        )
        step //= 2
    bits = count.bit_length() - 1
    order = [int(format(i, f"0{bits}b")[::-1], 2) for i in range(count)]
    return jnp.take(gathered, np.array(order), axis=0)


def upper_tree(device_coef, device_coupling, upper_transfer, upper_coupling):
    planes = lax.axis_size("z")
    plane_bits = lax.axis_size(PLANE).bit_length() - 1
    plane = lax.axis_index("z")
    seat = lax.axis_index(PLANE)
    matrices = as_float(jnp.concatenate([upper_transfer[0], upper_coupling[0]], 1))
    columns = device_coef.shape[1]
    plane_held = doubling_gather(jnp.concatenate([device_coef, matrices], 1), PLANE)
    plane_lift = plane_held[:, :, columns : columns + 2 * RANK]
    plane_mix = plane_held[:, :, columns + 2 * RANK :]
    inner = [plane_held[:, :, :columns]]
    for height in range(1, plane_bits + 1):
        inner.append(lift_up(plane_lift[2 ** (height - 1) :: 2**height], inner[-1]))
    tails = jnp.concatenate([level[-3:] for level in inner[:plane_bits]], 0)
    heads = jnp.concatenate([level[:3] for level in inner[:plane_bits]], 0)
    from_left = lax.ppermute(tails, "z", [(i, i + 1) for i in range(planes - 1)])
    from_right = lax.ppermute(heads, "z", [(i + 1, i) for i in range(planes - 1)])
    outer_held = doubling_gather(
        jnp.concatenate([inner[plane_bits][0], plane_held[0, :, columns:]], 1), "z"
    )
    summary = outer_held[:, :, :columns]
    outer_lift = outer_held[:, :, columns : columns + 2 * RANK]
    outer_mix = outer_held[:, :, columns + 2 * RANK :]
    outer = [summary]
    for height in range(1, (planes.bit_length() - 1) - 1):
        outer.append(lift_up(outer_lift[2 ** (height - 1) :: 2**height], outer[-1]))
    summit = plane_bits + len(outer) - 1
    fields = []
    lifts = []
    done = 0
    for height in range(plane_bits):
        width = min(3, inner[height].shape[0])
        extended = rims(
            inner[height], from_left[done : done + width], from_right[done : done + width]
        )
        done += width
        cluster = seat >> height
        if height == 0:
            mixer = device_coupling
        else:
            mixer = pick(plane_mix, cluster * 2**height + 2 ** (height - 1))
        fields.append(product(mixer, neighbours(extended, cluster)))
        parent = cluster >> 1
        lifts.append((cluster, pick(plane_lift, parent * 2 ** (height + 1) + 2**height)))
    for level, coefs in enumerate(outer):
        height = plane_bits + level
        cluster = plane >> level
        if level == 0:
            mixer = pick(plane_mix, 2 ** (height - 1))
        else:
            mixer = pick(outer_mix, cluster * 2**level + 2 ** (level - 1))
        padded = jnp.pad(coefs, ((3, 3), (0, 0), (0, 0)))
        fields.append(product(mixer, neighbours(padded, cluster)))
        if height < summit:
            parent = cluster >> 1
            lifts.append((cluster, pick(outer_lift, parent * 2 ** (level + 1) + 2**level)))
    downward = fields[summit]
    for height in range(summit - 1, -1, -1):
        cluster, lift = lifts[height]
        half = jnp.where(cluster % 2 == 1, lift[:, RANK:], lift[:, :RANK])
        downward = fields[height] + product(half.T, downward)
    return downward


def local(
    vectors, points, near_index, leaf_basis, transfer, coupling, upper_transfer, upper_coupling
):
    row_count, columns = vectors.shape
    leaf_count = row_count // LEAF
    depth_local = leaf_count.bit_length() - 1
    position = lax.axis_index(SPACE)
    leaf_zero = position * leaf_count
    basis_leaves = leaf_basis.reshape(RANK, leaf_count, LEAF)
    leaf_vectors = vectors.reshape(leaf_count, LEAF, columns)
    coefficients = [
        jnp.einsum("rlp,lpv->lrv", basis_leaves, leaf_vectors, preferred_element_type=jnp.float32)
    ]
    for height in range(1, depth_local + 1):
        cluster_count = leaf_count >> height
        first_slot = leaf_count - (2 * leaf_count >> height)
        lift_mats = as_float(transfer[0, first_slot : first_slot + cluster_count])
        children = coefficients[-1].reshape(cluster_count, 2 * RANK, columns)
        coefficients.append(jnp.einsum("cra,cav->crv", lift_mats, children, precision=HIGHEST))
    def rim(rows, clusters):
        edges = jnp.stack([coefficients[height][clusters] for height in range(depth_local)], 0)
        parts = [
            vectors[rows].astype(jnp.float32),
            points[:, rows],
            edges.astype(jnp.bfloat16).astype(jnp.float32),
        ]
        return jnp.concatenate([part.reshape(-1) for part in parts]), [p.shape for p in parts]

    head, shapes = rim(slice(0, LEAF), slice(0, 2))
    tail, _ = rim(slice(row_count - LEAF, row_count), slice(-2, None))
    count = lax.axis_size(SPACE)
    from_left = lax.ppermute(tail, SPACE, [(i, i + 1) for i in range(count - 1)])
    from_right = lax.ppermute(head, SPACE, [(i + 1, i) for i in range(count - 1)])

    def unpack(flat):
        pieces, done = [], 0
        for shape in shapes:
            size = int(np.prod(shape))
            pieces.append(flat[done : done + size].reshape(shape))
            done += size
        return pieces

    left_vectors, left_points, left_edges = unpack(from_left)
    right_vectors, right_points, right_edges = unpack(from_right)
    vector_rims = jnp.concatenate(
        [left_vectors.astype(vectors.dtype), vectors, right_vectors.astype(vectors.dtype)], 0
    )
    point_rims = jnp.concatenate([left_points, points, right_points], 1)
    nearby = near_field(vector_rims, point_rims, near_index, 0, leaf_zero, leaf_count)
    fields = []
    for height in range(depth_local):
        cluster_count = leaf_count >> height
        first_slot = 2 * leaf_count - (2 * leaf_count >> height)
        extended = jnp.concatenate([left_edges[height], coefficients[height], right_edges[height]], 0)
        stacked = extended[partner_table(cluster_count) + 2].reshape(
            cluster_count, 3 * RANK, columns
        )
        mixers = as_float(coupling[0, first_slot : first_slot + cluster_count])
        fields.append(jnp.einsum("cra,cav->crv", mixers, stacked, precision=HIGHEST))
    device_coupling = as_float(coupling[0, 2 * leaf_count - 2])
    device_coef = coefficients[depth_local][0]
    downward = upper_tree(device_coef, device_coupling, upper_transfer, upper_coupling)
    downward = downward[None]
    for height in range(depth_local - 1, -1, -1):
        cluster_count = leaf_count >> height + 1
        first_slot = leaf_count - (2 * leaf_count >> height + 1)
        lift_mats = as_float(transfer[0, first_slot : first_slot + cluster_count])
        spread = jnp.einsum("cra,crv->cav", lift_mats, downward, precision=HIGHEST)
        downward = fields[height] + spread.reshape(2 * cluster_count, RANK, columns)
    far_field = jnp.einsum(
        "rlp,lrv->lpv", as_float(basis_leaves), downward, precision=HIGHEST
    ).reshape(row_count, columns)
    return (nearby + NUGGET * vectors.astype(jnp.float32) + far_field).astype(jnp.bfloat16)


def solution(mesh):
    devices = mesh.devices.reshape(CUTS + (mesh.shape["vec"],))
    split_mesh = jax.sharding.Mesh(devices, SPACE + ("vec",))
    return jax.shard_map(
        local,
        mesh=split_mesh,
        in_specs=(
            P(SPACE, "vec"),
            P(None, SPACE),
            P(SPACE, None),
            P(None, SPACE),
            P(SPACE, None, None, None),
            P(SPACE, None, None, None),
            P(SPACE, None, None),
            P(SPACE, None, None),
        ),
        out_specs=P(SPACE, "vec"),
        check_vma=False,
    )
```

```python
import jax
import jax.numpy as jnp
import numpy as np
from jax import lax
from jax.sharding import PartitionSpec as P

LEAF = 64
RANK = 32


SCALE_A = 2.0 * 3.0**0.5
VARIANCE = 0.0625
NUGGET = 0.5
HIGHEST = lax.Precision.HIGHEST


def matern(own_points, other_points):
    difference = own_points[:, :, None, :, None] - other_points[:, :, :, None, :]
    distance = jnp.sqrt(jnp.sum(difference * difference, axis=0))
    return (VARIANCE * (1.0 + SCALE_A * distance) * jnp.exp(-SCALE_A * distance)).astype(
        jnp.bfloat16
    )


def near_field(source, extended_points, index_rows, first_leaf, leaf_zero, leaf_count):
    block_count = index_rows.shape[0]
    col_width = source.shape[1]
    group_size = block_count
    source_leaves = source.reshape(leaf_count + 2, LEAF, col_width)
    point_leaves = extended_points.reshape(3, leaf_count + 2, LEAF)
    present = (index_rows >= 0).astype(jnp.bfloat16)
    located = jnp.where(index_rows >= 0, index_rows - leaf_zero + 1, 0)

    def one_group(first_row):
        own_points = lax.dynamic_slice_in_dim(
            point_leaves, first_row + first_leaf + 1, group_size, 1
        )
        blocks = matern(own_points, point_leaves[:, located]) * present[:, :, None, None]
        return jnp.einsum(
            "gkij,gkjv->giv", blocks, source_leaves[located], preferred_element_type=jnp.float32
        )

    starts = jnp.arange(block_count // group_size, dtype=jnp.int32) * group_size
    return lax.map(one_group, starts).reshape(block_count * LEAF, col_width)


def partner_table(cluster_count):
    base = np.arange(cluster_count)
    odd_mask = base % 2 == 1
    return (
        np.stack(
            [np.where(odd_mask, -3, -2), np.where(odd_mask, -2, 2), np.where(odd_mask, 2, 3)], 1
        )
        + base[:, None]
    )


def as_float(matrix):
    return matrix.astype(jnp.float32)


def product(matrix, operand):
    return jnp.dot(matrix, operand, precision=HIGHEST)


SPACE = ("z", "y", "x")
PLANE = ("y", "x")
CUTS = (16, 4, 4)


def neighbours(padded, cluster):
    odd_mask = cluster % 2 == 1
    offsets = (
        jnp.where(odd_mask, -3, -2),
        jnp.where(odd_mask, -2, 2),
        jnp.where(odd_mask, 2, 3),
    )
    picked = [lax.dynamic_index_in_dim(padded, cluster + 3 + step, 0, False) for step in offsets]
    return jnp.concatenate(picked, 0)


def pick(stack, index):
    return lax.dynamic_index_in_dim(stack, index, 0, False)


def lift_up(lift_mats, coefs):
    children = coefs.reshape(lift_mats.shape[0], 2 * RANK, coefs.shape[-1])
    return jnp.einsum("cra,cav->crv", lift_mats, children, precision=HIGHEST)


def rims(own, left_tail, right_head):
    zeros = jnp.zeros((3 - left_tail.shape[0],) + own.shape[1:], own.dtype)
    return jnp.concatenate([zeros, left_tail, own, right_head, zeros], 0)


def spread_gather(block, axis):
    count = lax.axis_size(axis)
    copies = jnp.broadcast_to(block[None], (count,) + block.shape)
    return lax.all_to_all(copies, axis, 0, 0, tiled=True)


def doubling_gather(block, axis):
    count = lax.axis_size(axis)
    index = lax.axis_index(axis)
    gathered = block[None]
    step = count // 2
    while step >= 1:
        received = lax.ppermute(gathered, axis, [(i, i ^ step) for i in range(count)])
        upper = (index & step) != 0
        gathered = jnp.where(
            upper,
            jnp.concatenate([received, gathered], 0),
            jnp.concatenate([gathered, received], 0),
        )
        step //= 2
    bits = count.bit_length() - 1
    order = [int(format(i, f"0{bits}b")[::-1], 2) for i in range(count)]
    return jnp.take(gathered, np.array(order), axis=0)


def upper_tree(device_coef, device_coupling, upper_transfer, upper_coupling):
    planes = lax.axis_size("z")
    plane_bits = lax.axis_size(PLANE).bit_length() - 1
    plane = lax.axis_index("z")
    seat = lax.axis_index(PLANE)
    matrices = as_float(jnp.concatenate([upper_transfer[0], upper_coupling[0]], 1))
    columns = device_coef.shape[1]
    plane_held = spread_gather(jnp.concatenate([device_coef, matrices], 1), PLANE)
    plane_lift = plane_held[:, :, columns : columns + 2 * RANK]
    plane_mix = plane_held[:, :, columns + 2 * RANK :]
    inner = [plane_held[:, :, :columns]]
    for height in range(1, plane_bits + 1):
        inner.append(lift_up(plane_lift[2 ** (height - 1) :: 2**height], inner[-1]))
    tails = jnp.concatenate([level[-3:] for level in inner[:plane_bits]], 0)
    heads = jnp.concatenate([level[:3] for level in inner[:plane_bits]], 0)
    from_left = lax.ppermute(tails, "z", [(i, i + 1) for i in range(planes - 1)])
    from_right = lax.ppermute(heads, "z", [(i + 1, i) for i in range(planes - 1)])
    outer_held = spread_gather(
        jnp.concatenate([inner[plane_bits][0], plane_held[0, :, columns:]], 1), "z"
    )
    summary = outer_held[:, :, :columns]
    outer_lift = outer_held[:, :, columns : columns + 2 * RANK]
    outer_mix = outer_held[:, :, columns + 2 * RANK :]
    outer = [summary]
    for height in range(1, (planes.bit_length() - 1) - 1):
        outer.append(lift_up(outer_lift[2 ** (height - 1) :: 2**height], outer[-1]))
    summit = plane_bits + len(outer) - 1
    fields = []
    lifts = []
    done = 0
    for height in range(plane_bits):
        width = min(3, inner[height].shape[0])
        extended = rims(
            inner[height], from_left[done : done + width], from_right[done : done + width]
        )
        done += width
        cluster = seat >> height
        if height == 0:
            mixer = device_coupling
        else:
            mixer = pick(plane_mix, cluster * 2**height + 2 ** (height - 1))
        fields.append(product(mixer, neighbours(extended, cluster)))
        parent = cluster >> 1
        lifts.append((cluster, pick(plane_lift, parent * 2 ** (height + 1) + 2**height)))
    for level, coefs in enumerate(outer):
        height = plane_bits + level
        cluster = plane >> level
        if level == 0:
            mixer = pick(plane_mix, 2 ** (height - 1))
        else:
            mixer = pick(outer_mix, cluster * 2**level + 2 ** (level - 1))
        padded = jnp.pad(coefs, ((3, 3), (0, 0), (0, 0)))
        fields.append(product(mixer, neighbours(padded, cluster)))
        if height < summit:
            parent = cluster >> 1
            lifts.append((cluster, pick(outer_lift, parent * 2 ** (level + 1) + 2**level)))
    downward = fields[summit]
    for height in range(summit - 1, -1, -1):
        cluster, lift = lifts[height]
        half = jnp.where(cluster % 2 == 1, lift[:, RANK:], lift[:, :RANK])
        downward = fields[height] + product(half.T, downward)
    return downward


def local(
    vectors, points, near_index, leaf_basis, transfer, coupling, upper_transfer, upper_coupling
):
    row_count, columns = vectors.shape
    leaf_count = row_count // LEAF
    depth_local = leaf_count.bit_length() - 1
    position = lax.axis_index(SPACE)
    leaf_zero = position * leaf_count
    basis_leaves = leaf_basis.reshape(RANK, leaf_count, LEAF)
    leaf_vectors = vectors.reshape(leaf_count, LEAF, columns)
    coefficients = [
        jnp.einsum("rlp,lpv->lrv", basis_leaves, leaf_vectors, preferred_element_type=jnp.float32)
    ]
    for height in range(1, depth_local + 1):
        cluster_count = leaf_count >> height
        first_slot = leaf_count - (2 * leaf_count >> height)
        lift_mats = as_float(transfer[0, first_slot : first_slot + cluster_count])
        children = coefficients[-1].reshape(cluster_count, 2 * RANK, columns)
        coefficients.append(jnp.einsum("cra,cav->crv", lift_mats, children, precision=HIGHEST))
    def rim(rows, clusters):
        edges = jnp.stack([coefficients[height][clusters] for height in range(depth_local)], 0)
        parts = [
            vectors[rows].astype(jnp.float32),
            points[:, rows],
            edges.astype(jnp.bfloat16).astype(jnp.float32),
        ]
        return jnp.concatenate([part.reshape(-1) for part in parts]), [p.shape for p in parts]

    head, shapes = rim(slice(0, LEAF), slice(0, 2))
    tail, _ = rim(slice(row_count - LEAF, row_count), slice(-2, None))
    count = lax.axis_size(SPACE)
    from_left = lax.ppermute(tail, SPACE, [(i, i + 1) for i in range(count - 1)])
    from_right = lax.ppermute(head, SPACE, [(i + 1, i) for i in range(count - 1)])

    def unpack(flat):
        pieces, done = [], 0
        for shape in shapes:
            size = int(np.prod(shape))
            pieces.append(flat[done : done + size].reshape(shape))
            done += size
        return pieces

    left_vectors, left_points, left_edges = unpack(from_left)
    right_vectors, right_points, right_edges = unpack(from_right)
    vector_rims = jnp.concatenate(
        [left_vectors.astype(vectors.dtype), vectors, right_vectors.astype(vectors.dtype)], 0
    )
    point_rims = jnp.concatenate([left_points, points, right_points], 1)
    nearby = near_field(vector_rims, point_rims, near_index, 0, leaf_zero, leaf_count)
    fields = []
    for height in range(depth_local):
        cluster_count = leaf_count >> height
        first_slot = 2 * leaf_count - (2 * leaf_count >> height)
        extended = jnp.concatenate([left_edges[height], coefficients[height], right_edges[height]], 0)
        stacked = extended[partner_table(cluster_count) + 2].reshape(
            cluster_count, 3 * RANK, columns
        )
        mixers = as_float(coupling[0, first_slot : first_slot + cluster_count])
        fields.append(jnp.einsum("cra,cav->crv", mixers, stacked, precision=HIGHEST))
    device_coupling = as_float(coupling[0, 2 * leaf_count - 2])
    device_coef = coefficients[depth_local][0]
    downward = upper_tree(device_coef, device_coupling, upper_transfer, upper_coupling)
    downward = downward[None]
    for height in range(depth_local - 1, -1, -1):
        cluster_count = leaf_count >> height + 1
        first_slot = leaf_count - (2 * leaf_count >> height + 1)
        lift_mats = as_float(transfer[0, first_slot : first_slot + cluster_count])
        spread = jnp.einsum("cra,crv->cav", lift_mats, downward, precision=HIGHEST)
        downward = fields[height] + spread.reshape(2 * cluster_count, RANK, columns)
    far_field = jnp.einsum(
        "rlp,lrv->lpv", as_float(basis_leaves), downward, precision=HIGHEST
    ).reshape(row_count, columns)
    return (nearby + NUGGET * vectors.astype(jnp.float32) + far_field).astype(jnp.bfloat16)


def solution(mesh):
    devices = mesh.devices.reshape(CUTS + (mesh.shape["vec"],))
    split_mesh = jax.sharding.Mesh(devices, SPACE + ("vec",))
    return jax.shard_map(
        local,
        mesh=split_mesh,
        in_specs=(
            P(SPACE, "vec"),
            P(None, SPACE),
            P(SPACE, None),
            P(None, SPACE),
            P(SPACE, None, None, None),
            P(SPACE, None, None, None),
            P(SPACE, None, None),
            P(SPACE, None, None),
        ),
        out_specs=P(SPACE, "vec"),
        check_vma=False,
    )
```

```python
import jax
import jax.numpy as jnp
import numpy as np
from jax import lax
from jax.sharding import PartitionSpec as P

LEAF = 64
RANK = 32


SCALE_A = 2.0 * 3.0**0.5
VARIANCE = 0.0625
NUGGET = 0.5
HIGHEST = lax.Precision.HIGHEST


def matern(own_points, other_points):
    difference = own_points[:, :, None, :, None] - other_points[:, :, :, None, :]
    distance = jnp.sqrt(jnp.sum(difference * difference, axis=0))
    return (VARIANCE * (1.0 + SCALE_A * distance) * jnp.exp(-SCALE_A * distance)).astype(
        jnp.bfloat16
    )


def near_field(source, extended_points, index_rows, first_leaf, leaf_zero, leaf_count):
    block_count = index_rows.shape[0]
    col_width = source.shape[1]
    group_size = block_count
    source_leaves = source.reshape(leaf_count + 2, LEAF, col_width)
    point_leaves = extended_points.reshape(3, leaf_count + 2, LEAF)
    present = (index_rows >= 0).astype(jnp.bfloat16)
    located = jnp.where(index_rows >= 0, index_rows - leaf_zero + 1, 0)

    def one_group(first_row):
        own_points = lax.dynamic_slice_in_dim(
            point_leaves, first_row + first_leaf + 1, group_size, 1
        )
        blocks = matern(own_points, point_leaves[:, located]) * present[:, :, None, None]
        return jnp.einsum(
            "gkij,gkjv->giv", blocks, source_leaves[located], preferred_element_type=jnp.float32
        )

    starts = jnp.arange(block_count // group_size, dtype=jnp.int32) * group_size
    return lax.map(one_group, starts).reshape(block_count * LEAF, col_width)


def partner_table(cluster_count):
    base = np.arange(cluster_count)
    odd_mask = base % 2 == 1
    return (
        np.stack(
            [np.where(odd_mask, -3, -2), np.where(odd_mask, -2, 2), np.where(odd_mask, 2, 3)], 1
        )
        + base[:, None]
    )


def as_float(matrix):
    return matrix.astype(jnp.float32)


def product(matrix, operand):
    return jnp.dot(matrix, operand, precision=HIGHEST)


SPACE = ("z", "y", "x")
PLANE = ("y", "x")
CUTS = (16, 4, 4)


def neighbours(padded, cluster):
    odd_mask = cluster % 2 == 1
    offsets = (
        jnp.where(odd_mask, -3, -2),
        jnp.where(odd_mask, -2, 2),
        jnp.where(odd_mask, 2, 3),
    )
    picked = [lax.dynamic_index_in_dim(padded, cluster + 3 + step, 0, False) for step in offsets]
    return jnp.concatenate(picked, 0)


def pick(stack, index):
    return lax.dynamic_index_in_dim(stack, index, 0, False)


def lift_up(lift_mats, coefs):
    children = coefs.reshape(lift_mats.shape[0], 2 * RANK, coefs.shape[-1])
    return jnp.einsum("cra,cav->crv", lift_mats, children, precision=HIGHEST)


def rims(own, left_tail, right_head):
    zeros = jnp.zeros((3 - left_tail.shape[0],) + own.shape[1:], own.dtype)
    return jnp.concatenate([zeros, left_tail, own, right_head, zeros], 0)


def spread_gather(block, axis):
    count = lax.axis_size(axis)
    copies = jnp.broadcast_to(block[None], (count,) + block.shape)
    return lax.all_to_all(copies, axis, 0, 0, tiled=True)


def doubling_gather(block, axis):
    count = lax.axis_size(axis)
    index = lax.axis_index(axis)
    gathered = block[None]
    step = count // 2
    while step >= 1:
        received = lax.ppermute(gathered, axis, [(i, i ^ step) for i in range(count)])
        upper = (index & step) != 0
        gathered = jnp.where(
            upper,
            jnp.concatenate([received, gathered], 0),
            jnp.concatenate([gathered, received], 0),
        )
        step //= 2
    bits = count.bit_length() - 1
    order = [int(format(i, f"0{bits}b")[::-1], 2) for i in range(count)]
    return jnp.take(gathered, np.array(order), axis=0)


def upper_tree(device_coef, device_coupling, upper_transfer, upper_coupling):
    planes = lax.axis_size("z")
    plane_bits = lax.axis_size(PLANE).bit_length() - 1
    plane = lax.axis_index("z")
    seat = lax.axis_index(PLANE)
    matrices = as_float(jnp.concatenate([upper_transfer[0], upper_coupling[0]], 1))
    columns = device_coef.shape[1]
    plane_held = spread_gather(jnp.concatenate([device_coef, matrices], 1), PLANE)
    plane_lift = plane_held[:, :, columns : columns + 2 * RANK]
    plane_mix = plane_held[:, :, columns + 2 * RANK :]
    inner = [plane_held[:, :, :columns]]
    for height in range(1, plane_bits + 1):
        inner.append(lift_up(plane_lift[2 ** (height - 1) :: 2**height], inner[-1]))
    tails = jnp.concatenate([level[-3:] for level in inner[:plane_bits]], 0)
    heads = jnp.concatenate([level[:3] for level in inner[:plane_bits]], 0)
    from_left = lax.ppermute(tails, "z", [(i, i + 1) for i in range(planes - 1)])
    from_right = lax.ppermute(heads, "z", [(i + 1, i) for i in range(planes - 1)])
    outer_unit = jnp.concatenate([inner[plane_bits][0], plane_held[0, :, columns:]], 1)
    outer_held = as_float(spread_gather(outer_unit.astype(jnp.bfloat16), "z"))
    summary = outer_held[:, :, :columns]
    outer_lift = outer_held[:, :, columns : columns + 2 * RANK]
    outer_mix = outer_held[:, :, columns + 2 * RANK :]
    outer = [summary]
    for height in range(1, (planes.bit_length() - 1) - 1):
        outer.append(lift_up(outer_lift[2 ** (height - 1) :: 2**height], outer[-1]))
    summit = plane_bits + len(outer) - 1
    fields = []
    lifts = []
    done = 0
    for height in range(plane_bits):
        width = min(3, inner[height].shape[0])
        extended = rims(
            inner[height], from_left[done : done + width], from_right[done : done + width]
        )
        done += width
        cluster = seat >> height
        if height == 0:
            mixer = device_coupling
        else:
            mixer = pick(plane_mix, cluster * 2**height + 2 ** (height - 1))
        fields.append(product(mixer, neighbours(extended, cluster)))
        parent = cluster >> 1
        lifts.append((cluster, pick(plane_lift, parent * 2 ** (height + 1) + 2**height)))
    for level, coefs in enumerate(outer):
        height = plane_bits + level
        cluster = plane >> level
        if level == 0:
            mixer = pick(plane_mix, 2 ** (height - 1))
        else:
            mixer = pick(outer_mix, cluster * 2**level + 2 ** (level - 1))
        padded = jnp.pad(coefs, ((3, 3), (0, 0), (0, 0)))
        fields.append(product(mixer, neighbours(padded, cluster)))
        if height < summit:
            parent = cluster >> 1
            lifts.append((cluster, pick(outer_lift, parent * 2 ** (level + 1) + 2**level)))
    downward = fields[summit]
    for height in range(summit - 1, -1, -1):
        cluster, lift = lifts[height]
        half = jnp.where(cluster % 2 == 1, lift[:, RANK:], lift[:, :RANK])
        downward = fields[height] + product(half.T, downward)
    return downward


def local(
    vectors, points, near_index, leaf_basis, transfer, coupling, upper_transfer, upper_coupling
):
    row_count, columns = vectors.shape
    leaf_count = row_count // LEAF
    depth_local = leaf_count.bit_length() - 1
    position = lax.axis_index(SPACE)
    leaf_zero = position * leaf_count
    basis_leaves = leaf_basis.reshape(RANK, leaf_count, LEAF)
    leaf_vectors = vectors.reshape(leaf_count, LEAF, columns)
    coefficients = [
        jnp.einsum("rlp,lpv->lrv", basis_leaves, leaf_vectors, preferred_element_type=jnp.float32)
    ]
    for height in range(1, depth_local + 1):
        cluster_count = leaf_count >> height
        first_slot = leaf_count - (2 * leaf_count >> height)
        lift_mats = as_float(transfer[0, first_slot : first_slot + cluster_count])
        children = coefficients[-1].reshape(cluster_count, 2 * RANK, columns)
        coefficients.append(jnp.einsum("cra,cav->crv", lift_mats, children, precision=HIGHEST))
    def rim(rows, clusters):
        edges = jnp.stack([coefficients[height][clusters] for height in range(depth_local)], 0)
        parts = [
            vectors[rows].astype(jnp.float32),
            points[:, rows],
            edges.astype(jnp.bfloat16).astype(jnp.float32),
        ]
        return jnp.concatenate([part.reshape(-1) for part in parts]), [p.shape for p in parts]

    head, shapes = rim(slice(0, LEAF), slice(0, 2))
    tail, _ = rim(slice(row_count - LEAF, row_count), slice(-2, None))
    count = lax.axis_size(SPACE)
    from_left = lax.ppermute(tail, SPACE, [(i, i + 1) for i in range(count - 1)])
    from_right = lax.ppermute(head, SPACE, [(i + 1, i) for i in range(count - 1)])

    def unpack(flat):
        pieces, done = [], 0
        for shape in shapes:
            size = int(np.prod(shape))
            pieces.append(flat[done : done + size].reshape(shape))
            done += size
        return pieces

    left_vectors, left_points, left_edges = unpack(from_left)
    right_vectors, right_points, right_edges = unpack(from_right)
    vector_rims = jnp.concatenate(
        [left_vectors.astype(vectors.dtype), vectors, right_vectors.astype(vectors.dtype)], 0
    )
    point_rims = jnp.concatenate([left_points, points, right_points], 1)
    nearby = near_field(vector_rims, point_rims, near_index, 0, leaf_zero, leaf_count)
    fields = []
    for height in range(depth_local):
        cluster_count = leaf_count >> height
        first_slot = 2 * leaf_count - (2 * leaf_count >> height)
        extended = jnp.concatenate([left_edges[height], coefficients[height], right_edges[height]], 0)
        stacked = extended[partner_table(cluster_count) + 2].reshape(
            cluster_count, 3 * RANK, columns
        )
        mixers = as_float(coupling[0, first_slot : first_slot + cluster_count])
        fields.append(jnp.einsum("cra,cav->crv", mixers, stacked, precision=HIGHEST))
    device_coupling = as_float(coupling[0, 2 * leaf_count - 2])
    device_coef = coefficients[depth_local][0]
    downward = upper_tree(device_coef, device_coupling, upper_transfer, upper_coupling)
    downward = downward[None]
    for height in range(depth_local - 1, -1, -1):
        cluster_count = leaf_count >> height + 1
        first_slot = leaf_count - (2 * leaf_count >> height + 1)
        lift_mats = as_float(transfer[0, first_slot : first_slot + cluster_count])
        spread = jnp.einsum("cra,crv->cav", lift_mats, downward, precision=HIGHEST)
        downward = fields[height] + spread.reshape(2 * cluster_count, RANK, columns)
    far_field = jnp.einsum(
        "rlp,lrv->lpv", as_float(basis_leaves), downward, precision=HIGHEST
    ).reshape(row_count, columns)
    return (nearby + NUGGET * vectors.astype(jnp.float32) + far_field).astype(jnp.bfloat16)


def solution(mesh):
    devices = mesh.devices.reshape(CUTS + (mesh.shape["vec"],))
    split_mesh = jax.sharding.Mesh(devices, SPACE + ("vec",))
    return jax.shard_map(
        local,
        mesh=split_mesh,
        in_specs=(
            P(SPACE, "vec"),
            P(None, SPACE),
            P(SPACE, None),
            P(None, SPACE),
            P(SPACE, None, None, None),
            P(SPACE, None, None, None),
            P(SPACE, None, None),
            P(SPACE, None, None),
        ),
        out_specs=P(SPACE, "vec"),
        check_vma=False,
    )
```

```python
import jax
import jax.numpy as jnp
import numpy as np
from jax import lax
from jax.sharding import PartitionSpec as P

LEAF = 64
RANK = 32


SCALE_A = 2.0 * 3.0**0.5
VARIANCE = 0.0625
NUGGET = 0.5
HIGHEST = lax.Precision.HIGHEST


def matern(own_points, other_points):
    difference = own_points[:, :, None, :, None] - other_points[:, :, :, None, :]
    distance = jnp.sqrt(jnp.sum(difference * difference, axis=0))
    return (VARIANCE * (1.0 + SCALE_A * distance) * jnp.exp(-SCALE_A * distance)).astype(
        jnp.bfloat16
    )


def near_field(source, extended_points, index_rows, first_leaf, leaf_zero, leaf_count):
    block_count = index_rows.shape[0]
    col_width = source.shape[1]
    group_size = block_count
    source_leaves = source.reshape(leaf_count + 2, LEAF, col_width)
    point_leaves = extended_points.reshape(3, leaf_count + 2, LEAF)
    present = (index_rows >= 0).astype(jnp.bfloat16)
    located = jnp.where(index_rows >= 0, index_rows - leaf_zero + 1, 0)

    def one_group(first_row):
        own_points = lax.dynamic_slice_in_dim(
            point_leaves, first_row + first_leaf + 1, group_size, 1
        )
        blocks = matern(own_points, point_leaves[:, located]) * present[:, :, None, None]
        return jnp.einsum(
            "gkij,gkjv->giv", blocks, source_leaves[located], preferred_element_type=jnp.float32
        )

    starts = jnp.arange(block_count // group_size, dtype=jnp.int32) * group_size
    return lax.map(one_group, starts).reshape(block_count * LEAF, col_width)


def partner_table(cluster_count):
    base = np.arange(cluster_count)
    odd_mask = base % 2 == 1
    return (
        np.stack(
            [np.where(odd_mask, -3, -2), np.where(odd_mask, -2, 2), np.where(odd_mask, 2, 3)], 1
        )
        + base[:, None]
    )


def as_float(matrix):
    return matrix.astype(jnp.float32)


def product(matrix, operand):
    return jnp.dot(matrix, operand, precision=HIGHEST)


SPACE = ("z", "y", "x")
PLANE = ("y", "x")
CUTS = (16, 4, 4)


def neighbours(padded, cluster):
    odd_mask = cluster % 2 == 1
    offsets = (
        jnp.where(odd_mask, -3, -2),
        jnp.where(odd_mask, -2, 2),
        jnp.where(odd_mask, 2, 3),
    )
    picked = [lax.dynamic_index_in_dim(padded, cluster + 3 + step, 0, False) for step in offsets]
    return jnp.concatenate(picked, 0)


def pick(stack, index):
    return lax.dynamic_index_in_dim(stack, index, 0, False)


def lift_up(lift_mats, coefs):
    children = coefs.reshape(lift_mats.shape[0], 2 * RANK, coefs.shape[-1])
    return jnp.einsum("cra,cav->crv", lift_mats, children, precision=HIGHEST)


def rims(own, left_tail, right_head):
    zeros = jnp.zeros((3 - left_tail.shape[0],) + own.shape[1:], own.dtype)
    return jnp.concatenate([zeros, left_tail, own, right_head, zeros], 0)


def spread_gather(block, axis):
    count = lax.axis_size(axis)
    copies = jnp.broadcast_to(block[None], (count,) + block.shape)
    return lax.all_to_all(copies, axis, 0, 0, tiled=True)


def doubling_gather(block, axis):
    count = lax.axis_size(axis)
    index = lax.axis_index(axis)
    gathered = block[None]
    step = count // 2
    while step >= 1:
        received = lax.ppermute(gathered, axis, [(i, i ^ step) for i in range(count)])
        upper = (index & step) != 0
        gathered = jnp.where(
            upper,
            jnp.concatenate([received, gathered], 0),
            jnp.concatenate([gathered, received], 0),
        )
        step //= 2
    bits = count.bit_length() - 1
    order = [int(format(i, f"0{bits}b")[::-1], 2) for i in range(count)]
    return jnp.take(gathered, np.array(order), axis=0)


def upper_tree(device_coef, device_coupling, upper_transfer, upper_coupling, held, late):
    planes = lax.axis_size("z")
    plane_bits = lax.axis_size(PLANE).bit_length() - 1
    plane = lax.axis_index("z")
    seat = lax.axis_index(PLANE)
    matrices = as_float(jnp.concatenate([upper_transfer[0], upper_coupling[0]], 1))
    columns = device_coef.shape[1]
    plane_held = spread_gather(jnp.concatenate([device_coef, matrices], 1), PLANE)
    plane_lift = plane_held[:, :, columns : columns + 2 * RANK]
    plane_mix = plane_held[:, :, columns + 2 * RANK :]
    inner = [plane_held[:, :, :columns]]
    for height in range(1, plane_bits + 1):
        inner.append(lift_up(plane_lift[2 ** (height - 1) :: 2**height], inner[-1]))
    tails = jnp.concatenate([level[-3:] for level in inner[:plane_bits]], 0)
    heads = jnp.concatenate([level[:3] for level in inner[:plane_bits]], 0)
    from_left = lax.ppermute(tails, "z", [(i, i + 1) for i in range(planes - 1)])
    from_right = lax.ppermute(heads, "z", [(i + 1, i) for i in range(planes - 1)])
    outer_unit = jnp.concatenate([inner[plane_bits][0], plane_held[0, :, columns:]], 1)
    outer_unit, held = lax.optimization_barrier((outer_unit.astype(jnp.bfloat16), held))
    outer_held = as_float(spread_gather(outer_unit, "z"))
    late_result = late(held)
    summary = outer_held[:, :, :columns]
    outer_lift = outer_held[:, :, columns : columns + 2 * RANK]
    outer_mix = outer_held[:, :, columns + 2 * RANK :]
    outer = [summary]
    for height in range(1, (planes.bit_length() - 1) - 1):
        outer.append(lift_up(outer_lift[2 ** (height - 1) :: 2**height], outer[-1]))
    summit = plane_bits + len(outer) - 1
    fields = []
    lifts = []
    done = 0
    for height in range(plane_bits):
        width = min(3, inner[height].shape[0])
        extended = rims(
            inner[height], from_left[done : done + width], from_right[done : done + width]
        )
        done += width
        cluster = seat >> height
        if height == 0:
            mixer = device_coupling
        else:
            mixer = pick(plane_mix, cluster * 2**height + 2 ** (height - 1))
        fields.append(product(mixer, neighbours(extended, cluster)))
        parent = cluster >> 1
        lifts.append((cluster, pick(plane_lift, parent * 2 ** (height + 1) + 2**height)))
    for level, coefs in enumerate(outer):
        height = plane_bits + level
        cluster = plane >> level
        if level == 0:
            mixer = pick(plane_mix, 2 ** (height - 1))
        else:
            mixer = pick(outer_mix, cluster * 2**level + 2 ** (level - 1))
        padded = jnp.pad(coefs, ((3, 3), (0, 0), (0, 0)))
        fields.append(product(mixer, neighbours(padded, cluster)))
        if height < summit:
            parent = cluster >> 1
            lifts.append((cluster, pick(outer_lift, parent * 2 ** (level + 1) + 2**level)))
    downward = fields[summit]
    for height in range(summit - 1, -1, -1):
        cluster, lift = lifts[height]
        half = jnp.where(cluster % 2 == 1, lift[:, RANK:], lift[:, :RANK])
        downward = fields[height] + product(half.T, downward)
    return downward, late_result


def local(
    vectors, points, near_index, leaf_basis, transfer, coupling, upper_transfer, upper_coupling
):
    row_count, columns = vectors.shape
    leaf_count = row_count // LEAF
    depth_local = leaf_count.bit_length() - 1
    position = lax.axis_index(SPACE)
    leaf_zero = position * leaf_count
    basis_leaves = leaf_basis.reshape(RANK, leaf_count, LEAF)
    leaf_vectors = vectors.reshape(leaf_count, LEAF, columns)
    coefficients = [
        jnp.einsum("rlp,lpv->lrv", basis_leaves, leaf_vectors, preferred_element_type=jnp.float32)
    ]
    for height in range(1, depth_local + 1):
        cluster_count = leaf_count >> height
        first_slot = leaf_count - (2 * leaf_count >> height)
        lift_mats = as_float(transfer[0, first_slot : first_slot + cluster_count])
        children = coefficients[-1].reshape(cluster_count, 2 * RANK, columns)
        coefficients.append(jnp.einsum("cra,cav->crv", lift_mats, children, precision=HIGHEST))
    def rim(rows, clusters):
        edges = jnp.stack([coefficients[height][clusters] for height in range(depth_local)], 0)
        parts = [
            vectors[rows].astype(jnp.float32),
            points[:, rows],
            edges.astype(jnp.bfloat16).astype(jnp.float32),
        ]
        return jnp.concatenate([part.reshape(-1) for part in parts]), [p.shape for p in parts]

    head, shapes = rim(slice(0, LEAF), slice(0, 2))
    tail, _ = rim(slice(row_count - LEAF, row_count), slice(-2, None))
    count = lax.axis_size(SPACE)
    from_left = lax.ppermute(tail, SPACE, [(i, i + 1) for i in range(count - 1)])
    from_right = lax.ppermute(head, SPACE, [(i + 1, i) for i in range(count - 1)])

    def unpack(flat):
        pieces, done = [], 0
        for shape in shapes:
            size = int(np.prod(shape))
            pieces.append(flat[done : done + size].reshape(shape))
            done += size
        return pieces

    def late(held):
        from_left, from_right = held
        left_vectors, left_points, left_edges = unpack(from_left)
        right_vectors, right_points, right_edges = unpack(from_right)
        vector_rims = jnp.concatenate(
            [left_vectors.astype(vectors.dtype), vectors, right_vectors.astype(vectors.dtype)], 0
        )
        point_rims = jnp.concatenate([left_points, points, right_points], 1)
        nearby = near_field(vector_rims, point_rims, near_index, 0, leaf_zero, leaf_count)
        fields = []
        for height in range(depth_local):
            cluster_count = leaf_count >> height
            first_slot = 2 * leaf_count - (2 * leaf_count >> height)
            extended = jnp.concatenate([left_edges[height], coefficients[height], right_edges[height]], 0)
            stacked = extended[partner_table(cluster_count) + 2].reshape(
                cluster_count, 3 * RANK, columns
            )
            mixers = as_float(coupling[0, first_slot : first_slot + cluster_count])
            fields.append(jnp.einsum("cra,cav->crv", mixers, stacked, precision=HIGHEST))
        return nearby, fields

    device_coupling = as_float(coupling[0, 2 * leaf_count - 2])
    device_coef = coefficients[depth_local][0]
    downward, (nearby, fields) = upper_tree(
        device_coef, device_coupling, upper_transfer, upper_coupling, (from_left, from_right), late
    )
    downward = downward[None]
    for height in range(depth_local - 1, -1, -1):
        cluster_count = leaf_count >> height + 1
        first_slot = leaf_count - (2 * leaf_count >> height + 1)
        lift_mats = as_float(transfer[0, first_slot : first_slot + cluster_count])
        spread = jnp.einsum("cra,crv->cav", lift_mats, downward, precision=HIGHEST)
        downward = fields[height] + spread.reshape(2 * cluster_count, RANK, columns)
    far_field = jnp.einsum(
        "rlp,lrv->lpv", as_float(basis_leaves), downward, precision=HIGHEST
    ).reshape(row_count, columns)
    return (nearby + NUGGET * vectors.astype(jnp.float32) + far_field).astype(jnp.bfloat16)


def solution(mesh):
    devices = mesh.devices.reshape(CUTS + (mesh.shape["vec"],))
    split_mesh = jax.sharding.Mesh(devices, SPACE + ("vec",))
    return jax.shard_map(
        local,
        mesh=split_mesh,
        in_specs=(
            P(SPACE, "vec"),
            P(None, SPACE),
            P(SPACE, None),
            P(None, SPACE),
            P(SPACE, None, None, None),
            P(SPACE, None, None, None),
            P(SPACE, None, None),
            P(SPACE, None, None),
        ),
        out_specs=P(SPACE, "vec"),
        check_vma=False,
    )
```

```python
import jax
import jax.numpy as jnp
import numpy as np
from jax import lax
from jax.sharding import PartitionSpec as P

LEAF = 64
RANK = 32


SCALE_A = 2.0 * 3.0**0.5
VARIANCE = 0.0625
NUGGET = 0.5
HIGHEST = lax.Precision.HIGHEST


def matern(own_points, other_points):
    difference = own_points[:, :, None, :, None] - other_points[:, :, :, None, :]
    distance = jnp.sqrt(jnp.sum(difference * difference, axis=0))
    return (VARIANCE * (1.0 + SCALE_A * distance) * jnp.exp(-SCALE_A * distance)).astype(
        jnp.bfloat16
    )


def near_field(source, extended_points, index_rows, first_leaf, leaf_zero, leaf_count):
    block_count = index_rows.shape[0]
    col_width = source.shape[1]
    group_size = block_count
    source_leaves = source.reshape(leaf_count + 2, LEAF, col_width)
    point_leaves = extended_points.reshape(3, leaf_count + 2, LEAF)
    present = (index_rows >= 0).astype(jnp.bfloat16)
    located = jnp.where(index_rows >= 0, index_rows - leaf_zero + 1, 0)

    def one_group(first_row):
        own_points = lax.dynamic_slice_in_dim(
            point_leaves, first_row + first_leaf + 1, group_size, 1
        )
        blocks = matern(own_points, point_leaves[:, located]) * present[:, :, None, None]
        return jnp.einsum(
            "gkij,gkjv->giv", blocks, source_leaves[located], preferred_element_type=jnp.float32
        )

    starts = jnp.arange(block_count // group_size, dtype=jnp.int32) * group_size
    return lax.map(one_group, starts).reshape(block_count * LEAF, col_width)


def partner_table(cluster_count):
    base = np.arange(cluster_count)
    odd_mask = base % 2 == 1
    return (
        np.stack(
            [np.where(odd_mask, -3, -2), np.where(odd_mask, -2, 2), np.where(odd_mask, 2, 3)], 1
        )
        + base[:, None]
    )


def as_float(matrix):
    return matrix.astype(jnp.float32)


def product(matrix, operand):
    return jnp.dot(matrix, operand, precision=HIGHEST)


SPACE = ("zh", "zl", "y", "x")
DEPTH = ("zh", "zl")
PLANE = ("y", "x")
CUTS = (4, 4, 4, 4)


def neighbours(padded, cluster):
    odd_mask = cluster % 2 == 1
    offsets = (
        jnp.where(odd_mask, -3, -2),
        jnp.where(odd_mask, -2, 2),
        jnp.where(odd_mask, 2, 3),
    )
    picked = [lax.dynamic_index_in_dim(padded, cluster + 3 + step, 0, False) for step in offsets]
    return jnp.concatenate(picked, 0)


def pick(stack, index):
    return lax.dynamic_index_in_dim(stack, index, 0, False)


def lift_up(lift_mats, coefs):
    children = coefs.reshape(lift_mats.shape[0], 2 * RANK, coefs.shape[-1])
    return jnp.einsum("cra,cav->crv", lift_mats, children, precision=HIGHEST)


def rims(own, left_tail, right_head):
    zeros = jnp.zeros((3 - left_tail.shape[0],) + own.shape[1:], own.dtype)
    return jnp.concatenate([zeros, left_tail, own, right_head, zeros], 0)


def spread_gather(block, axis):
    count = lax.axis_size(axis)
    copies = jnp.broadcast_to(block[None], (count,) + block.shape)
    return lax.all_to_all(copies, axis, 0, 0, tiled=True)


def doubling_gather(block, axis):
    count = lax.axis_size(axis)
    index = lax.axis_index(axis)
    gathered = block[None]
    step = count // 2
    while step >= 1:
        received = lax.ppermute(gathered, axis, [(i, i ^ step) for i in range(count)])
        upper = (index & step) != 0
        gathered = jnp.where(
            upper,
            jnp.concatenate([received, gathered], 0),
            jnp.concatenate([gathered, received], 0),
        )
        step //= 2
    bits = count.bit_length() - 1
    order = [int(format(i, f"0{bits}b")[::-1], 2) for i in range(count)]
    return jnp.take(gathered, np.array(order), axis=0)


def upper_tree(device_coef, device_coupling, upper_transfer, upper_coupling, held, late):
    planes = lax.axis_size(DEPTH)
    plane_bits = lax.axis_size(PLANE).bit_length() - 1
    plane = lax.axis_index(DEPTH)
    seat = lax.axis_index(PLANE)
    matrices = as_float(jnp.concatenate([upper_transfer[0], upper_coupling[0]], 1))
    columns = device_coef.shape[1]
    plane_held = spread_gather(jnp.concatenate([device_coef, matrices], 1), PLANE)
    plane_lift = plane_held[:, :, columns : columns + 2 * RANK]
    plane_mix = plane_held[:, :, columns + 2 * RANK :]
    inner = [plane_held[:, :, :columns]]
    for height in range(1, plane_bits + 1):
        inner.append(lift_up(plane_lift[2 ** (height - 1) :: 2**height], inner[-1]))
    tails = jnp.concatenate([level[-3:] for level in inner[:plane_bits]], 0)
    heads = jnp.concatenate([level[:3] for level in inner[:plane_bits]], 0)
    from_left = lax.ppermute(tails, DEPTH, [(i, i + 1) for i in range(planes - 1)])
    from_right = lax.ppermute(heads, DEPTH, [(i + 1, i) for i in range(planes - 1)])
    outer_unit = jnp.concatenate([inner[plane_bits][0], plane_held[0, :, columns:]], 1)
    outer_unit, held = lax.optimization_barrier((outer_unit.astype(jnp.bfloat16), held))
    nearby_planes = spread_gather(outer_unit, "zl")
    outer_held = as_float(spread_gather(nearby_planes, "zh").reshape((planes,) + outer_unit.shape))
    late_result = late(held)
    summary = outer_held[:, :, :columns]
    outer_lift = outer_held[:, :, columns : columns + 2 * RANK]
    outer_mix = outer_held[:, :, columns + 2 * RANK :]
    outer = [summary]
    for height in range(1, (planes.bit_length() - 1) - 1):
        outer.append(lift_up(outer_lift[2 ** (height - 1) :: 2**height], outer[-1]))
    summit = plane_bits + len(outer) - 1
    fields = []
    lifts = []
    done = 0
    for height in range(plane_bits):
        width = min(3, inner[height].shape[0])
        extended = rims(
            inner[height], from_left[done : done + width], from_right[done : done + width]
        )
        done += width
        cluster = seat >> height
        if height == 0:
            mixer = device_coupling
        else:
            mixer = pick(plane_mix, cluster * 2**height + 2 ** (height - 1))
        fields.append(product(mixer, neighbours(extended, cluster)))
        parent = cluster >> 1
        lifts.append((cluster, pick(plane_lift, parent * 2 ** (height + 1) + 2**height)))
    for level, coefs in enumerate(outer):
        height = plane_bits + level
        cluster = plane >> level
        if level == 0:
            mixer = pick(plane_mix, 2 ** (height - 1))
        else:
            mixer = pick(outer_mix, cluster * 2**level + 2 ** (level - 1))
        padded = jnp.pad(coefs, ((3, 3), (0, 0), (0, 0)))
        fields.append(product(mixer, neighbours(padded, cluster)))
        if height < summit:
            parent = cluster >> 1
            lifts.append((cluster, pick(outer_lift, parent * 2 ** (level + 1) + 2**level)))
    downward = fields[summit]
    for height in range(summit - 1, -1, -1):
        cluster, lift = lifts[height]
        half = jnp.where(cluster % 2 == 1, lift[:, RANK:], lift[:, :RANK])
        downward = fields[height] + product(half.T, downward)
    return downward, late_result


def local(
    vectors, points, near_index, leaf_basis, transfer, coupling, upper_transfer, upper_coupling
):
    row_count, columns = vectors.shape
    leaf_count = row_count // LEAF
    depth_local = leaf_count.bit_length() - 1
    position = lax.axis_index(SPACE)
    leaf_zero = position * leaf_count
    basis_leaves = leaf_basis.reshape(RANK, leaf_count, LEAF)
    leaf_vectors = vectors.reshape(leaf_count, LEAF, columns)
    coefficients = [
        jnp.einsum("rlp,lpv->lrv", basis_leaves, leaf_vectors, preferred_element_type=jnp.float32)
    ]
    for height in range(1, depth_local + 1):
        cluster_count = leaf_count >> height
        first_slot = leaf_count - (2 * leaf_count >> height)
        lift_mats = as_float(transfer[0, first_slot : first_slot + cluster_count])
        children = coefficients[-1].reshape(cluster_count, 2 * RANK, columns)
        coefficients.append(jnp.einsum("cra,cav->crv", lift_mats, children, precision=HIGHEST))
    def rim(rows, clusters):
        edges = jnp.stack([coefficients[height][clusters] for height in range(depth_local)], 0)
        parts = [
            vectors[rows].astype(jnp.float32),
            points[:, rows],
            edges.astype(jnp.bfloat16).astype(jnp.float32),
        ]
        return jnp.concatenate([part.reshape(-1) for part in parts]), [p.shape for p in parts]

    head, shapes = rim(slice(0, LEAF), slice(0, 2))
    tail, _ = rim(slice(row_count - LEAF, row_count), slice(-2, None))
    count = lax.axis_size(SPACE)
    from_left = lax.ppermute(tail, SPACE, [(i, i + 1) for i in range(count - 1)])
    from_right = lax.ppermute(head, SPACE, [(i + 1, i) for i in range(count - 1)])

    def unpack(flat):
        pieces, done = [], 0
        for shape in shapes:
            size = int(np.prod(shape))
            pieces.append(flat[done : done + size].reshape(shape))
            done += size
        return pieces

    def late(held):
        from_left, from_right = held
        left_vectors, left_points, left_edges = unpack(from_left)
        right_vectors, right_points, right_edges = unpack(from_right)
        vector_rims = jnp.concatenate(
            [left_vectors.astype(vectors.dtype), vectors, right_vectors.astype(vectors.dtype)], 0
        )
        point_rims = jnp.concatenate([left_points, points, right_points], 1)
        nearby = near_field(vector_rims, point_rims, near_index, 0, leaf_zero, leaf_count)
        fields = []
        for height in range(depth_local):
            cluster_count = leaf_count >> height
            first_slot = 2 * leaf_count - (2 * leaf_count >> height)
            extended = jnp.concatenate([left_edges[height], coefficients[height], right_edges[height]], 0)
            stacked = extended[partner_table(cluster_count) + 2].reshape(
                cluster_count, 3 * RANK, columns
            )
            mixers = as_float(coupling[0, first_slot : first_slot + cluster_count])
            fields.append(jnp.einsum("cra,cav->crv", mixers, stacked, precision=HIGHEST))
        return nearby, fields

    device_coupling = as_float(coupling[0, 2 * leaf_count - 2])
    device_coef = coefficients[depth_local][0]
    downward, (nearby, fields) = upper_tree(
        device_coef, device_coupling, upper_transfer, upper_coupling, (from_left, from_right), late
    )
    downward = downward[None]
    for height in range(depth_local - 1, -1, -1):
        cluster_count = leaf_count >> height + 1
        first_slot = leaf_count - (2 * leaf_count >> height + 1)
        lift_mats = as_float(transfer[0, first_slot : first_slot + cluster_count])
        spread = jnp.einsum("cra,crv->cav", lift_mats, downward, precision=HIGHEST)
        downward = fields[height] + spread.reshape(2 * cluster_count, RANK, columns)
    far_field = jnp.einsum(
        "rlp,lrv->lpv", as_float(basis_leaves), downward, precision=HIGHEST
    ).reshape(row_count, columns)
    return (nearby + NUGGET * vectors.astype(jnp.float32) + far_field).astype(jnp.bfloat16)


def solution(mesh):
    devices = mesh.devices.reshape(CUTS + (mesh.shape["vec"],))
    split_mesh = jax.sharding.Mesh(devices, SPACE + ("vec",))
    return jax.shard_map(
        local,
        mesh=split_mesh,
        in_specs=(
            P(SPACE, "vec"),
            P(None, SPACE),
            P(SPACE, None),
            P(None, SPACE),
            P(SPACE, None, None, None),
            P(SPACE, None, None, None),
            P(SPACE, None, None),
            P(SPACE, None, None),
        ),
        out_specs=P(SPACE, "vec"),
        check_vma=False,
    )
```

```python
import jax
import jax.numpy as jnp
import numpy as np
from jax import lax
from jax.sharding import PartitionSpec as P

LEAF = 64
RANK = 32


SCALE_A = 2.0 * 3.0**0.5
VARIANCE = 0.0625
NUGGET = 0.5
HIGHEST = lax.Precision.HIGHEST


def matern(own_points, other_points):
    difference = own_points[:, :, None, :, None] - other_points[:, :, :, None, :]
    distance = jnp.sqrt(jnp.sum(difference * difference, axis=0))
    return (VARIANCE * (1.0 + SCALE_A * distance) * jnp.exp(-SCALE_A * distance)).astype(
        jnp.bfloat16
    )


def near_field(source, extended_points, index_rows, first_leaf, leaf_zero, leaf_count):
    block_count = index_rows.shape[0]
    col_width = source.shape[1]
    group_size = block_count
    source_leaves = source.reshape(leaf_count + 2, LEAF, col_width)
    point_leaves = extended_points.reshape(3, leaf_count + 2, LEAF)
    present = (index_rows >= 0).astype(jnp.bfloat16)
    located = jnp.where(index_rows >= 0, index_rows - leaf_zero + 1, 0)

    def one_group(first_row):
        own_points = lax.dynamic_slice_in_dim(
            point_leaves, first_row + first_leaf + 1, group_size, 1
        )
        blocks = matern(own_points, point_leaves[:, located]) * present[:, :, None, None]
        return jnp.einsum(
            "gkij,gkjv->giv", blocks, source_leaves[located], preferred_element_type=jnp.float32
        )

    starts = jnp.arange(block_count // group_size, dtype=jnp.int32) * group_size
    return lax.map(one_group, starts).reshape(block_count * LEAF, col_width)


def partner_table(cluster_count):
    base = np.arange(cluster_count)
    odd_mask = base % 2 == 1
    return (
        np.stack(
            [np.where(odd_mask, -3, -2), np.where(odd_mask, -2, 2), np.where(odd_mask, 2, 3)], 1
        )
        + base[:, None]
    )


def as_float(matrix):
    return matrix.astype(jnp.float32)


def product(matrix, operand):
    return jnp.dot(matrix, operand, precision=HIGHEST)


SPACE = ("z", "y", "x")
PLANE = ("y", "x")
CUTS = (16, 4, 4)


def neighbours(padded, cluster):
    odd_mask = cluster % 2 == 1
    offsets = (
        jnp.where(odd_mask, -3, -2),
        jnp.where(odd_mask, -2, 2),
        jnp.where(odd_mask, 2, 3),
    )
    picked = [lax.dynamic_index_in_dim(padded, cluster + 3 + step, 0, False) for step in offsets]
    return jnp.concatenate(picked, 0)


def pick(stack, index):
    return lax.dynamic_index_in_dim(stack, index, 0, False)


def lift_up(lift_mats, coefs):
    children = coefs.reshape(lift_mats.shape[0], 2 * RANK, coefs.shape[-1])
    return jnp.einsum("cra,cav->crv", lift_mats, children, precision=HIGHEST)


def rims(own, left_tail, right_head):
    zeros = jnp.zeros((3 - left_tail.shape[0],) + own.shape[1:], own.dtype)
    return jnp.concatenate([zeros, left_tail, own, right_head, zeros], 0)


def spread_gather(block, axis):
    count = lax.axis_size(axis)
    copies = jnp.broadcast_to(block[None], (count,) + block.shape)
    return lax.all_to_all(copies, axis, 0, 0, tiled=True)


def doubling_gather(block, axis):
    count = lax.axis_size(axis)
    index = lax.axis_index(axis)
    gathered = block[None]
    step = count // 2
    while step >= 1:
        received = lax.ppermute(gathered, axis, [(i, i ^ step) for i in range(count)])
        upper = (index & step) != 0
        gathered = jnp.where(
            upper,
            jnp.concatenate([received, gathered], 0),
            jnp.concatenate([gathered, received], 0),
        )
        step //= 2
    bits = count.bit_length() - 1
    order = [int(format(i, f"0{bits}b")[::-1], 2) for i in range(count)]
    return jnp.take(gathered, np.array(order), axis=0)


def upper_tree(device_coef, device_coupling, upper_transfer, upper_coupling, held, late):
    planes = lax.axis_size("z")
    plane_bits = lax.axis_size(PLANE).bit_length() - 1
    plane = lax.axis_index("z")
    seat = lax.axis_index(PLANE)
    columns = device_coef.shape[1]
    high = device_coef.astype(jnp.bfloat16)
    low = (device_coef - high.astype(jnp.float32)).astype(jnp.bfloat16)
    plane_unit = jnp.concatenate([high, low, upper_transfer[0], upper_coupling[0]], 1)
    plane_sent = spread_gather(plane_unit, PLANE)
    plane_held = as_float(plane_sent[:, :, columns:])
    plane_lift = plane_held[:, :, columns : columns + 2 * RANK]
    plane_mix = plane_held[:, :, columns + 2 * RANK :]
    inner = [as_float(plane_sent[:, :, :columns]) + plane_held[:, :, :columns]]
    for height in range(1, plane_bits + 1):
        inner.append(lift_up(plane_lift[2 ** (height - 1) :: 2**height], inner[-1]))
    tails = jnp.concatenate([level[-3:] for level in inner[:plane_bits]], 0)
    heads = jnp.concatenate([level[:3] for level in inner[:plane_bits]], 0)
    from_left = lax.ppermute(tails, "z", [(i, i + 1) for i in range(planes - 1)])
    from_right = lax.ppermute(heads, "z", [(i + 1, i) for i in range(planes - 1)])
    outer_unit = jnp.concatenate([inner[plane_bits][0], plane_held[0, :, columns:]], 1)
    outer_unit, held = lax.optimization_barrier((outer_unit.astype(jnp.bfloat16), held))
    outer_held = as_float(spread_gather(outer_unit, "z"))
    late_result = late(held)
    summary = outer_held[:, :, :columns]
    outer_lift = outer_held[:, :, columns : columns + 2 * RANK]
    outer_mix = outer_held[:, :, columns + 2 * RANK :]
    outer = [summary]
    for height in range(1, (planes.bit_length() - 1) - 1):
        outer.append(lift_up(outer_lift[2 ** (height - 1) :: 2**height], outer[-1]))
    summit = plane_bits + len(outer) - 1
    fields = []
    lifts = []
    done = 0
    for height in range(plane_bits):
        width = min(3, inner[height].shape[0])
        extended = rims(
            inner[height], from_left[done : done + width], from_right[done : done + width]
        )
        done += width
        cluster = seat >> height
        if height == 0:
            mixer = device_coupling
        else:
            mixer = pick(plane_mix, cluster * 2**height + 2 ** (height - 1))
        fields.append(product(mixer, neighbours(extended, cluster)))
        parent = cluster >> 1
        lifts.append((cluster, pick(plane_lift, parent * 2 ** (height + 1) + 2**height)))
    for level, coefs in enumerate(outer):
        height = plane_bits + level
        cluster = plane >> level
        if level == 0:
            mixer = pick(plane_mix, 2 ** (height - 1))
        else:
            mixer = pick(outer_mix, cluster * 2**level + 2 ** (level - 1))
        padded = jnp.pad(coefs, ((3, 3), (0, 0), (0, 0)))
        fields.append(product(mixer, neighbours(padded, cluster)))
        if height < summit:
            parent = cluster >> 1
            lifts.append((cluster, pick(outer_lift, parent * 2 ** (level + 1) + 2**level)))
    downward = fields[summit]
    for height in range(summit - 1, -1, -1):
        cluster, lift = lifts[height]
        half = jnp.where(cluster % 2 == 1, lift[:, RANK:], lift[:, :RANK])
        downward = fields[height] + product(half.T, downward)
    return downward, late_result


def local(
    vectors, points, near_index, leaf_basis, transfer, coupling, upper_transfer, upper_coupling
):
    row_count, columns = vectors.shape
    leaf_count = row_count // LEAF
    depth_local = leaf_count.bit_length() - 1
    position = lax.axis_index(SPACE)
    leaf_zero = position * leaf_count
    basis_leaves = leaf_basis.reshape(RANK, leaf_count, LEAF)
    leaf_vectors = vectors.reshape(leaf_count, LEAF, columns)
    coefficients = [
        jnp.einsum("rlp,lpv->lrv", basis_leaves, leaf_vectors, preferred_element_type=jnp.float32)
    ]
    for height in range(1, depth_local + 1):
        cluster_count = leaf_count >> height
        first_slot = leaf_count - (2 * leaf_count >> height)
        lift_mats = as_float(transfer[0, first_slot : first_slot + cluster_count])
        children = coefficients[-1].reshape(cluster_count, 2 * RANK, columns)
        coefficients.append(jnp.einsum("cra,cav->crv", lift_mats, children, precision=HIGHEST))
    def rim(rows, clusters):
        edges = jnp.stack([coefficients[height][clusters] for height in range(depth_local)], 0)
        parts = [
            vectors[rows].astype(jnp.float32),
            points[:, rows],
            edges.astype(jnp.bfloat16).astype(jnp.float32),
        ]
        return jnp.concatenate([part.reshape(-1) for part in parts]), [p.shape for p in parts]

    head, shapes = rim(slice(0, LEAF), slice(0, 2))
    tail, _ = rim(slice(row_count - LEAF, row_count), slice(-2, None))
    count = lax.axis_size(SPACE)
    from_left = lax.ppermute(tail, SPACE, [(i, i + 1) for i in range(count - 1)])
    from_right = lax.ppermute(head, SPACE, [(i + 1, i) for i in range(count - 1)])

    def unpack(flat):
        pieces, done = [], 0
        for shape in shapes:
            size = int(np.prod(shape))
            pieces.append(flat[done : done + size].reshape(shape))
            done += size
        return pieces

    def late(held):
        from_left, from_right = held
        left_vectors, left_points, left_edges = unpack(from_left)
        right_vectors, right_points, right_edges = unpack(from_right)
        vector_rims = jnp.concatenate(
            [left_vectors.astype(vectors.dtype), vectors, right_vectors.astype(vectors.dtype)], 0
        )
        point_rims = jnp.concatenate([left_points, points, right_points], 1)
        nearby = near_field(vector_rims, point_rims, near_index, 0, leaf_zero, leaf_count)
        fields = []
        for height in range(depth_local):
            cluster_count = leaf_count >> height
            first_slot = 2 * leaf_count - (2 * leaf_count >> height)
            extended = jnp.concatenate([left_edges[height], coefficients[height], right_edges[height]], 0)
            stacked = extended[partner_table(cluster_count) + 2].reshape(
                cluster_count, 3 * RANK, columns
            )
            mixers = as_float(coupling[0, first_slot : first_slot + cluster_count])
            fields.append(jnp.einsum("cra,cav->crv", mixers, stacked, precision=HIGHEST))
        return nearby, fields

    device_coupling = as_float(coupling[0, 2 * leaf_count - 2])
    device_coef = coefficients[depth_local][0]
    downward, (nearby, fields) = upper_tree(
        device_coef, device_coupling, upper_transfer, upper_coupling, (from_left, from_right), late
    )
    downward = downward[None]
    for height in range(depth_local - 1, -1, -1):
        cluster_count = leaf_count >> height + 1
        first_slot = leaf_count - (2 * leaf_count >> height + 1)
        lift_mats = as_float(transfer[0, first_slot : first_slot + cluster_count])
        spread = jnp.einsum("cra,crv->cav", lift_mats, downward, precision=HIGHEST)
        downward = fields[height] + spread.reshape(2 * cluster_count, RANK, columns)
    far_field = jnp.einsum(
        "rlp,lrv->lpv", as_float(basis_leaves), downward, precision=HIGHEST
    ).reshape(row_count, columns)
    return (nearby + NUGGET * vectors.astype(jnp.float32) + far_field).astype(jnp.bfloat16)


def solution(mesh):
    devices = mesh.devices.reshape(CUTS + (mesh.shape["vec"],))
    split_mesh = jax.sharding.Mesh(devices, SPACE + ("vec",))
    return jax.shard_map(
        local,
        mesh=split_mesh,
        in_specs=(
            P(SPACE, "vec"),
            P(None, SPACE),
            P(SPACE, None),
            P(None, SPACE),
            P(SPACE, None, None, None),
            P(SPACE, None, None, None),
            P(SPACE, None, None),
            P(SPACE, None, None),
        ),
        out_specs=P(SPACE, "vec"),
        check_vma=False,
    )
```

```python
import jax
import jax.numpy as jnp
import numpy as np
from jax import lax
from jax.sharding import PartitionSpec as P

LEAF = 64
RANK = 32


SCALE_A = 2.0 * 3.0**0.5
VARIANCE = 0.0625
NUGGET = 0.5
HIGHEST = lax.Precision.HIGHEST


def matern(own_points, other_points):
    difference = own_points[:, :, None, :, None] - other_points[:, :, :, None, :]
    distance = jnp.sqrt(jnp.sum(difference * difference, axis=0))
    return (VARIANCE * (1.0 + SCALE_A * distance) * jnp.exp(-SCALE_A * distance)).astype(
        jnp.bfloat16
    )


def near_field(source, extended_points, index_rows, first_leaf, leaf_zero, leaf_count):
    block_count = index_rows.shape[0]
    col_width = source.shape[1]
    group_size = block_count
    source_leaves = source.reshape(leaf_count + 2, LEAF, col_width)
    point_leaves = extended_points.reshape(3, leaf_count + 2, LEAF)
    present = (index_rows >= 0).astype(jnp.bfloat16)
    located = jnp.where(index_rows >= 0, index_rows - leaf_zero + 1, 0)

    def one_group(first_row):
        own_points = lax.dynamic_slice_in_dim(
            point_leaves, first_row + first_leaf + 1, group_size, 1
        )
        blocks = matern(own_points, point_leaves[:, located]) * present[:, :, None, None]
        return jnp.einsum(
            "gkij,gkjv->giv", blocks, source_leaves[located], preferred_element_type=jnp.float32
        )

    starts = jnp.arange(block_count // group_size, dtype=jnp.int32) * group_size
    return lax.map(one_group, starts).reshape(block_count * LEAF, col_width)


def partner_table(cluster_count):
    base = np.arange(cluster_count)
    odd_mask = base % 2 == 1
    return (
        np.stack(
            [np.where(odd_mask, -3, -2), np.where(odd_mask, -2, 2), np.where(odd_mask, 2, 3)], 1
        )
        + base[:, None]
    )


def as_float(matrix):
    return matrix.astype(jnp.float32)


def product(matrix, operand):
    return jnp.dot(matrix, operand, precision=HIGHEST)


SPACE = ("z", "y", "x")
PLANE = ("y", "x")
CUTS = (16, 4, 4)


def neighbours(padded, cluster):
    odd_mask = cluster % 2 == 1
    offsets = (
        jnp.where(odd_mask, -3, -2),
        jnp.where(odd_mask, -2, 2),
        jnp.where(odd_mask, 2, 3),
    )
    picked = [lax.dynamic_index_in_dim(padded, cluster + 3 + step, 0, False) for step in offsets]
    return jnp.concatenate(picked, 0)


def pick(stack, index):
    return lax.dynamic_index_in_dim(stack, index, 0, False)


def lift_up(lift_mats, coefs):
    children = coefs.reshape(lift_mats.shape[0], 2 * RANK, coefs.shape[-1])
    return jnp.einsum("cra,cav->crv", lift_mats, children, precision=HIGHEST)


def rims(own, left_tail, right_head):
    zeros = jnp.zeros((3 - left_tail.shape[0],) + own.shape[1:], own.dtype)
    return jnp.concatenate([zeros, left_tail, own, right_head, zeros], 0)


def spread_gather(block, axis):
    count = lax.axis_size(axis)
    copies = jnp.broadcast_to(block[None], (count,) + block.shape)
    return lax.all_to_all(copies, axis, 0, 0, tiled=True)


def doubling_gather(block, axis):
    count = lax.axis_size(axis)
    index = lax.axis_index(axis)
    gathered = block[None]
    step = count // 2
    while step >= 1:
        received = lax.ppermute(gathered, axis, [(i, i ^ step) for i in range(count)])
        upper = (index & step) != 0
        gathered = jnp.where(
            upper,
            jnp.concatenate([received, gathered], 0),
            jnp.concatenate([gathered, received], 0),
        )
        step //= 2
    bits = count.bit_length() - 1
    order = [int(format(i, f"0{bits}b")[::-1], 2) for i in range(count)]
    return jnp.take(gathered, np.array(order), axis=0)


def upper_tree(device_coef, device_coupling, upper_transfer, upper_coupling, held, late):
    planes = lax.axis_size("z")
    plane_bits = lax.axis_size(PLANE).bit_length() - 1
    plane = lax.axis_index("z")
    seat = lax.axis_index(PLANE)
    columns = device_coef.shape[1]
    rounded = lax.reduce_precision(device_coef, exponent_bits=8, mantissa_bits=7)
    high = rounded.astype(jnp.bfloat16)
    low = (device_coef - rounded).astype(jnp.bfloat16)
    plane_unit = jnp.concatenate([high, low, upper_transfer[0], upper_coupling[0]], 1)
    plane_sent = spread_gather(plane_unit, PLANE)
    plane_held = as_float(plane_sent[:, :, columns:])
    plane_lift = plane_held[:, :, columns : columns + 2 * RANK]
    plane_mix = plane_held[:, :, columns + 2 * RANK :]
    inner = [as_float(plane_sent[:, :, :columns]) + plane_held[:, :, :columns]]
    for height in range(1, plane_bits + 1):
        inner.append(lift_up(plane_lift[2 ** (height - 1) :: 2**height], inner[-1]))
    tails = jnp.concatenate([level[-3:] for level in inner[:plane_bits]], 0)
    heads = jnp.concatenate([level[:3] for level in inner[:plane_bits]], 0)
    from_left = lax.ppermute(tails, "z", [(i, i + 1) for i in range(planes - 1)])
    from_right = lax.ppermute(heads, "z", [(i + 1, i) for i in range(planes - 1)])
    outer_unit = jnp.concatenate([inner[plane_bits][0], plane_held[0, :, columns:]], 1)
    outer_unit, held = lax.optimization_barrier((outer_unit.astype(jnp.bfloat16), held))
    outer_held = as_float(spread_gather(outer_unit, "z"))
    late_result = late(held)
    summary = outer_held[:, :, :columns]
    outer_lift = outer_held[:, :, columns : columns + 2 * RANK]
    outer_mix = outer_held[:, :, columns + 2 * RANK :]
    outer = [summary]
    for height in range(1, (planes.bit_length() - 1) - 1):
        outer.append(lift_up(outer_lift[2 ** (height - 1) :: 2**height], outer[-1]))
    summit = plane_bits + len(outer) - 1
    fields = []
    lifts = []
    done = 0
    for height in range(plane_bits):
        width = min(3, inner[height].shape[0])
        extended = rims(
            inner[height], from_left[done : done + width], from_right[done : done + width]
        )
        done += width
        cluster = seat >> height
        if height == 0:
            mixer = device_coupling
        else:
            mixer = pick(plane_mix, cluster * 2**height + 2 ** (height - 1))
        fields.append(product(mixer, neighbours(extended, cluster)))
        parent = cluster >> 1
        lifts.append((cluster, pick(plane_lift, parent * 2 ** (height + 1) + 2**height)))
    for level, coefs in enumerate(outer):
        height = plane_bits + level
        cluster = plane >> level
        if level == 0:
            mixer = pick(plane_mix, 2 ** (height - 1))
        else:
            mixer = pick(outer_mix, cluster * 2**level + 2 ** (level - 1))
        padded = jnp.pad(coefs, ((3, 3), (0, 0), (0, 0)))
        fields.append(product(mixer, neighbours(padded, cluster)))
        if height < summit:
            parent = cluster >> 1
            lifts.append((cluster, pick(outer_lift, parent * 2 ** (level + 1) + 2**level)))
    downward = fields[summit]
    for height in range(summit - 1, -1, -1):
        cluster, lift = lifts[height]
        half = jnp.where(cluster % 2 == 1, lift[:, RANK:], lift[:, :RANK])
        downward = fields[height] + product(half.T, downward)
    return downward, late_result


def local(
    vectors, points, near_index, leaf_basis, transfer, coupling, upper_transfer, upper_coupling
):
    row_count, columns = vectors.shape
    leaf_count = row_count // LEAF
    depth_local = leaf_count.bit_length() - 1
    position = lax.axis_index(SPACE)
    leaf_zero = position * leaf_count
    basis_leaves = leaf_basis.reshape(RANK, leaf_count, LEAF)
    leaf_vectors = vectors.reshape(leaf_count, LEAF, columns)
    coefficients = [
        jnp.einsum("rlp,lpv->lrv", basis_leaves, leaf_vectors, preferred_element_type=jnp.float32)
    ]
    for height in range(1, depth_local + 1):
        cluster_count = leaf_count >> height
        first_slot = leaf_count - (2 * leaf_count >> height)
        lift_mats = as_float(transfer[0, first_slot : first_slot + cluster_count])
        children = coefficients[-1].reshape(cluster_count, 2 * RANK, columns)
        coefficients.append(jnp.einsum("cra,cav->crv", lift_mats, children, precision=HIGHEST))
    def rim(rows, clusters):
        edges = jnp.stack([coefficients[height][clusters] for height in range(depth_local)], 0)
        parts = [
            vectors[rows].astype(jnp.float32),
            points[:, rows],
            edges.astype(jnp.bfloat16).astype(jnp.float32),
        ]
        return jnp.concatenate([part.reshape(-1) for part in parts]), [p.shape for p in parts]

    head, shapes = rim(slice(0, LEAF), slice(0, 2))
    tail, _ = rim(slice(row_count - LEAF, row_count), slice(-2, None))
    count = lax.axis_size(SPACE)
    from_left = lax.ppermute(tail, SPACE, [(i, i + 1) for i in range(count - 1)])
    from_right = lax.ppermute(head, SPACE, [(i + 1, i) for i in range(count - 1)])

    def unpack(flat):
        pieces, done = [], 0
        for shape in shapes:
            size = int(np.prod(shape))
            pieces.append(flat[done : done + size].reshape(shape))
            done += size
        return pieces

    def late(held):
        from_left, from_right = held
        left_vectors, left_points, left_edges = unpack(from_left)
        right_vectors, right_points, right_edges = unpack(from_right)
        vector_rims = jnp.concatenate(
            [left_vectors.astype(vectors.dtype), vectors, right_vectors.astype(vectors.dtype)], 0
        )
        point_rims = jnp.concatenate([left_points, points, right_points], 1)
        nearby = near_field(vector_rims, point_rims, near_index, 0, leaf_zero, leaf_count)
        fields = []
        for height in range(depth_local):
            cluster_count = leaf_count >> height
            first_slot = 2 * leaf_count - (2 * leaf_count >> height)
            extended = jnp.concatenate([left_edges[height], coefficients[height], right_edges[height]], 0)
            stacked = extended[partner_table(cluster_count) + 2].reshape(
                cluster_count, 3 * RANK, columns
            )
            mixers = as_float(coupling[0, first_slot : first_slot + cluster_count])
            fields.append(jnp.einsum("cra,cav->crv", mixers, stacked, precision=HIGHEST))
        return nearby, fields

    device_coupling = as_float(coupling[0, 2 * leaf_count - 2])
    device_coef = coefficients[depth_local][0]
    downward, (nearby, fields) = upper_tree(
        device_coef, device_coupling, upper_transfer, upper_coupling, (from_left, from_right), late
    )
    downward = downward[None]
    for height in range(depth_local - 1, -1, -1):
        cluster_count = leaf_count >> height + 1
        first_slot = leaf_count - (2 * leaf_count >> height + 1)
        lift_mats = as_float(transfer[0, first_slot : first_slot + cluster_count])
        spread = jnp.einsum("cra,crv->cav", lift_mats, downward, precision=HIGHEST)
        downward = fields[height] + spread.reshape(2 * cluster_count, RANK, columns)
    far_field = jnp.einsum(
        "rlp,lrv->lpv", as_float(basis_leaves), downward, precision=HIGHEST
    ).reshape(row_count, columns)
    return (nearby + NUGGET * vectors.astype(jnp.float32) + far_field).astype(jnp.bfloat16)


def solution(mesh):
    devices = mesh.devices.reshape(CUTS + (mesh.shape["vec"],))
    split_mesh = jax.sharding.Mesh(devices, SPACE + ("vec",))
    return jax.shard_map(
        local,
        mesh=split_mesh,
        in_specs=(
            P(SPACE, "vec"),
            P(None, SPACE),
            P(SPACE, None),
            P(None, SPACE),
            P(SPACE, None, None, None),
            P(SPACE, None, None, None),
            P(SPACE, None, None),
            P(SPACE, None, None),
        ),
        out_specs=P(SPACE, "vec"),
        check_vma=False,
    )
```

```python
import jax
import jax.numpy as jnp
import numpy as np
from jax import lax
from jax.sharding import PartitionSpec as P

LEAF = 64
RANK = 32


SCALE_A = 2.0 * 3.0**0.5
VARIANCE = 0.0625
NUGGET = 0.5
HIGHEST = lax.Precision.HIGHEST


def matern(own_points, other_points):
    difference = own_points[:, :, None, :, None] - other_points[:, :, :, None, :]
    distance = jnp.sqrt(jnp.sum(difference * difference, axis=0))
    return (VARIANCE * (1.0 + SCALE_A * distance) * jnp.exp(-SCALE_A * distance)).astype(
        jnp.bfloat16
    )


def near_field(source, extended_points, index_rows, first_leaf, leaf_zero, leaf_count):
    block_count = index_rows.shape[0]
    col_width = source.shape[1]
    group_size = block_count
    source_leaves = source.reshape(leaf_count + 2, LEAF, col_width)
    point_leaves = extended_points.reshape(3, leaf_count + 2, LEAF)
    present = (index_rows >= 0).astype(jnp.bfloat16)
    located = jnp.where(index_rows >= 0, index_rows - leaf_zero + 1, 0)

    def one_group(first_row):
        own_points = lax.dynamic_slice_in_dim(
            point_leaves, first_row + first_leaf + 1, group_size, 1
        )
        blocks = matern(own_points, point_leaves[:, located]) * present[:, :, None, None]
        return jnp.einsum(
            "gkij,gkjv->giv", blocks, source_leaves[located], preferred_element_type=jnp.float32
        )

    starts = jnp.arange(block_count // group_size, dtype=jnp.int32) * group_size
    return lax.map(one_group, starts).reshape(block_count * LEAF, col_width)


def partner_table(cluster_count):
    base = np.arange(cluster_count)
    odd_mask = base % 2 == 1
    return (
        np.stack(
            [np.where(odd_mask, -3, -2), np.where(odd_mask, -2, 2), np.where(odd_mask, 2, 3)], 1
        )
        + base[:, None]
    )


def as_float(matrix):
    return matrix.astype(jnp.float32)


def product(matrix, operand):
    return jnp.dot(matrix, operand, precision=HIGHEST)


SPACE = ("z", "y", "x")
PLANE = ("y", "x")
CUTS = (16, 4, 4)


def neighbours(padded, cluster):
    odd_mask = cluster % 2 == 1
    offsets = (
        jnp.where(odd_mask, -3, -2),
        jnp.where(odd_mask, -2, 2),
        jnp.where(odd_mask, 2, 3),
    )
    picked = [lax.dynamic_index_in_dim(padded, cluster + 3 + step, 0, False) for step in offsets]
    return jnp.concatenate(picked, 0)


def pick(stack, index):
    return lax.dynamic_index_in_dim(stack, index, 0, False)


def lift_up(lift_mats, coefs):
    children = coefs.reshape(lift_mats.shape[0], 2 * RANK, coefs.shape[-1])
    return jnp.einsum("cra,cav->crv", lift_mats, children, precision=HIGHEST)


def rims(own, left_tail, right_head):
    zeros = jnp.zeros((3 - left_tail.shape[0],) + own.shape[1:], own.dtype)
    return jnp.concatenate([zeros, left_tail, own, right_head, zeros], 0)


def spread_gather(block, axis):
    count = lax.axis_size(axis)
    copies = jnp.broadcast_to(block[None], (count,) + block.shape)
    return lax.all_to_all(copies, axis, 0, 0, tiled=True)


def doubling_gather(block, axis):
    count = lax.axis_size(axis)
    index = lax.axis_index(axis)
    gathered = block[None]
    step = count // 2
    while step >= 1:
        received = lax.ppermute(gathered, axis, [(i, i ^ step) for i in range(count)])
        upper = (index & step) != 0
        gathered = jnp.where(
            upper,
            jnp.concatenate([received, gathered], 0),
            jnp.concatenate([gathered, received], 0),
        )
        step //= 2
    bits = count.bit_length() - 1
    order = [int(format(i, f"0{bits}b")[::-1], 2) for i in range(count)]
    return jnp.take(gathered, np.array(order), axis=0)


def upper_tree(device_coef, device_coupling, upper_transfer, upper_coupling, held, late):
    planes = lax.axis_size("z")
    plane_bits = lax.axis_size(PLANE).bit_length() - 1
    plane = lax.axis_index("z")
    seat = lax.axis_index(PLANE)
    columns = device_coef.shape[1]
    rounded = lax.reduce_precision(device_coef, exponent_bits=8, mantissa_bits=7)
    high = rounded.astype(jnp.bfloat16)
    low = (device_coef - rounded).astype(jnp.bfloat16)
    plane_unit = jnp.concatenate([high, low, upper_transfer[0], upper_coupling[0]], 1)
    plane_sent = spread_gather(plane_unit, PLANE)
    plane_held = as_float(plane_sent[:, :, columns:])
    plane_lift = plane_held[:, :, columns : columns + 2 * RANK]
    plane_mix = plane_held[:, :, columns + 2 * RANK :]
    inner = [as_float(plane_sent[:, :, :columns]) + plane_held[:, :, :columns]]
    for height in range(1, plane_bits + 1):
        inner.append(lift_up(plane_lift[2 ** (height - 1) :: 2**height], inner[-1]))
    tails = jnp.concatenate([level[-3:] for level in inner[:plane_bits]], 0)
    heads = jnp.concatenate([level[:3] for level in inner[:plane_bits]], 0)
    from_left = lax.ppermute(tails, "z", [(i, i + 1) for i in range(planes - 1)])
    from_right = lax.ppermute(heads, "z", [(i + 1, i) for i in range(planes - 1)])
    outer_unit = jnp.concatenate([inner[plane_bits][0], plane_held[0, :, columns:]], 1)
    outer_unit, held = lax.optimization_barrier((outer_unit.astype(jnp.bfloat16), held))
    outer_held = as_float(spread_gather(outer_unit, "z"))
    late_result = late(held)
    summary = outer_held[:, :, :columns]
    outer_lift = outer_held[:, :, columns : columns + 2 * RANK]
    outer_mix = outer_held[:, :, columns + 2 * RANK :]
    outer = [summary]
    for height in range(1, (planes.bit_length() - 1) - 1):
        outer.append(lift_up(outer_lift[2 ** (height - 1) :: 2**height], outer[-1]))
    summit = plane_bits + len(outer) - 1
    fields = []
    lifts = []
    done = 0
    for height in range(plane_bits):
        width = min(3, inner[height].shape[0])
        extended = rims(
            inner[height], from_left[done : done + width], from_right[done : done + width]
        )
        done += width
        cluster = seat >> height
        if height == 0:
            mixer = device_coupling
        else:
            mixer = pick(plane_mix, cluster * 2**height + 2 ** (height - 1))
        fields.append(product(mixer, neighbours(extended, cluster)))
        parent = cluster >> 1
        lifts.append((cluster, pick(plane_lift, parent * 2 ** (height + 1) + 2**height)))
    for level, coefs in enumerate(outer):
        height = plane_bits + level
        cluster = plane >> level
        if level == 0:
            mixer = pick(plane_mix, 2 ** (height - 1))
        else:
            mixer = pick(outer_mix, cluster * 2**level + 2 ** (level - 1))
        padded = jnp.pad(coefs, ((3, 3), (0, 0), (0, 0)))
        fields.append(product(mixer, neighbours(padded, cluster)))
        if height < summit:
            parent = cluster >> 1
            lifts.append((cluster, pick(outer_lift, parent * 2 ** (level + 1) + 2**level)))
    prefix = None
    downward = fields[0]
    for height in range(1, summit + 1):
        cluster, lift = lifts[height - 1]
        half = jnp.where(cluster % 2 == 1, lift[:, RANK:], lift[:, :RANK]).T
        prefix = half if prefix is None else product(prefix, half)
        downward = downward + product(prefix, fields[height])
    return downward, late_result


def local(
    vectors, points, near_index, leaf_basis, transfer, coupling, upper_transfer, upper_coupling
):
    row_count, columns = vectors.shape
    leaf_count = row_count // LEAF
    depth_local = leaf_count.bit_length() - 1
    position = lax.axis_index(SPACE)
    leaf_zero = position * leaf_count
    basis_leaves = leaf_basis.reshape(RANK, leaf_count, LEAF)
    leaf_vectors = vectors.reshape(leaf_count, LEAF, columns)
    coefficients = [
        jnp.einsum("rlp,lpv->lrv", basis_leaves, leaf_vectors, preferred_element_type=jnp.float32)
    ]
    for height in range(1, depth_local + 1):
        cluster_count = leaf_count >> height
        first_slot = leaf_count - (2 * leaf_count >> height)
        lift_mats = as_float(transfer[0, first_slot : first_slot + cluster_count])
        children = coefficients[-1].reshape(cluster_count, 2 * RANK, columns)
        coefficients.append(jnp.einsum("cra,cav->crv", lift_mats, children, precision=HIGHEST))
    def rim(rows, clusters):
        edges = jnp.stack([coefficients[height][clusters] for height in range(depth_local)], 0)
        parts = [
            vectors[rows].astype(jnp.float32),
            points[:, rows],
            edges.astype(jnp.bfloat16).astype(jnp.float32),
        ]
        return jnp.concatenate([part.reshape(-1) for part in parts]), [p.shape for p in parts]

    head, shapes = rim(slice(0, LEAF), slice(0, 2))
    tail, _ = rim(slice(row_count - LEAF, row_count), slice(-2, None))
    count = lax.axis_size(SPACE)
    from_left = lax.ppermute(tail, SPACE, [(i, i + 1) for i in range(count - 1)])
    from_right = lax.ppermute(head, SPACE, [(i + 1, i) for i in range(count - 1)])

    def unpack(flat):
        pieces, done = [], 0
        for shape in shapes:
            size = int(np.prod(shape))
            pieces.append(flat[done : done + size].reshape(shape))
            done += size
        return pieces

    def late(held):
        from_left, from_right = held
        left_vectors, left_points, left_edges = unpack(from_left)
        right_vectors, right_points, right_edges = unpack(from_right)
        vector_rims = jnp.concatenate(
            [left_vectors.astype(vectors.dtype), vectors, right_vectors.astype(vectors.dtype)], 0
        )
        point_rims = jnp.concatenate([left_points, points, right_points], 1)
        nearby = near_field(vector_rims, point_rims, near_index, 0, leaf_zero, leaf_count)
        fields = []
        for height in range(depth_local):
            cluster_count = leaf_count >> height
            first_slot = 2 * leaf_count - (2 * leaf_count >> height)
            extended = jnp.concatenate([left_edges[height], coefficients[height], right_edges[height]], 0)
            stacked = extended[partner_table(cluster_count) + 2].reshape(
                cluster_count, 3 * RANK, columns
            )
            mixers = as_float(coupling[0, first_slot : first_slot + cluster_count])
            fields.append(jnp.einsum("cra,cav->crv", mixers, stacked, precision=HIGHEST))
        return nearby, fields

    device_coupling = as_float(coupling[0, 2 * leaf_count - 2])
    device_coef = coefficients[depth_local][0]
    downward, (nearby, fields) = upper_tree(
        device_coef, device_coupling, upper_transfer, upper_coupling, (from_left, from_right), late
    )
    local_down = None
    reach = jnp.eye(RANK, dtype=jnp.float32)[None]
    for height in range(depth_local - 1, -1, -1):
        cluster_count = leaf_count >> height + 1
        first_slot = leaf_count - (2 * leaf_count >> height + 1)
        lift_mats = as_float(transfer[0, first_slot : first_slot + cluster_count])
        reach = jnp.einsum("cra,crk->cak", lift_mats, reach, precision=HIGHEST)
        reach = reach.reshape(2 * cluster_count, RANK, RANK)
        if local_down is None:
            local_down = fields[height]
        else:
            spread = jnp.einsum("cra,crv->cav", lift_mats, local_down, precision=HIGHEST)
            local_down = fields[height] + spread.reshape(2 * cluster_count, RANK, columns)
    basis_float = as_float(basis_leaves)
    reach_rows = jnp.einsum("rlp,lrk->lpk", basis_float, reach, precision=HIGHEST)
    far_field = (
        jnp.einsum("rlp,lrv->lpv", basis_float, local_down, precision=HIGHEST)
        + jnp.einsum("lpk,kv->lpv", reach_rows, downward, precision=HIGHEST)
    ).reshape(row_count, columns)
    return (nearby + NUGGET * vectors.astype(jnp.float32) + far_field).astype(jnp.bfloat16)


def solution(mesh):
    devices = mesh.devices.reshape(CUTS + (mesh.shape["vec"],))
    split_mesh = jax.sharding.Mesh(devices, SPACE + ("vec",))
    return jax.shard_map(
        local,
        mesh=split_mesh,
        in_specs=(
            P(SPACE, "vec"),
            P(None, SPACE),
            P(SPACE, None),
            P(None, SPACE),
            P(SPACE, None, None, None),
            P(SPACE, None, None, None),
            P(SPACE, None, None),
            P(SPACE, None, None),
        ),
        out_specs=P(SPACE, "vec"),
        check_vma=False,
    )
```

```python
import jax
import jax.numpy as jnp
import numpy as np
from jax import lax
from jax.sharding import PartitionSpec as P

LEAF = 64
RANK = 32


SCALE_A = 2.0 * 3.0**0.5
VARIANCE = 0.0625
NUGGET = 0.5
HIGHEST = lax.Precision.HIGHEST


def matern(own_points, other_points):
    difference = own_points[:, :, None, :, None] - other_points[:, :, :, None, :]
    distance = jnp.sqrt(jnp.sum(difference * difference, axis=0))
    return (VARIANCE * (1.0 + SCALE_A * distance) * jnp.exp(-SCALE_A * distance)).astype(
        jnp.bfloat16
    )


def near_field(source, extended_points, index_rows, first_leaf, leaf_zero, leaf_count):
    block_count = index_rows.shape[0]
    col_width = source.shape[1]
    group_size = block_count
    source_leaves = source.reshape(leaf_count + 2, LEAF, col_width)
    point_leaves = extended_points.reshape(3, leaf_count + 2, LEAF)
    present = (index_rows >= 0).astype(jnp.bfloat16)
    located = jnp.where(index_rows >= 0, index_rows - leaf_zero + 1, 0)

    def one_group(first_row):
        own_points = lax.dynamic_slice_in_dim(
            point_leaves, first_row + first_leaf + 1, group_size, 1
        )
        blocks = matern(own_points, point_leaves[:, located]) * present[:, :, None, None]
        return jnp.einsum(
            "gkij,gkjv->giv", blocks, source_leaves[located], preferred_element_type=jnp.float32
        )

    starts = jnp.arange(block_count // group_size, dtype=jnp.int32) * group_size
    return lax.map(one_group, starts).reshape(block_count * LEAF, col_width)


def partner_table(cluster_count):
    base = np.arange(cluster_count)
    odd_mask = base % 2 == 1
    return (
        np.stack(
            [np.where(odd_mask, -3, -2), np.where(odd_mask, -2, 2), np.where(odd_mask, 2, 3)], 1
        )
        + base[:, None]
    )


def as_float(matrix):
    return matrix.astype(jnp.float32)


def product(matrix, operand):
    return jnp.dot(matrix, operand, precision=HIGHEST)


SPACE = ("z", "y", "x")
PLANE = ("y", "x")
CUTS = (16, 4, 4)


def neighbours(padded, cluster):
    odd_mask = cluster % 2 == 1
    offsets = (
        jnp.where(odd_mask, -3, -2),
        jnp.where(odd_mask, -2, 2),
        jnp.where(odd_mask, 2, 3),
    )
    picked = [lax.dynamic_index_in_dim(padded, cluster + 3 + step, 0, False) for step in offsets]
    return jnp.concatenate(picked, 0)


def pick(stack, index):
    return lax.dynamic_index_in_dim(stack, index, 0, False)


def lift_up(lift_mats, coefs):
    children = coefs.reshape(lift_mats.shape[0], 2 * RANK, coefs.shape[-1])
    return jnp.einsum("cra,cav->crv", lift_mats, children, precision=HIGHEST)


def rims(own, left_tail, right_head):
    zeros = jnp.zeros((3 - left_tail.shape[0],) + own.shape[1:], own.dtype)
    return jnp.concatenate([zeros, left_tail, own, right_head, zeros], 0)


def spread_gather(block, axis):
    count = lax.axis_size(axis)
    copies = jnp.broadcast_to(block[None], (count,) + block.shape)
    return lax.all_to_all(copies, axis, 0, 0, tiled=True)


def doubling_gather(block, axis):
    count = lax.axis_size(axis)
    index = lax.axis_index(axis)
    gathered = block[None]
    step = count // 2
    while step >= 1:
        received = lax.ppermute(gathered, axis, [(i, i ^ step) for i in range(count)])
        upper = (index & step) != 0
        gathered = jnp.where(
            upper,
            jnp.concatenate([received, gathered], 0),
            jnp.concatenate([gathered, received], 0),
        )
        step //= 2
    bits = count.bit_length() - 1
    order = [int(format(i, f"0{bits}b")[::-1], 2) for i in range(count)]
    return jnp.take(gathered, np.array(order), axis=0)


def upper_tree(device_coef, device_coupling, upper_transfer, upper_coupling, held, late):
    planes = lax.axis_size("z")
    plane_bits = lax.axis_size(PLANE).bit_length() - 1
    plane = lax.axis_index("z")
    seat = lax.axis_index(PLANE)
    columns = device_coef.shape[1]
    rounded = lax.reduce_precision(device_coef, exponent_bits=8, mantissa_bits=7)
    high = rounded.astype(jnp.bfloat16)
    low = (device_coef - rounded).astype(jnp.bfloat16)
    plane_unit = jnp.concatenate([high, low, upper_transfer[0], upper_coupling[0]], 1)
    plane_sent = spread_gather(plane_unit, PLANE)
    plane_held = as_float(plane_sent[:, :, columns:])
    plane_lift = plane_held[:, :, columns : columns + 2 * RANK]
    plane_mix = plane_held[:, :, columns + 2 * RANK :]
    inner = [as_float(plane_sent[:, :, :columns]) + plane_held[:, :, :columns]]
    for height in range(1, plane_bits + 1):
        inner.append(lift_up(plane_lift[2 ** (height - 1) :: 2**height], inner[-1]))
    tails = jnp.concatenate([level[-3:] for level in inner[:plane_bits]], 0)
    heads = jnp.concatenate([level[:3] for level in inner[:plane_bits]], 0)
    from_left = lax.ppermute(tails, "z", [(i, i + 1) for i in range(planes - 1)])
    from_right = lax.ppermute(heads, "z", [(i + 1, i) for i in range(planes - 1)])
    outer_unit = jnp.concatenate([inner[plane_bits][0], plane_held[0, :, columns:]], 1)
    outer_unit, held, plane_lift, plane_mix = lax.optimization_barrier(
        (outer_unit.astype(jnp.bfloat16), held, plane_lift, plane_mix)
    )
    outer_held = as_float(spread_gather(outer_unit, "z"))
    late_result = late(held)
    summary = outer_held[:, :, :columns]
    outer_lift = outer_held[:, :, columns : columns + 2 * RANK]
    outer_mix = outer_held[:, :, columns + 2 * RANK :]
    outer = [summary]
    for height in range(1, (planes.bit_length() - 1) - 1):
        outer.append(lift_up(outer_lift[2 ** (height - 1) :: 2**height], outer[-1]))
    summit = plane_bits + len(outer) - 1
    fields = []
    lifts = []
    done = 0
    for height in range(plane_bits):
        width = min(3, inner[height].shape[0])
        extended = rims(
            inner[height], from_left[done : done + width], from_right[done : done + width]
        )
        done += width
        cluster = seat >> height
        if height == 0:
            mixer = device_coupling
        else:
            mixer = pick(plane_mix, cluster * 2**height + 2 ** (height - 1))
        fields.append(product(mixer, neighbours(extended, cluster)))
        parent = cluster >> 1
        lifts.append((cluster, pick(plane_lift, parent * 2 ** (height + 1) + 2**height)))
    for level, coefs in enumerate(outer):
        height = plane_bits + level
        cluster = plane >> level
        if level == 0:
            mixer = pick(plane_mix, 2 ** (height - 1))
        else:
            mixer = pick(outer_mix, cluster * 2**level + 2 ** (level - 1))
        padded = jnp.pad(coefs, ((3, 3), (0, 0), (0, 0)))
        fields.append(product(mixer, neighbours(padded, cluster)))
        if height < summit:
            parent = cluster >> 1
            lifts.append((cluster, pick(outer_lift, parent * 2 ** (level + 1) + 2**level)))
    prefix = None
    downward = fields[0]
    for height in range(1, summit + 1):
        cluster, lift = lifts[height - 1]
        half = jnp.where(cluster % 2 == 1, lift[:, RANK:], lift[:, :RANK]).T
        prefix = half if prefix is None else product(prefix, half)
        downward = downward + product(prefix, fields[height])
    return downward, late_result


def local(
    vectors, points, near_index, leaf_basis, transfer, coupling, upper_transfer, upper_coupling
):
    row_count, columns = vectors.shape
    leaf_count = row_count // LEAF
    depth_local = leaf_count.bit_length() - 1
    position = lax.axis_index(SPACE)
    leaf_zero = position * leaf_count
    basis_leaves = leaf_basis.reshape(RANK, leaf_count, LEAF)
    leaf_vectors = vectors.reshape(leaf_count, LEAF, columns)
    coefficients = [
        jnp.einsum("rlp,lpv->lrv", basis_leaves, leaf_vectors, preferred_element_type=jnp.float32)
    ]
    for height in range(1, depth_local + 1):
        cluster_count = leaf_count >> height
        first_slot = leaf_count - (2 * leaf_count >> height)
        lift_mats = as_float(transfer[0, first_slot : first_slot + cluster_count])
        children = coefficients[-1].reshape(cluster_count, 2 * RANK, columns)
        coefficients.append(jnp.einsum("cra,cav->crv", lift_mats, children, precision=HIGHEST))
    def rim(rows, clusters):
        edges = jnp.stack([coefficients[height][clusters] for height in range(depth_local)], 0)
        parts = [
            vectors[rows].astype(jnp.float32),
            points[:, rows],
            edges.astype(jnp.bfloat16).astype(jnp.float32),
        ]
        return jnp.concatenate([part.reshape(-1) for part in parts]), [p.shape for p in parts]

    head, shapes = rim(slice(0, LEAF), slice(0, 2))
    tail, _ = rim(slice(row_count - LEAF, row_count), slice(-2, None))
    count = lax.axis_size(SPACE)
    from_left = lax.ppermute(tail, SPACE, [(i, i + 1) for i in range(count - 1)])
    from_right = lax.ppermute(head, SPACE, [(i + 1, i) for i in range(count - 1)])

    def unpack(flat):
        pieces, done = [], 0
        for shape in shapes:
            size = int(np.prod(shape))
            pieces.append(flat[done : done + size].reshape(shape))
            done += size
        return pieces

    def late(held):
        (from_left, from_right), lift_stack, basis_float = held
        reach = jnp.eye(RANK, dtype=jnp.float32)[None]
        for height in range(depth_local - 1, -1, -1):
            cluster_count = leaf_count >> height + 1
            first_slot = leaf_count - (2 * leaf_count >> height + 1)
            lift_mats = lift_stack[first_slot : first_slot + cluster_count]
            reach = jnp.einsum("cra,crk->cak", lift_mats, reach, precision=HIGHEST)
            reach = reach.reshape(2 * cluster_count, RANK, RANK)
        reach_rows = jnp.einsum("rlp,lrk->lpk", basis_float, reach, precision=HIGHEST)
        left_vectors, left_points, left_edges = unpack(from_left)
        right_vectors, right_points, right_edges = unpack(from_right)
        vector_rims = jnp.concatenate(
            [left_vectors.astype(vectors.dtype), vectors, right_vectors.astype(vectors.dtype)], 0
        )
        point_rims = jnp.concatenate([left_points, points, right_points], 1)
        nearby = near_field(vector_rims, point_rims, near_index, 0, leaf_zero, leaf_count)
        fields = []
        for height in range(depth_local):
            cluster_count = leaf_count >> height
            first_slot = 2 * leaf_count - (2 * leaf_count >> height)
            extended = jnp.concatenate([left_edges[height], coefficients[height], right_edges[height]], 0)
            stacked = extended[partner_table(cluster_count) + 2].reshape(
                cluster_count, 3 * RANK, columns
            )
            mixers = as_float(coupling[0, first_slot : first_slot + cluster_count])
            fields.append(jnp.einsum("cra,cav->crv", mixers, stacked, precision=HIGHEST))
        return nearby, fields, reach_rows

    device_coupling = as_float(coupling[0, 2 * leaf_count - 2])
    device_coef = coefficients[depth_local][0]
    downward, (nearby, fields, reach_rows) = upper_tree(
        device_coef, device_coupling, upper_transfer, upper_coupling, ((from_left, from_right), as_float(transfer[0]), as_float(basis_leaves)), late
    )
    local_down = None
    for height in range(depth_local - 1, -1, -1):
        cluster_count = leaf_count >> height + 1
        first_slot = leaf_count - (2 * leaf_count >> height + 1)
        lift_mats = as_float(transfer[0, first_slot : first_slot + cluster_count])
        if local_down is None:
            local_down = fields[height]
        else:
            spread = jnp.einsum("cra,crv->cav", lift_mats, local_down, precision=HIGHEST)
            local_down = fields[height] + spread.reshape(2 * cluster_count, RANK, columns)
    basis_float = as_float(basis_leaves)
    far_field = (
        jnp.einsum("rlp,lrv->lpv", basis_float, local_down, precision=HIGHEST)
        + jnp.einsum("lpk,kv->lpv", reach_rows, downward, precision=HIGHEST)
    ).reshape(row_count, columns)
    return (nearby + NUGGET * vectors.astype(jnp.float32) + far_field).astype(jnp.bfloat16)


def solution(mesh):
    devices = mesh.devices.reshape(CUTS + (mesh.shape["vec"],))
    split_mesh = jax.sharding.Mesh(devices, SPACE + ("vec",))
    return jax.shard_map(
        local,
        mesh=split_mesh,
        in_specs=(
            P(SPACE, "vec"),
            P(None, SPACE),
            P(SPACE, None),
            P(None, SPACE),
            P(SPACE, None, None, None),
            P(SPACE, None, None, None),
            P(SPACE, None, None),
            P(SPACE, None, None),
        ),
        out_specs=P(SPACE, "vec"),
        check_vma=False,
    )
```

```python
import jax
import jax.numpy as jnp
import numpy as np
from jax import lax
from jax.sharding import PartitionSpec as P

LEAF = 64
RANK = 32


SCALE_A = 2.0 * 3.0**0.5
VARIANCE = 0.0625
NUGGET = 0.5
HIGHEST = lax.Precision.HIGHEST


def matern(own_points, other_points):
    difference = own_points[:, :, None, :, None] - other_points[:, :, :, None, :]
    distance = jnp.sqrt(jnp.sum(difference * difference, axis=0))
    return (VARIANCE * (1.0 + SCALE_A * distance) * jnp.exp(-SCALE_A * distance)).astype(
        jnp.bfloat16
    )


def near_field(source, extended_points, index_rows, first_leaf, leaf_zero, leaf_count):
    block_count = index_rows.shape[0]
    col_width = source.shape[1]
    group_size = block_count
    source_leaves = source.reshape(leaf_count + 2, LEAF, col_width)
    point_leaves = extended_points.reshape(3, leaf_count + 2, LEAF)
    present = (index_rows >= 0).astype(jnp.bfloat16)
    located = jnp.where(index_rows >= 0, index_rows - leaf_zero + 1, 0)

    def one_group(first_row):
        own_points = lax.dynamic_slice_in_dim(
            point_leaves, first_row + first_leaf + 1, group_size, 1
        )
        blocks = matern(own_points, point_leaves[:, located]) * present[:, :, None, None]
        return jnp.einsum(
            "gkij,gkjv->giv", blocks, source_leaves[located], preferred_element_type=jnp.float32
        )

    starts = jnp.arange(block_count // group_size, dtype=jnp.int32) * group_size
    return lax.map(one_group, starts).reshape(block_count * LEAF, col_width)


def partner_table(cluster_count):
    base = np.arange(cluster_count)
    odd_mask = base % 2 == 1
    return (
        np.stack(
            [np.where(odd_mask, -3, -2), np.where(odd_mask, -2, 2), np.where(odd_mask, 2, 3)], 1
        )
        + base[:, None]
    )


def as_float(matrix):
    return matrix.astype(jnp.float32)


def product(matrix, operand):
    return jnp.dot(matrix, operand, precision=HIGHEST)


SPACE = ("z", "y", "x")
PLANE = ("y", "x")
CUTS = (16, 4, 4)


def neighbours(padded, cluster):
    odd_mask = cluster % 2 == 1
    offsets = (
        jnp.where(odd_mask, -3, -2),
        jnp.where(odd_mask, -2, 2),
        jnp.where(odd_mask, 2, 3),
    )
    picked = [lax.dynamic_index_in_dim(padded, cluster + 3 + step, 0, False) for step in offsets]
    return jnp.concatenate(picked, 0)


def pick(stack, index):
    return lax.dynamic_index_in_dim(stack, index, 0, False)


def lift_up(lift_mats, coefs):
    children = coefs.reshape(lift_mats.shape[0], 2 * RANK, coefs.shape[-1])
    return jnp.einsum("cra,cav->crv", lift_mats, children, precision=HIGHEST)


def rims(own, left_tail, right_head):
    zeros = jnp.zeros((3 - left_tail.shape[0],) + own.shape[1:], own.dtype)
    return jnp.concatenate([zeros, left_tail, own, right_head, zeros], 0)


def spread_gather(block, axis):
    count = lax.axis_size(axis)
    copies = jnp.broadcast_to(block[None], (count,) + block.shape)
    return lax.all_to_all(copies, axis, 0, 0, tiled=True)


def doubling_gather(block, axis):
    count = lax.axis_size(axis)
    index = lax.axis_index(axis)
    gathered = block[None]
    step = count // 2
    while step >= 1:
        received = lax.ppermute(gathered, axis, [(i, i ^ step) for i in range(count)])
        upper = (index & step) != 0
        gathered = jnp.where(
            upper,
            jnp.concatenate([received, gathered], 0),
            jnp.concatenate([gathered, received], 0),
        )
        step //= 2
    bits = count.bit_length() - 1
    order = [int(format(i, f"0{bits}b")[::-1], 2) for i in range(count)]
    return jnp.take(gathered, np.array(order), axis=0)


def upper_tree(device_coef, device_coupling, upper_transfer, upper_coupling, held, late):
    planes = lax.axis_size("z")
    plane_bits = lax.axis_size(PLANE).bit_length() - 1
    plane = lax.axis_index("z")
    seat = lax.axis_index(PLANE)
    columns = device_coef.shape[1]
    rounded = lax.reduce_precision(device_coef, exponent_bits=8, mantissa_bits=7)
    high = rounded.astype(jnp.bfloat16)
    low = (device_coef - rounded).astype(jnp.bfloat16)
    plane_unit = jnp.concatenate([high, low, upper_transfer[0], upper_coupling[0]], 1)
    plane_sent = spread_gather(plane_unit, PLANE)
    plane_held = as_float(plane_sent[:, :, columns:])
    plane_lift = plane_held[:, :, columns : columns + 2 * RANK]
    plane_mix = plane_held[:, :, columns + 2 * RANK :]
    inner = [as_float(plane_sent[:, :, :columns]) + plane_held[:, :, :columns]]
    for height in range(1, plane_bits + 1):
        inner.append(lift_up(plane_lift[2 ** (height - 1) :: 2**height], inner[-1]))
    tails = jnp.concatenate([level[-3:] for level in inner[:plane_bits]], 0)
    heads = jnp.concatenate([level[:3] for level in inner[:plane_bits]], 0)
    from_left = lax.ppermute(tails, "z", [(i, i + 1) for i in range(planes - 1)])
    from_right = lax.ppermute(heads, "z", [(i + 1, i) for i in range(planes - 1)])
    outer_unit = jnp.concatenate([inner[plane_bits][0], plane_held[0, :, columns:]], 1)
    outer_unit, held, plane_lift, plane_mix = lax.optimization_barrier(
        (outer_unit.astype(jnp.bfloat16), held, plane_lift, plane_mix)
    )
    outer_held = as_float(spread_gather(outer_unit, "z"))
    late_result = late(held)
    summary = outer_held[:, :, :columns]
    outer_lift = outer_held[:, :, columns : columns + 2 * RANK]
    outer_mix = outer_held[:, :, columns + 2 * RANK :]
    outer = [summary]
    for height in range(1, (planes.bit_length() - 1) - 1):
        outer.append(lift_up(outer_lift[2 ** (height - 1) :: 2**height], outer[-1]))
    summit = plane_bits + len(outer) - 1
    fields = []
    lifts = []
    done = 0
    for height in range(plane_bits):
        width = min(3, inner[height].shape[0])
        extended = rims(
            inner[height], from_left[done : done + width], from_right[done : done + width]
        )
        done += width
        cluster = seat >> height
        if height == 0:
            mixer = device_coupling
        else:
            mixer = pick(plane_mix, cluster * 2**height + 2 ** (height - 1))
        fields.append(product(mixer, neighbours(extended, cluster)))
        parent = cluster >> 1
        lifts.append((cluster, pick(plane_lift, parent * 2 ** (height + 1) + 2**height)))
    for level, coefs in enumerate(outer):
        height = plane_bits + level
        cluster = plane >> level
        if level == 0:
            mixer = pick(plane_mix, 2 ** (height - 1))
        else:
            mixer = pick(outer_mix, cluster * 2**level + 2 ** (level - 1))
        padded = jnp.pad(coefs, ((3, 3), (0, 0), (0, 0)))
        fields.append(product(mixer, neighbours(padded, cluster)))
        if height < summit:
            parent = cluster >> 1
            lifts.append((cluster, pick(outer_lift, parent * 2 ** (level + 1) + 2**level)))
    prefix = None
    downward = fields[0]
    for height in range(1, summit + 1):
        cluster, lift = lifts[height - 1]
        half = jnp.where(cluster % 2 == 1, lift[:, RANK:], lift[:, :RANK]).T
        prefix = half if prefix is None else product(prefix, half)
        downward = downward + product(prefix, fields[height])
    return downward, late_result


def local(
    vectors, points, near_index, leaf_basis, transfer, coupling, upper_transfer, upper_coupling
):
    row_count, columns = vectors.shape
    leaf_count = row_count // LEAF
    depth_local = leaf_count.bit_length() - 1
    position = lax.axis_index(SPACE)
    leaf_zero = position * leaf_count
    basis_leaves = leaf_basis.reshape(RANK, leaf_count, LEAF)
    leaf_vectors = vectors.reshape(leaf_count, LEAF, columns)
    coefficients = [
        jnp.einsum("rlp,lpv->lrv", basis_leaves, leaf_vectors, preferred_element_type=jnp.float32)
    ]
    for height in range(1, depth_local + 1):
        cluster_count = leaf_count >> height
        first_slot = leaf_count - (2 * leaf_count >> height)
        lift_mats = as_float(transfer[0, first_slot : first_slot + cluster_count])
        children = coefficients[-1].reshape(cluster_count, 2 * RANK, columns)
        coefficients.append(jnp.einsum("cra,cav->crv", lift_mats, children, precision=HIGHEST))
    def rim(rows, clusters):
        edges = jnp.stack([coefficients[height][clusters] for height in range(depth_local)], 0)
        parts = [
            vectors[rows].astype(jnp.float32),
            points[:, rows],
            edges.astype(jnp.bfloat16).astype(jnp.float32),
        ]
        return jnp.concatenate([part.reshape(-1) for part in parts]), [p.shape for p in parts]

    head, shapes = rim(slice(0, LEAF), slice(0, 2))
    tail, _ = rim(slice(row_count - LEAF, row_count), slice(-2, None))
    count = lax.axis_size(SPACE)
    from_left = lax.ppermute(tail, SPACE, [(i, i + 1) for i in range(count - 1)])
    from_right = lax.ppermute(head, SPACE, [(i + 1, i) for i in range(count - 1)])

    def unpack(flat):
        pieces, done = [], 0
        for shape in shapes:
            size = int(np.prod(shape))
            pieces.append(flat[done : done + size].reshape(shape))
            done += size
        return pieces

    def late(held):
        (from_left, from_right), lift_stack, basis_float = held
        reach = jnp.eye(RANK, dtype=jnp.float32)[None]
        for height in range(depth_local - 1, -1, -1):
            cluster_count = leaf_count >> height + 1
            first_slot = leaf_count - (2 * leaf_count >> height + 1)
            lift_mats = lift_stack[first_slot : first_slot + cluster_count]
            reach = jnp.einsum("cra,crk->cak", lift_mats, reach, precision=HIGHEST)
            reach = reach.reshape(2 * cluster_count, RANK, RANK)
        reach_rows = jnp.einsum("rlp,lrk->lpk", basis_float, reach, precision=HIGHEST)
        left_edges = unpack(from_left)[2]
        right_edges = unpack(from_right)[2]
        fields = []
        for height in range(depth_local):
            cluster_count = leaf_count >> height
            first_slot = 2 * leaf_count - (2 * leaf_count >> height)
            extended = jnp.concatenate([left_edges[height], coefficients[height], right_edges[height]], 0)
            stacked = extended[partner_table(cluster_count) + 2].reshape(
                cluster_count, 3 * RANK, columns
            )
            mixers = as_float(coupling[0, first_slot : first_slot + cluster_count])
            fields.append(jnp.einsum("cra,cav->crv", mixers, stacked, precision=HIGHEST))
        return fields, reach_rows

    left_vectors, left_points, _ = unpack(from_left)
    right_vectors, right_points, _ = unpack(from_right)
    vector_rims = jnp.concatenate(
        [left_vectors.astype(vectors.dtype), vectors, right_vectors.astype(vectors.dtype)], 0
    )
    point_rims = jnp.concatenate([left_points, points, right_points], 1)
    nearby = near_field(vector_rims, point_rims, near_index, 0, leaf_zero, leaf_count)
    device_coupling = as_float(coupling[0, 2 * leaf_count - 2])
    device_coef = coefficients[depth_local][0]
    downward, (fields, reach_rows) = upper_tree(
        device_coef, device_coupling, upper_transfer, upper_coupling, ((from_left, from_right), as_float(transfer[0]), as_float(basis_leaves)), late
    )
    local_down = None
    for height in range(depth_local - 1, -1, -1):
        cluster_count = leaf_count >> height + 1
        first_slot = leaf_count - (2 * leaf_count >> height + 1)
        lift_mats = as_float(transfer[0, first_slot : first_slot + cluster_count])
        if local_down is None:
            local_down = fields[height]
        else:
            spread = jnp.einsum("cra,crv->cav", lift_mats, local_down, precision=HIGHEST)
            local_down = fields[height] + spread.reshape(2 * cluster_count, RANK, columns)
    basis_float = as_float(basis_leaves)
    far_field = (
        jnp.einsum("rlp,lrv->lpv", basis_float, local_down, precision=HIGHEST)
        + jnp.einsum("lpk,kv->lpv", reach_rows, downward, precision=HIGHEST)
    ).reshape(row_count, columns)
    return (nearby + NUGGET * vectors.astype(jnp.float32) + far_field).astype(jnp.bfloat16)


def solution(mesh):
    devices = mesh.devices.reshape(CUTS + (mesh.shape["vec"],))
    split_mesh = jax.sharding.Mesh(devices, SPACE + ("vec",))
    return jax.shard_map(
        local,
        mesh=split_mesh,
        in_specs=(
            P(SPACE, "vec"),
            P(None, SPACE),
            P(SPACE, None),
            P(None, SPACE),
            P(SPACE, None, None, None),
            P(SPACE, None, None, None),
            P(SPACE, None, None),
            P(SPACE, None, None),
        ),
        out_specs=P(SPACE, "vec"),
        check_vma=False,
    )
```

```python
import jax
import jax.numpy as jnp
import numpy as np
from jax import lax
from jax.sharding import PartitionSpec as P

LEAF = 64
RANK = 32


SCALE_A = 2.0 * 3.0**0.5
VARIANCE = 0.0625
NUGGET = 0.5
HIGHEST = lax.Precision.HIGHEST


def matern(own_points, other_points):
    difference = own_points[:, :, None, :, None] - other_points[:, :, :, None, :]
    distance = jnp.sqrt(jnp.sum(difference * difference, axis=0))
    return (VARIANCE * (1.0 + SCALE_A * distance) * jnp.exp(-SCALE_A * distance)).astype(
        jnp.bfloat16
    )


def near_field(source, extended_points, index_rows, first_leaf, leaf_zero, leaf_count):
    block_count = index_rows.shape[0]
    col_width = source.shape[1]
    group_size = block_count
    source_leaves = source.reshape(leaf_count + 2, LEAF, col_width)
    point_leaves = extended_points.reshape(3, leaf_count + 2, LEAF)
    present = (index_rows >= 0).astype(jnp.bfloat16)
    located = jnp.where(index_rows >= 0, index_rows - leaf_zero + 1, 0)

    def one_group(first_row):
        own_points = lax.dynamic_slice_in_dim(
            point_leaves, first_row + first_leaf + 1, group_size, 1
        )
        blocks = matern(own_points, point_leaves[:, located]) * present[:, :, None, None]
        return jnp.einsum(
            "gkij,gkjv->giv", blocks, source_leaves[located], preferred_element_type=jnp.float32
        )

    starts = jnp.arange(block_count // group_size, dtype=jnp.int32) * group_size
    return lax.map(one_group, starts).reshape(block_count * LEAF, col_width)


def partner_table(cluster_count):
    base = np.arange(cluster_count)
    odd_mask = base % 2 == 1
    return (
        np.stack(
            [np.where(odd_mask, -3, -2), np.where(odd_mask, -2, 2), np.where(odd_mask, 2, 3)], 1
        )
        + base[:, None]
    )


def as_float(matrix):
    return matrix.astype(jnp.float32)


def product(matrix, operand):
    return jnp.dot(matrix, operand, precision=HIGHEST)


SPACE = ("z", "y", "x")
PLANE = ("y", "x")
CUTS = (16, 4, 4)


def neighbours(padded, cluster):
    odd_mask = cluster % 2 == 1
    offsets = (
        jnp.where(odd_mask, -3, -2),
        jnp.where(odd_mask, -2, 2),
        jnp.where(odd_mask, 2, 3),
    )
    picked = [lax.dynamic_index_in_dim(padded, cluster + 3 + step, 0, False) for step in offsets]
    return jnp.concatenate(picked, 0)


def pick(stack, index):
    return lax.dynamic_index_in_dim(stack, index, 0, False)


def lift_up(lift_mats, coefs):
    children = coefs.reshape(lift_mats.shape[0], 2 * RANK, coefs.shape[-1])
    return jnp.einsum("cra,cav->crv", lift_mats, children, precision=HIGHEST)


def rims(own, left_tail, right_head):
    zeros = jnp.zeros((3 - left_tail.shape[0],) + own.shape[1:], own.dtype)
    return jnp.concatenate([zeros, left_tail, own, right_head, zeros], 0)


def spread_gather(block, axis):
    count = lax.axis_size(axis)
    copies = jnp.broadcast_to(block[None], (count,) + block.shape)
    return lax.all_to_all(copies, axis, 0, 0, tiled=True)


def doubling_gather(block, axis):
    count = lax.axis_size(axis)
    index = lax.axis_index(axis)
    gathered = block[None]
    step = count // 2
    while step >= 1:
        received = lax.ppermute(gathered, axis, [(i, i ^ step) for i in range(count)])
        upper = (index & step) != 0
        gathered = jnp.where(
            upper,
            jnp.concatenate([received, gathered], 0),
            jnp.concatenate([gathered, received], 0),
        )
        step //= 2
    bits = count.bit_length() - 1
    order = [int(format(i, f"0{bits}b")[::-1], 2) for i in range(count)]
    return jnp.take(gathered, np.array(order), axis=0)


def upper_tree(device_coef, device_coupling, upper_transfer, upper_coupling, held, late):
    planes = lax.axis_size("z")
    plane_bits = lax.axis_size(PLANE).bit_length() - 1
    plane = lax.axis_index("z")
    seat = lax.axis_index(PLANE)
    columns = device_coef.shape[1]
    rounded = lax.reduce_precision(device_coef, exponent_bits=8, mantissa_bits=7)
    high = rounded.astype(jnp.bfloat16)
    low = (device_coef - rounded).astype(jnp.bfloat16)
    plane_unit = jnp.concatenate([high, low, upper_transfer[0], upper_coupling[0]], 1)
    plane_sent = spread_gather(plane_unit, PLANE)
    plane_held = as_float(plane_sent[:, :, columns:])
    plane_lift = plane_held[:, :, columns : columns + 2 * RANK]
    plane_mix = plane_held[:, :, columns + 2 * RANK :]
    inner = [as_float(plane_sent[:, :, :columns]) + plane_held[:, :, :columns]]
    for height in range(1, plane_bits + 1):
        inner.append(lift_up(plane_lift[2 ** (height - 1) :: 2**height], inner[-1]))
    tails = jnp.concatenate([level[-3:] for level in inner[:plane_bits]], 0)
    heads = jnp.concatenate([level[:3] for level in inner[:plane_bits]], 0)
    from_left = lax.ppermute(tails, "z", [(i, i + 1) for i in range(planes - 1)])
    from_right = lax.ppermute(heads, "z", [(i + 1, i) for i in range(planes - 1)])
    outer_unit = jnp.concatenate([inner[plane_bits][0], plane_held[0, :, columns:]], 1)
    outer_unit, held, plane_lift, plane_mix = lax.optimization_barrier(
        (outer_unit.astype(jnp.bfloat16), held, plane_lift, plane_mix)
    )
    outer_held = as_float(spread_gather(outer_unit, "z"))
    late_result = late(held)
    summary = outer_held[:, :, :columns]
    outer_lift = outer_held[:, :, columns : columns + 2 * RANK]
    outer_mix = outer_held[:, :, columns + 2 * RANK :]
    outer = [summary]
    for height in range(1, (planes.bit_length() - 1) - 1):
        outer.append(lift_up(outer_lift[2 ** (height - 1) :: 2**height], outer[-1]))
    summit = plane_bits + len(outer) - 1
    fields = []
    lifts = []
    done = 0
    for height in range(plane_bits):
        width = min(3, inner[height].shape[0])
        extended = rims(
            inner[height], from_left[done : done + width], from_right[done : done + width]
        )
        done += width
        cluster = seat >> height
        if height == 0:
            mixer = device_coupling
        else:
            mixer = pick(plane_mix, cluster * 2**height + 2 ** (height - 1))
        fields.append(product(mixer, neighbours(extended, cluster)))
        parent = cluster >> 1
        lifts.append((cluster, pick(plane_lift, parent * 2 ** (height + 1) + 2**height)))
    for level, coefs in enumerate(outer):
        height = plane_bits + level
        cluster = plane >> level
        if level == 0:
            mixer = pick(plane_mix, 2 ** (height - 1))
        else:
            mixer = pick(outer_mix, cluster * 2**level + 2 ** (level - 1))
        padded = jnp.pad(coefs, ((3, 3), (0, 0), (0, 0)))
        fields.append(product(mixer, neighbours(padded, cluster)))
        if height < summit:
            parent = cluster >> 1
            lifts.append((cluster, pick(outer_lift, parent * 2 ** (level + 1) + 2**level)))
    prefix = None
    downward = fields[0]
    for height in range(1, summit + 1):
        cluster, lift = lifts[height - 1]
        half = jnp.where(cluster % 2 == 1, lift[:, RANK:], lift[:, :RANK]).T
        prefix = half if prefix is None else product(prefix, half)
        downward = downward + product(prefix, fields[height])
    return downward, late_result


def local(
    vectors, points, near_index, leaf_basis, transfer, coupling, upper_transfer, upper_coupling
):
    row_count, columns = vectors.shape
    leaf_count = row_count // LEAF
    depth_local = leaf_count.bit_length() - 1
    position = lax.axis_index(SPACE)
    leaf_zero = position * leaf_count
    basis_leaves = leaf_basis.reshape(RANK, leaf_count, LEAF)
    leaf_vectors = vectors.reshape(leaf_count, LEAF, columns)
    coefficients = [
        jnp.einsum("rlp,lpv->lrv", basis_leaves, leaf_vectors, preferred_element_type=jnp.float32)
    ]
    for height in range(1, depth_local + 1):
        cluster_count = leaf_count >> height
        first_slot = leaf_count - (2 * leaf_count >> height)
        lift_mats = as_float(transfer[0, first_slot : first_slot + cluster_count])
        children = coefficients[-1].reshape(cluster_count, 2 * RANK, columns)
        coefficients.append(jnp.einsum("cra,cav->crv", lift_mats, children, precision=HIGHEST))
    def rim(rows, clusters):
        edges = jnp.stack([coefficients[height][clusters] for height in range(depth_local)], 0)
        parts = [
            vectors[rows].astype(jnp.float32),
            points[:, rows],
            edges.astype(jnp.bfloat16).astype(jnp.float32),
        ]
        return jnp.concatenate([part.reshape(-1) for part in parts]), [p.shape for p in parts]

    head, shapes = rim(slice(0, LEAF), slice(0, 2))
    tail, _ = rim(slice(row_count - LEAF, row_count), slice(-2, None))
    count = lax.axis_size(SPACE)
    from_left = lax.ppermute(tail, SPACE, [(i, i + 1) for i in range(count - 1)])
    from_right = lax.ppermute(head, SPACE, [(i + 1, i) for i in range(count - 1)])

    def unpack(flat):
        pieces, done = [], 0
        for shape in shapes:
            size = int(np.prod(shape))
            pieces.append(flat[done : done + size].reshape(shape))
            done += size
        return pieces

    def early(held):
        (from_left, from_right), lift_stack, basis_float = held
        reach = jnp.eye(RANK, dtype=jnp.float32)[None]
        for height in range(depth_local - 1, -1, -1):
            cluster_count = leaf_count >> height + 1
            first_slot = leaf_count - (2 * leaf_count >> height + 1)
            lift_mats = lift_stack[first_slot : first_slot + cluster_count]
            reach = jnp.einsum("cra,crk->cak", lift_mats, reach, precision=HIGHEST)
            reach = reach.reshape(2 * cluster_count, RANK, RANK)
        reach_rows = jnp.einsum("rlp,lrk->lpk", basis_float, reach, precision=HIGHEST)
        left_edges = unpack(from_left)[2]
        right_edges = unpack(from_right)[2]
        fields = []
        for height in range(depth_local):
            cluster_count = leaf_count >> height
            first_slot = 2 * leaf_count - (2 * leaf_count >> height)
            extended = jnp.concatenate([left_edges[height], coefficients[height], right_edges[height]], 0)
            stacked = extended[partner_table(cluster_count) + 2].reshape(
                cluster_count, 3 * RANK, columns
            )
            mixers = as_float(coupling[0, first_slot : first_slot + cluster_count])
            fields.append(jnp.einsum("cra,cav->crv", mixers, stacked, precision=HIGHEST))
        return fields, reach_rows

    left_vectors, left_points, _ = unpack(from_left)
    right_vectors, right_points, _ = unpack(from_right)
    vector_rims = jnp.concatenate(
        [left_vectors.astype(vectors.dtype), vectors, right_vectors.astype(vectors.dtype)], 0
    )
    point_rims = jnp.concatenate([left_points, points, right_points], 1)
    nearby = near_field(vector_rims, point_rims, near_index, 0, leaf_zero, leaf_count)
    device_coupling = as_float(coupling[0, 2 * leaf_count - 2])
    device_coef = coefficients[depth_local][0]
    fields, reach_rows = early(
        ((from_left, from_right), as_float(transfer[0]), as_float(basis_leaves))
    )
    downward, _ = upper_tree(
        device_coef, device_coupling, upper_transfer, upper_coupling, (), lambda held: None
    )


    local_down = None
    for height in range(depth_local - 1, -1, -1):
        cluster_count = leaf_count >> height + 1
        first_slot = leaf_count - (2 * leaf_count >> height + 1)
        lift_mats = as_float(transfer[0, first_slot : first_slot + cluster_count])
        if local_down is None:
            local_down = fields[height]
        else:
            spread = jnp.einsum("cra,crv->cav", lift_mats, local_down, precision=HIGHEST)
            local_down = fields[height] + spread.reshape(2 * cluster_count, RANK, columns)
    basis_float = as_float(basis_leaves)
    far_field = (
        jnp.einsum("rlp,lrv->lpv", basis_float, local_down, precision=HIGHEST)
        + jnp.einsum("lpk,kv->lpv", reach_rows, downward, precision=HIGHEST)
    ).reshape(row_count, columns)
    return (nearby + NUGGET * vectors.astype(jnp.float32) + far_field).astype(jnp.bfloat16)


def solution(mesh):
    devices = mesh.devices.reshape(CUTS + (mesh.shape["vec"],))
    split_mesh = jax.sharding.Mesh(devices, SPACE + ("vec",))
    return jax.shard_map(
        local,
        mesh=split_mesh,
        in_specs=(
            P(SPACE, "vec"),
            P(None, SPACE),
            P(SPACE, None),
            P(None, SPACE),
            P(SPACE, None, None, None),
            P(SPACE, None, None, None),
            P(SPACE, None, None),
            P(SPACE, None, None),
        ),
        out_specs=P(SPACE, "vec"),
        check_vma=False,
    )
```

```python
import jax
import jax.numpy as jnp
import numpy as np
from jax import lax
from jax.sharding import PartitionSpec as P

LEAF = 64
RANK = 32


SCALE_A = 2.0 * 3.0**0.5
VARIANCE = 0.0625
NUGGET = 0.5
HIGHEST = lax.Precision.HIGHEST


def matern(own_points, other_points):
    difference = own_points[:, :, None, :, None] - other_points[:, :, :, None, :]
    distance = jnp.sqrt(jnp.sum(difference * difference, axis=0))
    return (VARIANCE * (1.0 + SCALE_A * distance) * jnp.exp(-SCALE_A * distance)).astype(
        jnp.bfloat16
    )


def near_field(source, extended_points, index_rows, first_leaf, leaf_zero, leaf_count):
    block_count = index_rows.shape[0]
    col_width = source.shape[1]
    group_size = block_count
    source_leaves = source.reshape(leaf_count + 2, LEAF, col_width)
    point_leaves = extended_points.reshape(3, leaf_count + 2, LEAF)
    present = (index_rows >= 0).astype(jnp.bfloat16)
    located = jnp.where(index_rows >= 0, index_rows - leaf_zero + 1, 0)

    def one_group(first_row):
        own_points = lax.dynamic_slice_in_dim(
            point_leaves, first_row + first_leaf + 1, group_size, 1
        )
        blocks = matern(own_points, point_leaves[:, located]) * present[:, :, None, None]
        return jnp.einsum(
            "gkij,gkjv->giv", blocks, source_leaves[located], preferred_element_type=jnp.float32
        )

    starts = jnp.arange(block_count // group_size, dtype=jnp.int32) * group_size
    return lax.map(one_group, starts).reshape(block_count * LEAF, col_width)


def partner_table(cluster_count):
    base = np.arange(cluster_count)
    odd_mask = base % 2 == 1
    return (
        np.stack(
            [np.where(odd_mask, -3, -2), np.where(odd_mask, -2, 2), np.where(odd_mask, 2, 3)], 1
        )
        + base[:, None]
    )


def as_float(matrix):
    return matrix.astype(jnp.float32)


def product(matrix, operand):
    return jnp.dot(matrix, operand, precision=HIGHEST)


SPACE = ("z", "y", "x")
PLANE = ("y", "x")
CUTS = (16, 4, 4)


def neighbours(padded, cluster):
    odd_mask = cluster % 2 == 1
    offsets = (
        jnp.where(odd_mask, -3, -2),
        jnp.where(odd_mask, -2, 2),
        jnp.where(odd_mask, 2, 3),
    )
    picked = [lax.dynamic_index_in_dim(padded, cluster + 3 + step, 0, False) for step in offsets]
    return jnp.concatenate(picked, 0)


def pick(stack, index):
    return lax.dynamic_index_in_dim(stack, index, 0, False)


def lift_up(lift_mats, coefs):
    children = coefs.reshape(lift_mats.shape[0], 2 * RANK, coefs.shape[-1])
    return jnp.einsum("cra,cav->crv", lift_mats, children, precision=HIGHEST)


def rims(own, left_tail, right_head):
    zeros = jnp.zeros((3 - left_tail.shape[0],) + own.shape[1:], own.dtype)
    return jnp.concatenate([zeros, left_tail, own, right_head, zeros], 0)


def spread_gather(block, axis):
    count = lax.axis_size(axis)
    copies = jnp.broadcast_to(block[None], (count,) + block.shape)
    return lax.all_to_all(copies, axis, 0, 0, tiled=True)


def doubling_gather(block, axis):
    count = lax.axis_size(axis)
    index = lax.axis_index(axis)
    gathered = block[None]
    step = count // 2
    while step >= 1:
        received = lax.ppermute(gathered, axis, [(i, i ^ step) for i in range(count)])
        upper = (index & step) != 0
        gathered = jnp.where(
            upper,
            jnp.concatenate([received, gathered], 0),
            jnp.concatenate([gathered, received], 0),
        )
        step //= 2
    bits = count.bit_length() - 1
    order = [int(format(i, f"0{bits}b")[::-1], 2) for i in range(count)]
    return jnp.take(gathered, np.array(order), axis=0)


def upper_tree(device_coef, device_coupling, upper_transfer, upper_coupling, held, late):
    planes = lax.axis_size("z")
    plane_bits = lax.axis_size(PLANE).bit_length() - 1
    plane = lax.axis_index("z")
    seat = lax.axis_index(PLANE)
    columns = device_coef.shape[1]
    rounded = lax.reduce_precision(device_coef, exponent_bits=8, mantissa_bits=7)
    high = rounded.astype(jnp.bfloat16)
    low = (device_coef - rounded).astype(jnp.bfloat16)
    plane_unit = jnp.concatenate([high, low, upper_transfer[0], upper_coupling[0]], 1)
    plane_sent = spread_gather(plane_unit, PLANE)
    plane_held = as_float(plane_sent[:, :, columns:])
    plane_lift = plane_held[:, :, columns : columns + 2 * RANK]
    plane_mix = plane_held[:, :, columns + 2 * RANK :]
    inner = [as_float(plane_sent[:, :, :columns]) + plane_held[:, :, :columns]]
    for height in range(1, plane_bits + 1):
        inner.append(lift_up(plane_lift[2 ** (height - 1) :: 2**height], inner[-1]))
    tails = jnp.concatenate([level[-3:] for level in inner[:plane_bits]], 0)
    heads = jnp.concatenate([level[:3] for level in inner[:plane_bits]], 0)
    from_left = as_float(
        lax.ppermute(tails.astype(jnp.bfloat16), "z", [(i, i + 1) for i in range(planes - 1)])
    )
    from_right = as_float(
        lax.ppermute(heads.astype(jnp.bfloat16), "z", [(i + 1, i) for i in range(planes - 1)])
    )
    outer_unit = jnp.concatenate([inner[plane_bits][0], plane_held[0, :, columns:]], 1)
    outer_unit, held, plane_lift, plane_mix = lax.optimization_barrier(
        (outer_unit.astype(jnp.bfloat16), held, plane_lift, plane_mix)
    )
    outer_held = as_float(spread_gather(outer_unit, "z"))
    late_result = late(held)
    summary = outer_held[:, :, :columns]
    outer_lift = outer_held[:, :, columns : columns + 2 * RANK]
    outer_mix = outer_held[:, :, columns + 2 * RANK :]
    outer = [summary]
    for height in range(1, (planes.bit_length() - 1) - 1):
        outer.append(lift_up(outer_lift[2 ** (height - 1) :: 2**height], outer[-1]))
    summit = plane_bits + len(outer) - 1
    fields = []
    lifts = []
    done = 0
    for height in range(plane_bits):
        width = min(3, inner[height].shape[0])
        extended = rims(
            inner[height], from_left[done : done + width], from_right[done : done + width]
        )
        done += width
        cluster = seat >> height
        if height == 0:
            mixer = device_coupling
        else:
            mixer = pick(plane_mix, cluster * 2**height + 2 ** (height - 1))
        fields.append(product(mixer, neighbours(extended, cluster)))
        parent = cluster >> 1
        lifts.append((cluster, pick(plane_lift, parent * 2 ** (height + 1) + 2**height)))
    for level, coefs in enumerate(outer):
        height = plane_bits + level
        cluster = plane >> level
        if level == 0:
            mixer = pick(plane_mix, 2 ** (height - 1))
        else:
            mixer = pick(outer_mix, cluster * 2**level + 2 ** (level - 1))
        padded = jnp.pad(coefs, ((3, 3), (0, 0), (0, 0)))
        fields.append(product(mixer, neighbours(padded, cluster)))
        if height < summit:
            parent = cluster >> 1
            lifts.append((cluster, pick(outer_lift, parent * 2 ** (level + 1) + 2**level)))
    prefix = None
    downward = fields[0]
    for height in range(1, summit + 1):
        cluster, lift = lifts[height - 1]
        half = jnp.where(cluster % 2 == 1, lift[:, RANK:], lift[:, :RANK]).T
        prefix = half if prefix is None else product(prefix, half)
        downward = downward + product(prefix, fields[height])
    return downward, late_result


def local(
    vectors, points, near_index, leaf_basis, transfer, coupling, upper_transfer, upper_coupling
):
    row_count, columns = vectors.shape
    leaf_count = row_count // LEAF
    depth_local = leaf_count.bit_length() - 1
    position = lax.axis_index(SPACE)
    leaf_zero = position * leaf_count
    basis_leaves = leaf_basis.reshape(RANK, leaf_count, LEAF)
    leaf_vectors = vectors.reshape(leaf_count, LEAF, columns)
    coefficients = [
        jnp.einsum("rlp,lpv->lrv", basis_leaves, leaf_vectors, preferred_element_type=jnp.float32)
    ]
    for height in range(1, depth_local + 1):
        cluster_count = leaf_count >> height
        first_slot = leaf_count - (2 * leaf_count >> height)
        lift_mats = as_float(transfer[0, first_slot : first_slot + cluster_count])
        children = coefficients[-1].reshape(cluster_count, 2 * RANK, columns)
        coefficients.append(jnp.einsum("cra,cav->crv", lift_mats, children, precision=HIGHEST))
    def rim(rows, clusters):
        edges = jnp.stack([coefficients[height][clusters] for height in range(depth_local)], 0)
        parts = [
            vectors[rows].astype(jnp.float32),
            points[:, rows],
            edges.astype(jnp.bfloat16).astype(jnp.float32),
        ]
        return jnp.concatenate([part.reshape(-1) for part in parts]), [p.shape for p in parts]

    head, shapes = rim(slice(0, LEAF), slice(0, 2))
    tail, _ = rim(slice(row_count - LEAF, row_count), slice(-2, None))
    count = lax.axis_size(SPACE)
    from_left = lax.ppermute(tail, SPACE, [(i, i + 1) for i in range(count - 1)])
    from_right = lax.ppermute(head, SPACE, [(i + 1, i) for i in range(count - 1)])

    def unpack(flat):
        pieces, done = [], 0
        for shape in shapes:
            size = int(np.prod(shape))
            pieces.append(flat[done : done + size].reshape(shape))
            done += size
        return pieces

    def late(held):
        (from_left, from_right), lift_stack, basis_float = held
        lift_stack = as_float(lift_stack)
        basis_float = as_float(basis_float)
        reach = jnp.eye(RANK, dtype=jnp.float32)[None]
        for height in range(depth_local - 1, -1, -1):
            cluster_count = leaf_count >> height + 1
            first_slot = leaf_count - (2 * leaf_count >> height + 1)
            lift_mats = lift_stack[first_slot : first_slot + cluster_count]
            reach = jnp.einsum("cra,crk->cak", lift_mats, reach, precision=HIGHEST)
            reach = reach.reshape(2 * cluster_count, RANK, RANK)
        reach_rows = jnp.einsum("rlp,lrk->lpk", basis_float, reach, precision=HIGHEST)
        left_edges = unpack(from_left)[2]
        right_edges = unpack(from_right)[2]
        fields = []
        for height in range(depth_local):
            cluster_count = leaf_count >> height
            first_slot = 2 * leaf_count - (2 * leaf_count >> height)
            extended = jnp.concatenate([left_edges[height], coefficients[height], right_edges[height]], 0)
            stacked = extended[partner_table(cluster_count) + 2].reshape(
                cluster_count, 3 * RANK, columns
            )
            mixers = as_float(coupling[0, first_slot : first_slot + cluster_count])
            fields.append(jnp.einsum("cra,cav->crv", mixers, stacked, precision=HIGHEST))
        return fields, reach_rows

    left_vectors, left_points, _ = unpack(from_left)
    right_vectors, right_points, _ = unpack(from_right)
    vector_rims = jnp.concatenate(
        [left_vectors.astype(vectors.dtype), vectors, right_vectors.astype(vectors.dtype)], 0
    )
    point_rims = jnp.concatenate([left_points, points, right_points], 1)
    nearby = near_field(vector_rims, point_rims, near_index, 0, leaf_zero, leaf_count)
    device_coupling = as_float(coupling[0, 2 * leaf_count - 2])
    device_coef = coefficients[depth_local][0]
    downward, (fields, reach_rows) = upper_tree(
        device_coef, device_coupling, upper_transfer, upper_coupling, ((from_left, from_right), transfer[0], basis_leaves), late
    )
    local_down = None
    for height in range(depth_local - 1, -1, -1):
        cluster_count = leaf_count >> height + 1
        first_slot = leaf_count - (2 * leaf_count >> height + 1)
        lift_mats = as_float(transfer[0, first_slot : first_slot + cluster_count])
        if local_down is None:
            local_down = fields[height]
        else:
            spread = jnp.einsum("cra,crv->cav", lift_mats, local_down, precision=HIGHEST)
            local_down = fields[height] + spread.reshape(2 * cluster_count, RANK, columns)
    basis_float = as_float(basis_leaves)
    far_field = (
        jnp.einsum("rlp,lrv->lpv", basis_float, local_down, precision=HIGHEST)
        + jnp.einsum("lpk,kv->lpv", reach_rows, downward, precision=HIGHEST)
    ).reshape(row_count, columns)
    return (nearby + NUGGET * vectors.astype(jnp.float32) + far_field).astype(jnp.bfloat16)


def solution(mesh):
    devices = mesh.devices.reshape(CUTS + (mesh.shape["vec"],))
    split_mesh = jax.sharding.Mesh(devices, SPACE + ("vec",))
    return jax.shard_map(
        local,
        mesh=split_mesh,
        in_specs=(
            P(SPACE, "vec"),
            P(None, SPACE),
            P(SPACE, None),
            P(None, SPACE),
            P(SPACE, None, None, None),
            P(SPACE, None, None, None),
            P(SPACE, None, None),
            P(SPACE, None, None),
        ),
        out_specs=P(SPACE, "vec"),
        check_vma=False,
    )
```

```python
import jax
import jax.numpy as jnp
import numpy as np
from jax import lax
from jax.sharding import PartitionSpec as P

LEAF = 64
RANK = 32


SCALE_A = 2.0 * 3.0**0.5
VARIANCE = 0.0625
NUGGET = 0.5
HIGHEST = lax.Precision.HIGHEST


def matern(own_points, other_points):
    difference = own_points[:, :, None, :, None] - other_points[:, :, :, None, :]
    distance = jnp.sqrt(jnp.sum(difference * difference, axis=0))
    return (VARIANCE * (1.0 + SCALE_A * distance) * jnp.exp(-SCALE_A * distance)).astype(
        jnp.bfloat16
    )


def near_field(source, extended_points, index_rows, first_leaf, leaf_zero, leaf_count):
    block_count = index_rows.shape[0]
    col_width = source.shape[1]
    group_size = block_count
    source_leaves = source.reshape(leaf_count + 2, LEAF, col_width)
    point_leaves = extended_points.reshape(3, leaf_count + 2, LEAF)
    present = (index_rows >= 0).astype(jnp.bfloat16)
    located = jnp.where(index_rows >= 0, index_rows - leaf_zero + 1, 0)

    def one_group(first_row):
        own_points = lax.dynamic_slice_in_dim(
            point_leaves, first_row + first_leaf + 1, group_size, 1
        )
        blocks = matern(own_points, point_leaves[:, located]) * present[:, :, None, None]
        return jnp.einsum(
            "gkij,gkjv->giv", blocks, source_leaves[located], preferred_element_type=jnp.float32
        )

    starts = jnp.arange(block_count // group_size, dtype=jnp.int32) * group_size
    return lax.map(one_group, starts).reshape(block_count * LEAF, col_width)


def partner_table(cluster_count):
    base = np.arange(cluster_count)
    odd_mask = base % 2 == 1
    return (
        np.stack(
            [np.where(odd_mask, -3, -2), np.where(odd_mask, -2, 2), np.where(odd_mask, 2, 3)], 1
        )
        + base[:, None]
    )


def as_float(matrix):
    return matrix.astype(jnp.float32)


def product(matrix, operand):
    return jnp.dot(matrix, operand, precision=HIGHEST)


SPACE = ("z", "y", "x")
PLANE = ("y", "x")
CUTS = (16, 4, 4)


def neighbours(padded, cluster):
    odd_mask = cluster % 2 == 1
    offsets = (
        jnp.where(odd_mask, -3, -2),
        jnp.where(odd_mask, -2, 2),
        jnp.where(odd_mask, 2, 3),
    )
    picked = [lax.dynamic_index_in_dim(padded, cluster + 3 + step, 0, False) for step in offsets]
    return jnp.concatenate(picked, 0)


def pick(stack, index):
    return lax.dynamic_index_in_dim(stack, index, 0, False)


def lift_up(lift_mats, coefs):
    children = coefs.reshape(lift_mats.shape[0], 2 * RANK, coefs.shape[-1])
    return jnp.einsum("cra,cav->crv", lift_mats, children, precision=HIGHEST)


def rims(own, left_tail, right_head):
    zeros = jnp.zeros((3 - left_tail.shape[0],) + own.shape[1:], own.dtype)
    return jnp.concatenate([zeros, left_tail, own, right_head, zeros], 0)


def spread_gather(block, axis):
    count = lax.axis_size(axis)
    copies = jnp.broadcast_to(block[None], (count,) + block.shape)
    return lax.all_to_all(copies, axis, 0, 0, tiled=True)


def doubling_gather(block, axis):
    count = lax.axis_size(axis)
    index = lax.axis_index(axis)
    gathered = block[None]
    step = count // 2
    while step >= 1:
        received = lax.ppermute(gathered, axis, [(i, i ^ step) for i in range(count)])
        upper = (index & step) != 0
        gathered = jnp.where(
            upper,
            jnp.concatenate([received, gathered], 0),
            jnp.concatenate([gathered, received], 0),
        )
        step //= 2
    bits = count.bit_length() - 1
    order = [int(format(i, f"0{bits}b")[::-1], 2) for i in range(count)]
    return jnp.take(gathered, np.array(order), axis=0)


def upper_tree(device_coef, device_coupling, upper_transfer, upper_coupling, held, late):
    planes = lax.axis_size("z")
    plane_bits = lax.axis_size(PLANE).bit_length() - 1
    plane = lax.axis_index("z")
    seat = lax.axis_index(PLANE)
    columns = device_coef.shape[1]
    rounded = lax.reduce_precision(device_coef, exponent_bits=8, mantissa_bits=7)
    high = rounded.astype(jnp.bfloat16)
    low = (device_coef - rounded).astype(jnp.bfloat16)
    plane_unit = jnp.concatenate([high, low, upper_transfer[0], upper_coupling[0]], 1)
    plane_sent = spread_gather(plane_unit, PLANE)
    plane_held = as_float(plane_sent[:, :, columns:])
    plane_lift = plane_held[:, :, columns : columns + 2 * RANK]
    plane_mix = plane_held[:, :, columns + 2 * RANK :]
    inner = [as_float(plane_sent[:, :, :columns]) + plane_held[:, :, :columns]]
    for height in range(1, plane_bits + 1):
        inner.append(lift_up(plane_lift[2 ** (height - 1) :: 2**height], inner[-1]))
    tails = jnp.concatenate([level[-3:] for level in inner[:plane_bits]], 0)
    heads = jnp.concatenate([level[:3] for level in inner[:plane_bits]], 0)
    from_left = as_float(
        lax.ppermute(tails.astype(jnp.bfloat16), "z", [(i, i + 1) for i in range(planes - 1)])
    )
    from_right = as_float(
        lax.ppermute(heads.astype(jnp.bfloat16), "z", [(i + 1, i) for i in range(planes - 1)])
    )
    outer_unit = jnp.concatenate([inner[plane_bits][0], plane_held[0, :, columns:]], 1)
    outer_unit, held, plane_lift, plane_mix = lax.optimization_barrier(
        (outer_unit.astype(jnp.bfloat16), held, plane_lift, plane_mix)
    )
    outer_held = as_float(spread_gather(outer_unit, "z"))
    late_result = late(held)
    summary = outer_held[:, :, :columns]
    outer_lift = outer_held[:, :, columns : columns + 2 * RANK]
    outer_mix = outer_held[:, :, columns + 2 * RANK :]
    outer = [summary]
    for height in range(1, (planes.bit_length() - 1) - 1):
        outer.append(lift_up(outer_lift[2 ** (height - 1) :: 2**height], outer[-1]))
    summit = plane_bits + len(outer) - 1
    fields = []
    lifts = []
    done = 0
    for height in range(plane_bits):
        width = min(3, inner[height].shape[0])
        extended = rims(
            inner[height], from_left[done : done + width], from_right[done : done + width]
        )
        done += width
        cluster = seat >> height
        if height == 0:
            mixer = device_coupling
        else:
            mixer = pick(plane_mix, cluster * 2**height + 2 ** (height - 1))
        fields.append(product(mixer, neighbours(extended, cluster)))
        parent = cluster >> 1
        lifts.append((cluster, pick(plane_lift, parent * 2 ** (height + 1) + 2**height)))
    for level, coefs in enumerate(outer):
        height = plane_bits + level
        cluster = plane >> level
        if level == 0:
            mixer = pick(plane_mix, 2 ** (height - 1))
        else:
            mixer = pick(outer_mix, cluster * 2**level + 2 ** (level - 1))
        padded = jnp.pad(coefs, ((3, 3), (0, 0), (0, 0)))
        fields.append(product(mixer, neighbours(padded, cluster)))
        if height < summit:
            parent = cluster >> 1
            lifts.append((cluster, pick(outer_lift, parent * 2 ** (level + 1) + 2**level)))
    prefix = None
    downward = fields[0]
    for height in range(1, summit + 1):
        cluster, lift = lifts[height - 1]
        half = jnp.where(cluster % 2 == 1, lift[:, RANK:], lift[:, :RANK]).T
        prefix = half if prefix is None else product(prefix, half)
        downward = downward + product(prefix, fields[height])
    return downward, late_result


def local(
    vectors, points, near_index, leaf_basis, transfer, coupling, upper_transfer, upper_coupling
):
    row_count, columns = vectors.shape
    leaf_count = row_count // LEAF
    depth_local = leaf_count.bit_length() - 1
    position = lax.axis_index(SPACE)
    leaf_zero = position * leaf_count
    basis_leaves = leaf_basis.reshape(RANK, leaf_count, LEAF)
    leaf_vectors = vectors.reshape(leaf_count, LEAF, columns)
    coefficients = [
        jnp.einsum("rlp,lpv->lrv", basis_leaves, leaf_vectors, preferred_element_type=jnp.float32)
    ]
    for height in range(1, depth_local + 1):
        cluster_count = leaf_count >> height
        first_slot = leaf_count - (2 * leaf_count >> height)
        lift_mats = as_float(transfer[0, first_slot : first_slot + cluster_count])
        children = coefficients[-1].reshape(cluster_count, 2 * RANK, columns)
        coefficients.append(jnp.einsum("cra,cav->crv", lift_mats, children, precision=HIGHEST))
    def rim(rows, clusters):
        edges = jnp.stack([coefficients[height][clusters] for height in range(depth_local)], 0)
        coords = points[:, rows]
        high = lax.reduce_precision(coords, exponent_bits=8, mantissa_bits=7)
        middle = lax.reduce_precision(coords - high, exponent_bits=8, mantissa_bits=7)
        pieces = jnp.stack([high, middle, coords - high - middle], 0).astype(jnp.bfloat16)
        parts = [vectors[rows], pieces, edges.astype(jnp.bfloat16)]
        return jnp.concatenate([part.reshape(-1) for part in parts]), [p.shape for p in parts]

    head, shapes = rim(slice(0, LEAF), slice(0, 2))
    tail, _ = rim(slice(row_count - LEAF, row_count), slice(-2, None))
    count = lax.axis_size(SPACE)
    from_left = lax.ppermute(tail, SPACE, [(i, i + 1) for i in range(count - 1)])
    from_right = lax.ppermute(head, SPACE, [(i + 1, i) for i in range(count - 1)])

    def unpack(flat):
        pieces, done = [], 0
        for shape in shapes:
            size = int(np.prod(shape))
            pieces.append(flat[done : done + size].reshape(shape))
            done += size
        coords = as_float(pieces[1])
        return pieces[0], (coords[0] + coords[1]) + coords[2], as_float(pieces[2])

    def late(held):
        (from_left, from_right), lift_stack, basis_float = held
        lift_stack = as_float(lift_stack)
        basis_float = as_float(basis_float)
        reach = jnp.eye(RANK, dtype=jnp.float32)[None]
        for height in range(depth_local - 1, -1, -1):
            cluster_count = leaf_count >> height + 1
            first_slot = leaf_count - (2 * leaf_count >> height + 1)
            lift_mats = lift_stack[first_slot : first_slot + cluster_count]
            reach = jnp.einsum("cra,crk->cak", lift_mats, reach, precision=HIGHEST)
            reach = reach.reshape(2 * cluster_count, RANK, RANK)
        reach_rows = jnp.einsum("rlp,lrk->lpk", basis_float, reach, precision=HIGHEST)
        left_edges = unpack(from_left)[2]
        right_edges = unpack(from_right)[2]
        fields = []
        for height in range(depth_local):
            cluster_count = leaf_count >> height
            first_slot = 2 * leaf_count - (2 * leaf_count >> height)
            extended = jnp.concatenate([left_edges[height], coefficients[height], right_edges[height]], 0)
            stacked = extended[partner_table(cluster_count) + 2].reshape(
                cluster_count, 3 * RANK, columns
            )
            mixers = as_float(coupling[0, first_slot : first_slot + cluster_count])
            fields.append(jnp.einsum("cra,cav->crv", mixers, stacked, precision=HIGHEST))
        return fields, reach_rows

    left_vectors, left_points, _ = unpack(from_left)
    right_vectors, right_points, _ = unpack(from_right)
    vector_rims = jnp.concatenate(
        [left_vectors.astype(vectors.dtype), vectors, right_vectors.astype(vectors.dtype)], 0
    )
    point_rims = jnp.concatenate([left_points, points, right_points], 1)
    nearby = near_field(vector_rims, point_rims, near_index, 0, leaf_zero, leaf_count)
    device_coupling = as_float(coupling[0, 2 * leaf_count - 2])
    device_coef = coefficients[depth_local][0]
    downward, (fields, reach_rows) = upper_tree(
        device_coef, device_coupling, upper_transfer, upper_coupling, ((from_left, from_right), transfer[0], basis_leaves), late
    )
    local_down = None
    for height in range(depth_local - 1, -1, -1):
        cluster_count = leaf_count >> height + 1
        first_slot = leaf_count - (2 * leaf_count >> height + 1)
        lift_mats = as_float(transfer[0, first_slot : first_slot + cluster_count])
        if local_down is None:
            local_down = fields[height]
        else:
            spread = jnp.einsum("cra,crv->cav", lift_mats, local_down, precision=HIGHEST)
            local_down = fields[height] + spread.reshape(2 * cluster_count, RANK, columns)
    basis_float = as_float(basis_leaves)
    far_field = (
        jnp.einsum("rlp,lrv->lpv", basis_float, local_down, precision=HIGHEST)
        + jnp.einsum("lpk,kv->lpv", reach_rows, downward, precision=HIGHEST)
    ).reshape(row_count, columns)
    return (nearby + NUGGET * vectors.astype(jnp.float32) + far_field).astype(jnp.bfloat16)


def solution(mesh):
    devices = mesh.devices.reshape(CUTS + (mesh.shape["vec"],))
    split_mesh = jax.sharding.Mesh(devices, SPACE + ("vec",))
    return jax.shard_map(
        local,
        mesh=split_mesh,
        in_specs=(
            P(SPACE, "vec"),
            P(None, SPACE),
            P(SPACE, None),
            P(None, SPACE),
            P(SPACE, None, None, None),
            P(SPACE, None, None, None),
            P(SPACE, None, None),
            P(SPACE, None, None),
        ),
        out_specs=P(SPACE, "vec"),
        check_vma=False,
    )
```
